32 devices in a mesh: dp: 8 (over y, x, core), tensor: 4 (over z).
Axes of the slice: x: 2, y: 2, z: 4, core: 2. Of those that a mesh axis runs over, the one named last changes fastest.
Arguments:
- frames: bfloat16 [8, 1024, 1024], P('dp'), may hold values from -6 to 6
- text_states: bfloat16 [8, 128, 1024], P('dp'), may hold values from -6 to 6
- frame_len: int32 [8], P('dp'), may hold values from 170 to 1024, as said below
- text_token_length: int32 [8], P('dp'), may hold values from 5 to 128, as said below
- self_gain: float32 [1024], replicated, may hold values from 0.5 to 1.5
- self_bias: float32 [1024], replicated, may hold values from -2 to 2
- cross_gain: float32 [1024], replicated, may hold values from 0.5 to 1.5
- cross_bias: float32 [1024], replicated, may hold values from -2 to 2
- feed_gain: float32 [1024], replicated, may hold values from 0.5 to 1.5
- feed_bias: float32 [1024], replicated, may hold values from -2 to 2
- self_qkv: bfloat16 [3, 1024, 1024], P(None, None, 'tensor'), may hold values from -0.1875 to 0.1875
- self_out: bfloat16 [1024, 1024], P('tensor'), may hold values from -0.75 to 0.75
- cross_query: bfloat16 [1024, 1024], P(None, 'tensor'), may hold values from -0.1875 to 0.1875
- cross_keyval: bfloat16 [2, 1024, 1024], P(None, None, 'tensor'), may hold values from -0.1875 to 0.1875
- cross_out: bfloat16 [1024, 1024], P('tensor'), may hold values from -0.75 to 0.75
- feed_up: bfloat16 [1024, 4096], P(None, 'tensor'), may hold values from -0.1875 to 0.1875
- feed_down: bfloat16 [4096, 1024], P('tensor'), may hold values from -0.125 to 0.125
- cotangent: bfloat16 [8, 1024, 1024], P('dp'), may hold values from -6 to 6
Outputs:
- block_out: bfloat16 [8, 1024, 1024], P('dp')
- frames_grad: float32 [8, 1024, 1024], P('dp')
- text_grad: float32 [8, 128, 1024], P('dp')
- self_gain_grad: float32 [1024], replicated
- self_bias_grad: float32 [1024], replicated
- cross_gain_grad: float32 [1024], replicated
- cross_bias_grad: float32 [1024], replicated
- feed_gain_grad: float32 [1024], replicated
- feed_bias_grad: float32 [1024], replicated
- self_qkv_grad: float32 [3, 1024, 1024], P(None, None, 'tensor')
- self_out_grad: float32 [1024, 1024], P('tensor')
- cross_query_grad: float32 [1024, 1024], P(None, 'tensor')
- cross_keyval_grad: float32 [2, 1024, 1024], P(None, None, 'tensor')
- cross_out_grad: float32 [1024, 1024], P('tensor')
- feed_up_grad: float32 [1024, 4096], P(None, 'tensor')
- feed_down_grad: float32 [4096, 1024], P('tensor')
The draws below stay inside these ranges and needn't reach their ends.
Inputs may be any that keep to these rules, and one draw needn't show every extreme that they name: Frames of a clip at or after its frame_len are padding: no query sees them as keys. Some clip of every draw has all 1024 frames. Text tokens of a clip at or after its text_token_length are padding that no query sees. Some clip of every draw has all 128 tokens.
All inputs are finite; a program needn't handle non-finite values.
Results may differ from the reference program's by a relative error of at most 0.03.
Values may be sent and summed in bfloat16 or wider, within the bound.
No kernel may reach another device: no remote copies, remote signals or barrier semaphores. Data moves between devices by JAX's collectives and lax.ppermute only.
A program may use at most 128 MiB of HBM per device.

```python
import jax
import jax.numpy as jnp
from jax import lax

D = 1024
HEADS = 16
HEAD = 64
FF = 4096
TEXT = 128
SLOT = 1024
CLIPS = 8
N_TENSOR = 4


def draw_frame_len(key, part):
    draw_key, place_key = jax.random.split(jax.random.fold_in(key, 11))
    lengths = jax.random.randint(draw_key, (CLIPS,), SLOT // 6, SLOT + 1, dtype=jnp.int32)
    chosen = jax.random.randint(place_key, (), 0, CLIPS, dtype=jnp.int32)
    return jnp.where(jnp.arange(CLIPS, dtype=jnp.int32) == chosen, SLOT, lengths).astype(jnp.int32)


def draw_text_token_length(key, part):
    draw_key, place_key = jax.random.split(jax.random.fold_in(key, 23))
    lengths = jax.random.randint(draw_key, (CLIPS,), TEXT // 32 + 1, TEXT + 1, dtype=jnp.int32)
    chosen = jax.random.randint(place_key, (), 0, CLIPS, dtype=jnp.int32)
    return jnp.where(jnp.arange(CLIPS, dtype=jnp.int32) == chosen, TEXT, lengths).astype(jnp.int32)


def steps_of(key, dims, pieces, smallest, high):
    level, own = 1.0, jax.random.fold_in(key, 6)
    for dim, parts in pieces:
        draws = jnp.exp(jax.random.uniform(jax.random.fold_in(own, dim), (parts,), jnp.float32, smallest / len(pieces), high / len(pieces)))
        level = level * jnp.repeat(draws, dims[dim] // parts).reshape([-1 if axis == dim else 1 for axis in range(len(dims))])
    return level


def bell_draw(key, dims, scale, most, cuts=(), held_as=jnp.bfloat16):
    values = scale * jax.random.normal(key, dims, jnp.float32)
    if cuts:
        values = values * steps_of(key, dims, cuts, -0.22, 0.18)
    return jnp.clip(values, -most, most).astype(held_as)


def setup_inputs(seed: int = 0) -> dict:
    key_of = jax.random.split(jax.random.key(seed), 19)
    frames = bell_draw(key_of[0], (CLIPS, SLOT, D), 1.0, 6.0, ((0, 8),))
    text_states = bell_draw(key_of[1], (CLIPS, TEXT, D), 1.0, 6.0, ((0, 8),))
    frame_len = draw_frame_len(jax.random.fold_in(key_of[18], 71), 0)
    text_token_length = draw_text_token_length(jax.random.fold_in(key_of[18], 71), 0)
    self_gain = jnp.clip(1.0 + 0.1 * jax.random.normal(key_of[4], (D,), jnp.float32), 0.5, 1.5)
    self_bias = bell_draw(key_of[5], (D,), 0.3, 2.0, (), jnp.float32)
    cross_gain = jnp.clip(1.0 + 0.1 * jax.random.normal(key_of[6], (D,), jnp.float32), 0.5, 1.5)
    cross_bias = bell_draw(key_of[7], (D,), 0.3, 2.0, (), jnp.float32)
    feed_gain = jnp.clip(1.0 + 0.1 * jax.random.normal(key_of[8], (D,), jnp.float32), 0.5, 1.5)
    feed_bias = bell_draw(key_of[9], (D,), 0.3, 2.0, (), jnp.float32)
    self_qkv = bell_draw(key_of[10], (3, D, D), D ** -0.5, 0.1875, ((2, 4),))
    self_out = bell_draw(key_of[11], (D, D), (D // 16) ** -0.5, 0.75, ((0, 4),))
    cross_query = bell_draw(key_of[12], (D, D), D ** -0.5, 0.1875, ((1, 4),))
    cross_keyval = bell_draw(key_of[13], (2, D, D), D ** -0.5, 0.1875, ((2, 4),))
    cross_out = bell_draw(key_of[14], (D, D), (D // 16) ** -0.5, 0.75, ((0, 4),))
    feed_up = bell_draw(key_of[15], (D, FF), D ** -0.5, 0.1875, ((1, 4),))
    feed_down = bell_draw(key_of[16], (FF, D), (FF // 2) ** -0.5, 0.125, ((0, 4),))
    cotangent = bell_draw(key_of[17], (CLIPS, SLOT, D), 1.0, 6.0, ((0, 8),))
    return {"frames": frames, "text_states": text_states, "frame_len": frame_len, "text_token_length": text_token_length, "self_gain": self_gain, "self_bias": self_bias, "cross_gain": cross_gain, "cross_bias": cross_bias, "feed_gain": feed_gain, "feed_bias": feed_bias, "self_qkv": self_qkv, "self_out": self_out, "cross_query": cross_query, "cross_keyval": cross_keyval, "cross_out": cross_out, "feed_up": feed_up, "feed_down": feed_down, "cotangent": cotangent}


EPSILON = 1e-05
MASKED = -1e+30
HIGHEST = lax.Precision.HIGHEST

@jax.custom_vjp
def low(v):
    return lax.optimization_barrier(v.astype(jnp.bfloat16)).astype(jnp.float32)

@jax.custom_vjp
def low_back(v):
    return v

def low_keep(v):
    return (low(v), None)

def low_pass(kept, grad):
    return (grad,)

def back_keep(v):
    return (v, None)

def back_low(kept, grad):
    return (low(grad),)
low.defvjp(low_keep, low_pass)
low_back.defvjp(back_keep, back_low)

def layer_norm(inputs, norm_gain, norm_bias):
    row_mean = lax.optimization_barrier(jnp.mean(inputs, axis=-1, keepdims=True))
    centred = inputs - row_mean
    spread = lax.optimization_barrier(jnp.mean(centred * centred, axis=-1, keepdims=True))
    return centred * lax.rsqrt(spread + EPSILON) * norm_gain + norm_bias

def attend(queries, key_rows, values, key_limit, causal):
    row_count = queries.shape[0]
    block_len = min(512, row_count)
    portions = queries.reshape(row_count // block_len, block_len, HEADS, HEAD)
    offsets = jnp.arange(row_count // block_len) * block_len
    key_pos = jnp.arange(key_rows.shape[0])

    def one_block(entries):
        portion, offset = entries
        scores = jnp.einsum('bhe,khe->hbk', portion, key_rows, precision=HIGHEST) * HEAD ** (-0.5)
        scores = low_back(scores)
        allowed = key_pos[None, :] < key_limit
        if causal:
            allowed = allowed & (key_pos[None, :] <= offset + jnp.arange(block_len)[:, None])
        scores = jnp.where(allowed[None], scores, MASKED)
        probs = jax.nn.softmax(scores, axis=-1)
        return jnp.einsum('hbk,khe->bhe', low(probs), values, precision=HIGHEST)
    result = lax.map(jax.checkpoint(one_block), (portions, offsets))
    return result.reshape(row_count, HEADS, HEAD)

def group_sum(by_group, weight_rows):
    partial_value = low(jnp.einsum('gsk,gkd->gsd', by_group, weight_rows, precision=HIGHEST))
    return low_back(lax.optimization_barrier(jnp.sum(partial_value, axis=0)))

def forward(frames, text, params, frame_len, text_token_length):
    self_gain, self_bias, cross_gain, cross_bias, feed_gain, feed_bias, self_qkv, self_out, cross_query, cross_keyval, cross_out, feed_up, feed_down = params
    groups = N_TENSOR
    local_width = D // groups
    hidden_activation = FF // groups
    normed = low(layer_norm(frames, self_gain, self_bias))
    copies = low_back(jnp.broadcast_to(normed, (groups,) + normed.shape))
    qkv_cols = self_qkv.reshape(3, D, groups, local_width).transpose(2, 0, 1, 3)
    projected = low_back(low(jnp.einsum('gsd,gcde->gcse', copies, qkv_cols, precision=HIGHEST)))
    heads_all = projected.transpose(1, 2, 0, 3).reshape(3, SLOT, HEADS, HEAD)
    attended = low_back(low(attend(heads_all[0], heads_all[1], heads_all[2], frame_len, True)))
    by_group = attended.reshape(SLOT, groups, local_width).transpose(1, 0, 2)
    after_self = frames + group_sum(by_group, self_out.reshape(groups, local_width, D))
    normed = low(layer_norm(after_self, cross_gain, cross_bias))
    copies = low_back(jnp.broadcast_to(normed, (groups,) + normed.shape))
    query_cols = cross_query.reshape(D, groups, local_width).transpose(1, 0, 2)
    queries = low_back(low(jnp.einsum('gsd,gde->gse', copies, query_cols, precision=HIGHEST)))
    queries = queries.transpose(1, 0, 2).reshape(SLOT, HEADS, HEAD)
    text_copies = low_back(jnp.broadcast_to(text, (groups,) + text.shape))
    keyval_cols = cross_keyval.reshape(2, D, groups, local_width).transpose(2, 0, 1, 3)
    keyvals = low_back(low(jnp.einsum('gtd,gcde->gcte', text_copies, keyval_cols, precision=HIGHEST)))
    keyvals = keyvals.transpose(1, 2, 0, 3).reshape(2, TEXT, HEADS, HEAD)
    attended = low_back(low(attend(queries, keyvals[0], keyvals[1], text_token_length, False)))
    by_group = attended.reshape(SLOT, groups, local_width).transpose(1, 0, 2)
    after_cross = after_self + group_sum(by_group, cross_out.reshape(groups, local_width, D))
    normed = low(layer_norm(after_cross, feed_gain, feed_bias))
    copies = low_back(jnp.broadcast_to(normed, (groups,) + normed.shape))
    up_cols = feed_up.reshape(D, groups, hidden_activation).transpose(1, 0, 2)
    upward = low_back(jnp.einsum('gsd,gdk->gsk', copies, up_cols, precision=HIGHEST))
    active = low(jax.nn.gelu(upward, approximate=False))
    return after_cross + group_sum(active, feed_down.reshape(groups, hidden_activation, D))

def reference(frames, text_states, frame_len, text_token_length, self_gain, self_bias, cross_gain, cross_bias, feed_gain, feed_bias, self_qkv, self_out, cross_query, cross_keyval, cross_out, feed_up, feed_down, cotangent):
    params = (self_gain.astype(jnp.float32), self_bias.astype(jnp.float32), cross_gain.astype(jnp.float32), cross_bias.astype(jnp.float32), feed_gain.astype(jnp.float32), feed_bias.astype(jnp.float32), self_qkv.astype(jnp.float32), self_out.astype(jnp.float32), cross_query.astype(jnp.float32), cross_keyval.astype(jnp.float32), cross_out.astype(jnp.float32), feed_up.astype(jnp.float32), feed_down.astype(jnp.float32))

    def clip_step(totals, entries):
        frames_clip, text_clip, frames_limit, text_limit, upstream = entries

        def clip_forward(frames_in, text_in, params_in):
            return forward(frames_in, text_in, params_in, frames_limit, text_limit)
        result, pullback = jax.vjp(clip_forward, frames_clip.astype(jnp.float32), text_clip.astype(jnp.float32), params)
        frame_portion_rows, text_part, params_part = pullback(upstream.astype(jnp.float32))
        totals = jax.tree.map(jnp.add, totals, params_part)
        return (totals, (result.astype(jnp.bfloat16), frame_portion_rows, text_part))
    zeros_start = jax.tree.map(jnp.zeros_like, params)
    totals, (outputs, frames_grads, text_grads) = lax.scan(clip_step, zeros_start, (frames, text_states, frame_len, text_token_length, cotangent))
    return (outputs, frames_grads, text_grads, totals[0], totals[1], totals[2], totals[3], totals[4], totals[5], totals[6], totals[7], totals[8], totals[9], totals[10], totals[11], totals[12])
```

```python
import jax
import jax.numpy as jnp
from jax import lax
from jax.sharding import PartitionSpec as P

HEAD = 64


EPSILON = 1e-05
MASKED = -1e30


def layer_norm(inputs, norm_gain, norm_bias):
    row_mean = jnp.mean(inputs, axis=-1, keepdims=True)
    centred = inputs - row_mean
    spread = jnp.mean(centred * centred, axis=-1, keepdims=True)
    return centred * lax.rsqrt(spread + EPSILON) * norm_gain + norm_bias


def norm_back(inputs, norm_gain, norm_bias, upstream):
    _, pullback = jax.vjp(layer_norm, inputs, norm_gain, norm_bias)
    return pullback(upstream)


def gelu_exact(inputs):
    return jax.nn.gelu(inputs, approximate=False)


def masked_scores(portion, offset, key_rows, key_limit, causal, score_scale):
    scores = (
        jnp.einsum("bhe,khe->hbk", portion, key_rows, preferred_element_type=jnp.float32)
        * score_scale
    )
    key_pos = jnp.arange(key_rows.shape[0])
    allowed = key_pos[None, :] < key_limit
    if causal:
        allowed = allowed & (key_pos[None, :] <= offset + jnp.arange(portion.shape[0])[:, None])
    return jnp.where(allowed[None], scores, MASKED)


def attend(queries, key_rows, values, key_limit, causal, score_scale):
    row_count, head_count, head_size = queries.shape
    block_len = min(512, row_count)
    portions = queries.reshape(row_count // block_len, block_len, head_count, head_size)
    offsets = jnp.arange(row_count // block_len) * block_len

    def one_block(entries):
        portion, offset = entries
        scores = masked_scores(portion, offset, key_rows, key_limit, causal, score_scale)
        row_max = jnp.max(scores, axis=-1, keepdims=True)
        unnormed = jnp.exp(scores - row_max)
        row_sum = jnp.sum(unnormed, axis=-1, keepdims=True)
        probs_low = (unnormed / row_sum).astype(jnp.bfloat16)
        result = jnp.einsum("hbk,khe->bhe", probs_low, values, preferred_element_type=jnp.float32)
        return (result.astype(jnp.bfloat16), row_max[..., 0] + jnp.log(row_sum[..., 0]))

    result, log_total = lax.map(one_block, (portions, offsets))
    return (result.reshape(row_count, head_count, head_size), log_total)


def attend_back(queries, key_rows, values, log_total, out_grad, key_limit, causal, score_scale):
    row_count, head_count, head_size = queries.shape
    block_len = min(512, row_count)
    portions = queries.reshape(row_count // block_len, block_len, head_count, head_size)
    grad_parts = out_grad.reshape(row_count // block_len, block_len, head_count, head_size)
    offsets = jnp.arange(row_count // block_len) * block_len

    def one_block(carry, entries):
        key_grad, value_grad = carry
        portion, grad_part, log_part, offset = entries
        scores = masked_scores(portion, offset, key_rows, key_limit, causal, score_scale)
        probs = jnp.exp(scores - log_part[..., None])
        probs_grad = jnp.einsum(
            "bhe,khe->hbk", grad_part, values, preferred_element_type=jnp.float32
        )
        row_dot = jnp.sum(probs * probs_grad, axis=-1, keepdims=True)
        scores_grad = (probs * (probs_grad - row_dot)).astype(jnp.bfloat16)
        value_grad = value_grad + jnp.einsum(
            "hbk,bhe->khe",
            probs.astype(jnp.bfloat16),
            grad_part,
            preferred_element_type=jnp.float32,
        )
        key_grad = (
            key_grad
            + jnp.einsum("hbk,bhe->khe", scores_grad, portion, preferred_element_type=jnp.float32)
            * score_scale
        )
        query_grad = (
            jnp.einsum("hbk,khe->bhe", scores_grad, key_rows, preferred_element_type=jnp.float32)
            * score_scale
        )
        return ((key_grad, value_grad), query_grad)

    empty = jnp.zeros(key_rows.shape, jnp.float32)
    (key_grad, value_grad), query_grad = lax.scan(
        one_block, (empty, empty), (portions, grad_parts, log_total, offsets)
    )
    return (query_grad.reshape(row_count, head_count, head_size), key_grad, value_grad)


def head_total(partial_value):
    return lax.psum(partial_value.astype(jnp.bfloat16), "tensor").astype(jnp.float32)


def _shift(value, axis, count, step):
    pairs = [(i, i + step) for i in range(count) if 0 <= i + step < count]
    return lax.ppermute(value, axis, pairs)


def relay_gather(block, axis):
    count = lax.axis_size(axis)
    me = lax.axis_index(axis)
    out = jnp.zeros((count + 1,) + block.shape, block.dtype)
    out = lax.dynamic_update_index_in_dim(out, block, me, 0)
    from_left, from_right = block, block
    for k in range(1, count):
        from_left = _shift(from_left, axis, count, 1)
        from_right = _shift(from_right, axis, count, -1)
        out = lax.dynamic_update_index_in_dim(
            out, from_left, jnp.where(me - k >= 0, me - k, count), 0
        )
        out = lax.dynamic_update_index_in_dim(
            out, from_right, jnp.where(me + k < count, me + k, count), 0
        )
    return out[:count]


def relay_scatter(value, axis):
    count = lax.axis_size(axis)
    me = lax.axis_index(axis)
    shards = value.reshape((count, value.shape[0] // count) + value.shape[1:])

    def pick(index):
        return lax.dynamic_index_in_dim(shards, jnp.clip(index, 0, count - 1), 0, keepdims=False)

    to_right = to_left = None
    for k in range(1, count):
        send_right = pick(me + count - k).astype(jnp.float32)
        send_left = pick(me - (count - k)).astype(jnp.float32)
        if to_right is not None:
            send_right = send_right + to_right.astype(jnp.float32)
            send_left = send_left + to_left.astype(jnp.float32)
        to_right = _shift(send_right.astype(value.dtype), axis, count, 1)
        to_left = _shift(send_left.astype(value.dtype), axis, count, -1)
    total = pick(me).astype(jnp.float32)
    if to_right is not None:
        total = total + to_right.astype(jnp.float32) + to_left.astype(jnp.float32)
    return total.astype(value.dtype)


def relay_total(partial_value):
    low_value = partial_value.astype(jnp.bfloat16)
    reduced = relay_scatter(low_value, "tensor")
    return relay_gather(reduced, "tensor").reshape(low_value.shape).astype(jnp.float32)


def gathered_sum(pieces, weights, spec):
    partial_value = jnp.einsum(spec, pieces, weights, preferred_element_type=jnp.float32)
    return jnp.sum(partial_value.astype(jnp.bfloat16).astype(jnp.float32), axis=0)


def local(
    frames,
    text_states,
    frame_len,
    text_token_length,
    self_gain,
    self_bias,
    cross_gain,
    cross_bias,
    feed_gain,
    feed_bias,
    self_qkv,
    self_out,
    cross_query,
    cross_keyval,
    cross_out,
    feed_up,
    feed_down,
    cotangent,
):
    clip_count, slot_len, model_width = frames.shape
    text_count = text_states.shape[1]
    local_width = self_out.shape[0]
    head_count = local_width // HEAD
    score_scale = HEAD ** (-0.5)
    row_total = clip_count * slot_len
    inputs = frames.reshape(row_total, model_width).astype(jnp.float32)
    out_grad = cotangent.reshape(row_total, model_width)
    normed_self = layer_norm(inputs, self_gain, self_bias).astype(jnp.bfloat16)
    projected = jnp.einsum(
        "sd,cde->cse", normed_self, self_qkv, preferred_element_type=jnp.float32
    ).astype(jnp.bfloat16)
    projected = projected.reshape(3, clip_count, slot_len, head_count, HEAD)

    def self_clip(entries):
        return attend(entries[0], entries[1], entries[2], entries[3], True, score_scale)

    self_heads, self_log = lax.map(self_clip, (projected[0], projected[1], projected[2], frame_len))
    self_flat = self_heads.reshape(row_total, local_width)
    self_out_all = lax.all_gather(self_out, "tensor")
    cross_out_all = lax.all_gather(cross_out, "tensor")
    cross_query_all = lax.all_gather(cross_query, "tensor")
    self_pieces = relay_gather(self_flat, "tensor")
    after_self = inputs + gathered_sum(self_pieces, self_out_all, "gsk,gkd->gsd")
    normed_cross = layer_norm(after_self, cross_gain, cross_bias).astype(jnp.bfloat16)
    cross_queries = jnp.dot(normed_cross, cross_query, preferred_element_type=jnp.float32).astype(
        jnp.bfloat16
    )
    cross_queries = cross_queries.reshape(clip_count, slot_len, head_count, HEAD)
    text_proj = jnp.einsum(
        "ctd,gde->gcte", text_states, cross_keyval, preferred_element_type=jnp.float32
    ).astype(jnp.bfloat16)
    text_proj = text_proj.reshape(2, clip_count, text_count, head_count, HEAD)

    def cross_clip(entries):
        return attend(entries[0], entries[1], entries[2], entries[3], False, score_scale)

    cross_heads, cross_log = lax.map(
        cross_clip, (cross_queries, text_proj[0], text_proj[1], text_token_length)
    )
    cross_flat = cross_heads.reshape(row_total, local_width)
    cross_pieces = relay_gather(cross_flat, "tensor")
    after_cross = after_self + gathered_sum(cross_pieces, cross_out_all, "gsk,gkd->gsd")
    normed_feed = layer_norm(after_cross, feed_gain, feed_bias).astype(jnp.bfloat16)
    upward = jnp.dot(normed_feed, feed_up, preferred_element_type=jnp.float32)
    active = gelu_exact(upward).astype(jnp.bfloat16)
    feed_part = jnp.dot(active, feed_down, preferred_element_type=jnp.float32)
    block_out = (after_cross + head_total(feed_part)).astype(jnp.bfloat16)
    active_grad = jnp.einsum("sd,kd->sk", out_grad, feed_down, preferred_element_type=jnp.float32)
    _, gelu_pull = jax.vjp(gelu_exact, upward)
    upward_grad = gelu_pull(active_grad)[0].astype(jnp.bfloat16)
    downward_gradient = jnp.einsum(
        "sk,sd->kd", active, out_grad, preferred_element_type=jnp.float32
    )
    up_grad = jnp.einsum("sd,sk->dk", normed_feed, upward_grad, preferred_element_type=jnp.float32)
    feed_input_part = jnp.einsum(
        "sk,dk->sd", upward_grad, feed_up, preferred_element_type=jnp.float32
    )
    feed_back = norm_back(after_cross, feed_gain, feed_bias, relay_total(feed_input_part))
    cross_grad_rows = out_grad.astype(jnp.float32) + feed_back[0]
    cross_grad_low = cross_grad_rows.astype(jnp.bfloat16)
    cout_grad = jnp.einsum(
        "sk,sd->kd", cross_flat, cross_grad_low, preferred_element_type=jnp.float32
    )
    cross_heads_grad = jnp.einsum(
        "sd,kd->sk", cross_grad_low, cross_out, preferred_element_type=jnp.float32
    ).astype(jnp.bfloat16)
    cross_heads_grad = cross_heads_grad.reshape(clip_count, slot_len, head_count, HEAD)

    def cross_clip_back(entries):
        return attend_back(
            entries[0],
            entries[1],
            entries[2],
            entries[3],
            entries[4],
            entries[5],
            False,
            score_scale,
        )

    cquery_heads, ckey_heads, cvalue_heads = lax.map(
        cross_clip_back,
        (cross_queries, text_proj[0], text_proj[1], cross_log, cross_heads_grad, text_token_length),
    )
    query_grad_low = cquery_heads.reshape(row_total, local_width).astype(jnp.bfloat16)
    keyval_grad_low = jnp.stack((ckey_heads, cvalue_heads)).astype(jnp.bfloat16)
    keyval_grad_low = keyval_grad_low.reshape(2, clip_count, text_count, local_width)
    cquery_grad = jnp.einsum(
        "sd,se->de", normed_cross, query_grad_low, preferred_element_type=jnp.float32
    )
    ckeyval_grad = jnp.einsum(
        "ctd,gcte->gde", text_states, keyval_grad_low, preferred_element_type=jnp.float32
    )
    text_part = jnp.einsum(
        "gcte,gde->ctd", keyval_grad_low, cross_keyval, preferred_element_type=jnp.float32
    )
    query_pieces = relay_gather(query_grad_low, "tensor")
    cross_sum = gathered_sum(query_pieces, cross_query_all, "gse,gde->gsd")
    text_grad = lax.psum(text_part.astype(jnp.bfloat16), "tensor").astype(jnp.float32)
    cross_back = norm_back(after_self, cross_gain, cross_bias, cross_sum)
    self_grad_rows = cross_grad_rows + cross_back[0]
    self_grad_low = self_grad_rows.astype(jnp.bfloat16)
    sout_grad = jnp.einsum(
        "sk,sd->kd", self_flat, self_grad_low, preferred_element_type=jnp.float32
    )
    self_heads_grad = jnp.einsum(
        "sd,kd->sk", self_grad_low, self_out, preferred_element_type=jnp.float32
    ).astype(jnp.bfloat16)
    self_heads_grad = self_heads_grad.reshape(clip_count, slot_len, head_count, HEAD)

    def self_clip_back(entries):
        return attend_back(
            entries[0],
            entries[1],
            entries[2],
            entries[3],
            entries[4],
            entries[5],
            True,
            score_scale,
        )

    self_query_heads, self_key_heads, self_value_heads = lax.map(
        self_clip_back,
        (projected[0], projected[1], projected[2], self_log, self_heads_grad, frame_len),
    )
    projection_gradient = jnp.stack((self_query_heads, self_key_heads, self_value_heads)).astype(
        jnp.bfloat16
    )
    projection_gradient = projection_gradient.reshape(3, row_total, local_width)
    qkv_grad = jnp.einsum(
        "sd,cse->cde", normed_self, projection_gradient, preferred_element_type=jnp.float32
    )
    self_input_part = jnp.einsum(
        "cse,cde->sd", projection_gradient, self_qkv, preferred_element_type=jnp.float32
    )
    self_back = norm_back(inputs, self_gain, self_bias, relay_total(self_input_part))
    frames_grad = self_grad_rows + self_back[0]
    gain_terms = (
        self_back[1],
        self_back[2],
        cross_back[1],
        cross_back[2],
        feed_back[1],
        feed_back[2],
    )
    summed = (
        lax.psum(gain_terms[0].astype(jnp.bfloat16), "dp").astype(jnp.float32),
        lax.psum(gain_terms[1].astype(jnp.bfloat16), "dp").astype(jnp.float32),
        lax.psum(gain_terms[2].astype(jnp.bfloat16), "dp").astype(jnp.float32),
        lax.psum(gain_terms[3].astype(jnp.bfloat16), "dp").astype(jnp.float32),
        lax.psum(gain_terms[4].astype(jnp.bfloat16), "dp").astype(jnp.float32),
        lax.psum(gain_terms[5].astype(jnp.bfloat16), "dp").astype(jnp.float32),
        lax.psum(qkv_grad.astype(jnp.bfloat16), "dp").astype(jnp.float32),
        lax.psum(sout_grad.astype(jnp.bfloat16), "dp").astype(jnp.float32),
        lax.psum(cquery_grad.astype(jnp.bfloat16), "dp").astype(jnp.float32),
        lax.psum(ckeyval_grad.astype(jnp.bfloat16), "dp").astype(jnp.float32),
        lax.psum(cout_grad.astype(jnp.bfloat16), "dp").astype(jnp.float32),
        lax.psum(up_grad.astype(jnp.bfloat16), "dp").astype(jnp.float32),
        lax.psum(downward_gradient.astype(jnp.bfloat16), "dp").astype(jnp.float32),
    )
    return (
        block_out.reshape(clip_count, slot_len, model_width),
        frames_grad.reshape(clip_count, slot_len, model_width),
        text_grad,
        summed[0],
        summed[1],
        summed[2],
        summed[3],
        summed[4],
        summed[5],
        summed[6],
        summed[7],
        summed[8],
        summed[9],
        summed[10],
        summed[11],
        summed[12],
    )


def solution(mesh):
    return jax.shard_map(
        local,
        mesh=mesh,
        in_specs=(
            P("dp", None, None),
            P("dp", None, None),
            P("dp"),
            P("dp"),
            P(),
            P(),
            P(),
            P(),
            P(),
            P(),
            P(None, None, "tensor"),
            P("tensor", None),
            P(None, "tensor"),
            P(None, None, "tensor"),
            P("tensor", None),
            P(None, "tensor"),
            P("tensor", None),
            P("dp", None, None),
        ),
        out_specs=(
            P("dp", None, None),
            P("dp", None, None),
            P("dp", None, None),
            P(),
            P(),
            P(),
            P(),
            P(),
            P(),
            P(None, None, "tensor"),
            P("tensor", None),
            P(None, "tensor"),
            P(None, None, "tensor"),
            P("tensor", None),
            P(None, "tensor"),
            P("tensor", None),
        ),
        check_vma=False,
    )
```

```python
import jax
import jax.numpy as jnp
from jax import lax
from jax.sharding import PartitionSpec as P

HEAD = 64


EPSILON = 1e-05
MASKED = -1e30


def layer_norm(inputs, norm_gain, norm_bias):
    row_mean = jnp.mean(inputs, axis=-1, keepdims=True)
    centred = inputs - row_mean
    spread = jnp.mean(centred * centred, axis=-1, keepdims=True)
    return centred * lax.rsqrt(spread + EPSILON) * norm_gain + norm_bias


def norm_back(inputs, norm_gain, norm_bias, upstream):
    _, pullback = jax.vjp(layer_norm, inputs, norm_gain, norm_bias)
    return pullback(upstream)


def gelu_exact(inputs):
    return jax.nn.gelu(inputs, approximate=False)


def masked_scores(portion, offset, key_rows, key_limit, causal, score_scale):
    scores = (
        jnp.einsum("bhe,khe->hbk", portion, key_rows, preferred_element_type=jnp.float32)
        * score_scale
    )
    key_pos = jnp.arange(key_rows.shape[0])
    allowed = key_pos[None, :] < key_limit
    if causal:
        allowed = allowed & (key_pos[None, :] <= offset + jnp.arange(portion.shape[0])[:, None])
    return jnp.where(allowed[None], scores, MASKED)


def attend(queries, key_rows, values, key_limit, causal, score_scale):
    row_count, head_count, head_size = queries.shape
    block_len = min(512, row_count)
    portions = queries.reshape(row_count // block_len, block_len, head_count, head_size)
    offsets = jnp.arange(row_count // block_len) * block_len

    def one_block(entries):
        portion, offset = entries
        scores = masked_scores(portion, offset, key_rows, key_limit, causal, score_scale)
        row_max = jnp.max(scores, axis=-1, keepdims=True)
        unnormed = jnp.exp(scores - row_max)
        row_sum = jnp.sum(unnormed, axis=-1, keepdims=True)
        probs_low = (unnormed / row_sum).astype(jnp.bfloat16)
        result = jnp.einsum("hbk,khe->bhe", probs_low, values, preferred_element_type=jnp.float32)
        return (result.astype(jnp.bfloat16), row_max[..., 0] + jnp.log(row_sum[..., 0]))

    result, log_total = lax.map(one_block, (portions, offsets))
    return (result.reshape(row_count, head_count, head_size), log_total)


def attend_back(queries, key_rows, values, log_total, out_grad, key_limit, causal, score_scale):
    row_count, head_count, head_size = queries.shape
    block_len = min(512, row_count)
    portions = queries.reshape(row_count // block_len, block_len, head_count, head_size)
    grad_parts = out_grad.reshape(row_count // block_len, block_len, head_count, head_size)
    offsets = jnp.arange(row_count // block_len) * block_len

    def one_block(carry, entries):
        key_grad, value_grad = carry
        portion, grad_part, log_part, offset = entries
        scores = masked_scores(portion, offset, key_rows, key_limit, causal, score_scale)
        probs = jnp.exp(scores - log_part[..., None])
        probs_grad = jnp.einsum(
            "bhe,khe->hbk", grad_part, values, preferred_element_type=jnp.float32
        )
        row_dot = jnp.sum(probs * probs_grad, axis=-1, keepdims=True)
        scores_grad = (probs * (probs_grad - row_dot)).astype(jnp.bfloat16)
        value_grad = value_grad + jnp.einsum(
            "hbk,bhe->khe",
            probs.astype(jnp.bfloat16),
            grad_part,
            preferred_element_type=jnp.float32,
        )
        key_grad = (
            key_grad
            + jnp.einsum("hbk,bhe->khe", scores_grad, portion, preferred_element_type=jnp.float32)
            * score_scale
        )
        query_grad = (
            jnp.einsum("hbk,khe->bhe", scores_grad, key_rows, preferred_element_type=jnp.float32)
            * score_scale
        )
        return ((key_grad, value_grad), query_grad)

    empty = jnp.zeros(key_rows.shape, jnp.float32)
    (key_grad, value_grad), query_grad = lax.scan(
        one_block, (empty, empty), (portions, grad_parts, log_total, offsets)
    )
    return (query_grad.reshape(row_count, head_count, head_size), key_grad, value_grad)


def head_total(partial_value):
    return lax.psum(partial_value.astype(jnp.bfloat16), "tensor").astype(jnp.float32)


def _rotate(value, axis, count, step):
    return lax.ppermute(value, axis, [(i, (i + step) % count) for i in range(count)])


def direct_gather(block, axis):
    count = lax.axis_size(axis)
    me = lax.axis_index(axis)
    pieces = [block] + [_rotate(block, axis, count, step) for step in range(1, count)]
    stacked = jnp.stack(pieces)
    owner = (me - jnp.arange(count)) % count
    return jnp.zeros_like(stacked).at[owner].set(stacked)


def direct_scatter(value, axis):
    count = lax.axis_size(axis)
    me = lax.axis_index(axis)
    shards = value.reshape((count, value.shape[0] // count) + value.shape[1:])
    total = lax.dynamic_index_in_dim(shards, me, 0, keepdims=False).astype(jnp.float32)
    for step in range(1, count):
        sent = lax.dynamic_index_in_dim(shards, (me + step) % count, 0, keepdims=False)
        total = total + _rotate(sent, axis, count, step).astype(jnp.float32)
    return total.astype(value.dtype)


def direct_total(partial_value):
    low_value = partial_value.astype(jnp.bfloat16)
    reduced = direct_scatter(low_value, "tensor")
    return direct_gather(reduced, "tensor").reshape(low_value.shape).astype(jnp.float32)


def gathered_sum(pieces, weights, spec):
    partial_value = jnp.einsum(spec, pieces, weights, preferred_element_type=jnp.float32)
    return jnp.sum(partial_value.astype(jnp.bfloat16).astype(jnp.float32), axis=0)


def local(
    frames,
    text_states,
    frame_len,
    text_token_length,
    self_gain,
    self_bias,
    cross_gain,
    cross_bias,
    feed_gain,
    feed_bias,
    self_qkv,
    self_out,
    cross_query,
    cross_keyval,
    cross_out,
    feed_up,
    feed_down,
    cotangent,
):
    clip_count, slot_len, model_width = frames.shape
    text_count = text_states.shape[1]
    local_width = self_out.shape[0]
    head_count = local_width // HEAD
    score_scale = HEAD ** (-0.5)
    row_total = clip_count * slot_len
    inputs = frames.reshape(row_total, model_width).astype(jnp.float32)
    out_grad = cotangent.reshape(row_total, model_width)
    normed_self = layer_norm(inputs, self_gain, self_bias).astype(jnp.bfloat16)
    projected = jnp.einsum(
        "sd,cde->cse", normed_self, self_qkv, preferred_element_type=jnp.float32
    ).astype(jnp.bfloat16)
    projected = projected.reshape(3, clip_count, slot_len, head_count, HEAD)

    def self_clip(entries):
        return attend(entries[0], entries[1], entries[2], entries[3], True, score_scale)

    self_heads, self_log = lax.map(self_clip, (projected[0], projected[1], projected[2], frame_len))
    self_flat = self_heads.reshape(row_total, local_width)
    self_out_all = lax.all_gather(self_out, "tensor")
    cross_out_all = lax.all_gather(cross_out, "tensor")
    cross_query_all = lax.all_gather(cross_query, "tensor")
    self_pieces = direct_gather(self_flat, "tensor")
    after_self = inputs + gathered_sum(self_pieces, self_out_all, "gsk,gkd->gsd")
    normed_cross = layer_norm(after_self, cross_gain, cross_bias).astype(jnp.bfloat16)
    cross_queries = jnp.dot(normed_cross, cross_query, preferred_element_type=jnp.float32).astype(
        jnp.bfloat16
    )
    cross_queries = cross_queries.reshape(clip_count, slot_len, head_count, HEAD)
    text_proj = jnp.einsum(
        "ctd,gde->gcte", text_states, cross_keyval, preferred_element_type=jnp.float32
    ).astype(jnp.bfloat16)
    text_proj = text_proj.reshape(2, clip_count, text_count, head_count, HEAD)

    def cross_clip(entries):
        return attend(entries[0], entries[1], entries[2], entries[3], False, score_scale)

    cross_heads, cross_log = lax.map(
        cross_clip, (cross_queries, text_proj[0], text_proj[1], text_token_length)
    )
    cross_flat = cross_heads.reshape(row_total, local_width)
    cross_pieces = direct_gather(cross_flat, "tensor")
    after_cross = after_self + gathered_sum(cross_pieces, cross_out_all, "gsk,gkd->gsd")
    normed_feed = layer_norm(after_cross, feed_gain, feed_bias).astype(jnp.bfloat16)
    upward = jnp.dot(normed_feed, feed_up, preferred_element_type=jnp.float32)
    active = gelu_exact(upward).astype(jnp.bfloat16)
    feed_part = jnp.dot(active, feed_down, preferred_element_type=jnp.float32)
    block_out = (after_cross + direct_total(feed_part)).astype(jnp.bfloat16)
    active_grad = jnp.einsum("sd,kd->sk", out_grad, feed_down, preferred_element_type=jnp.float32)
    _, gelu_pull = jax.vjp(gelu_exact, upward)
    upward_grad = gelu_pull(active_grad)[0].astype(jnp.bfloat16)
    downward_gradient = jnp.einsum(
        "sk,sd->kd", active, out_grad, preferred_element_type=jnp.float32
    )
    up_grad = jnp.einsum("sd,sk->dk", normed_feed, upward_grad, preferred_element_type=jnp.float32)
    feed_sums = (
        lax.psum(up_grad.astype(jnp.bfloat16), "dp").astype(jnp.float32),
        lax.psum(downward_gradient.astype(jnp.bfloat16), "dp").astype(jnp.float32),
    )
    feed_input_part = jnp.einsum(
        "sk,dk->sd", upward_grad, feed_up, preferred_element_type=jnp.float32
    )
    feed_back = norm_back(after_cross, feed_gain, feed_bias, direct_total(feed_input_part))
    cross_grad_rows = out_grad.astype(jnp.float32) + feed_back[0]
    cross_grad_low = cross_grad_rows.astype(jnp.bfloat16)
    cout_grad = jnp.einsum(
        "sk,sd->kd", cross_flat, cross_grad_low, preferred_element_type=jnp.float32
    )
    cross_heads_grad = jnp.einsum(
        "sd,kd->sk", cross_grad_low, cross_out, preferred_element_type=jnp.float32
    ).astype(jnp.bfloat16)
    cross_heads_grad = cross_heads_grad.reshape(clip_count, slot_len, head_count, HEAD)

    def cross_clip_back(entries):
        return attend_back(
            entries[0],
            entries[1],
            entries[2],
            entries[3],
            entries[4],
            entries[5],
            False,
            score_scale,
        )

    cquery_heads, ckey_heads, cvalue_heads = lax.map(
        cross_clip_back,
        (cross_queries, text_proj[0], text_proj[1], cross_log, cross_heads_grad, text_token_length),
    )
    query_grad_low = cquery_heads.reshape(row_total, local_width).astype(jnp.bfloat16)
    keyval_grad_low = jnp.stack((ckey_heads, cvalue_heads)).astype(jnp.bfloat16)
    keyval_grad_low = keyval_grad_low.reshape(2, clip_count, text_count, local_width)
    cquery_grad = jnp.einsum(
        "sd,se->de", normed_cross, query_grad_low, preferred_element_type=jnp.float32
    )
    ckeyval_grad = jnp.einsum(
        "ctd,gcte->gde", text_states, keyval_grad_low, preferred_element_type=jnp.float32
    )
    text_part = jnp.einsum(
        "gcte,gde->ctd", keyval_grad_low, cross_keyval, preferred_element_type=jnp.float32
    )
    query_pieces = direct_gather(query_grad_low, "tensor")
    cross_sum = gathered_sum(query_pieces, cross_query_all, "gse,gde->gsd")
    text_grad = lax.psum(text_part.astype(jnp.bfloat16), "tensor").astype(jnp.float32)
    cross_back = norm_back(after_self, cross_gain, cross_bias, cross_sum)
    self_grad_rows = cross_grad_rows + cross_back[0]
    feed_sums, self_grad_rows = lax.optimization_barrier((feed_sums, self_grad_rows))
    self_grad_low = self_grad_rows.astype(jnp.bfloat16)
    sout_grad = jnp.einsum(
        "sk,sd->kd", self_flat, self_grad_low, preferred_element_type=jnp.float32
    )
    self_heads_grad = jnp.einsum(
        "sd,kd->sk", self_grad_low, self_out, preferred_element_type=jnp.float32
    ).astype(jnp.bfloat16)
    self_heads_grad = self_heads_grad.reshape(clip_count, slot_len, head_count, HEAD)

    def self_clip_back(entries):
        return attend_back(
            entries[0],
            entries[1],
            entries[2],
            entries[3],
            entries[4],
            entries[5],
            True,
            score_scale,
        )

    self_query_heads, self_key_heads, self_value_heads = lax.map(
        self_clip_back,
        (projected[0], projected[1], projected[2], self_log, self_heads_grad, frame_len),
    )
    projection_gradient = jnp.stack((self_query_heads, self_key_heads, self_value_heads)).astype(
        jnp.bfloat16
    )
    projection_gradient = projection_gradient.reshape(3, row_total, local_width)
    qkv_grad = jnp.einsum(
        "sd,cse->cde", normed_self, projection_gradient, preferred_element_type=jnp.float32
    )
    self_input_part = jnp.einsum(
        "cse,cde->sd", projection_gradient, self_qkv, preferred_element_type=jnp.float32
    )
    self_back = norm_back(inputs, self_gain, self_bias, direct_total(self_input_part))
    frames_grad = self_grad_rows + self_back[0]
    gain_terms = (
        self_back[1],
        self_back[2],
        cross_back[1],
        cross_back[2],
        feed_back[1],
        feed_back[2],
    )
    summed = (
        lax.psum(gain_terms[0].astype(jnp.bfloat16), "dp").astype(jnp.float32),
        lax.psum(gain_terms[1].astype(jnp.bfloat16), "dp").astype(jnp.float32),
        lax.psum(gain_terms[2].astype(jnp.bfloat16), "dp").astype(jnp.float32),
        lax.psum(gain_terms[3].astype(jnp.bfloat16), "dp").astype(jnp.float32),
        lax.psum(gain_terms[4].astype(jnp.bfloat16), "dp").astype(jnp.float32),
        lax.psum(gain_terms[5].astype(jnp.bfloat16), "dp").astype(jnp.float32),
        lax.psum(qkv_grad.astype(jnp.bfloat16), "dp").astype(jnp.float32),
        lax.psum(sout_grad.astype(jnp.bfloat16), "dp").astype(jnp.float32),
        lax.psum(cquery_grad.astype(jnp.bfloat16), "dp").astype(jnp.float32),
        lax.psum(ckeyval_grad.astype(jnp.bfloat16), "dp").astype(jnp.float32),
        lax.psum(cout_grad.astype(jnp.bfloat16), "dp").astype(jnp.float32),
        feed_sums[0],
        feed_sums[1],
    )
    return (
        block_out.reshape(clip_count, slot_len, model_width),
        frames_grad.reshape(clip_count, slot_len, model_width),
        text_grad,
        summed[0],
        summed[1],
        summed[2],
        summed[3],
        summed[4],
        summed[5],
        summed[6],
        summed[7],
        summed[8],
        summed[9],
        summed[10],
        summed[11],
        summed[12],
    )


def solution(mesh):
    return jax.shard_map(
        local,
        mesh=mesh,
        in_specs=(
            P("dp", None, None),
            P("dp", None, None),
            P("dp"),
            P("dp"),
            P(),
            P(),
            P(),
            P(),
            P(),
            P(),
            P(None, None, "tensor"),
            P("tensor", None),
            P(None, "tensor"),
            P(None, None, "tensor"),
            P("tensor", None),
            P(None, "tensor"),
            P("tensor", None),
            P("dp", None, None),
        ),
        out_specs=(
            P("dp", None, None),
            P("dp", None, None),
            P("dp", None, None),
            P(),
            P(),
            P(),
            P(),
            P(),
            P(),
            P(None, None, "tensor"),
            P("tensor", None),
            P(None, "tensor"),
            P(None, None, "tensor"),
            P("tensor", None),
            P(None, "tensor"),
            P("tensor", None),
        ),
        check_vma=False,
    )
```

```python
import jax
import jax.numpy as jnp
from jax import lax
from jax.sharding import PartitionSpec as P

HEAD = 64


EPSILON = 1e-05
MASKED = -1e30


def layer_norm(inputs, norm_gain, norm_bias):
    row_mean = jnp.mean(inputs, axis=-1, keepdims=True)
    centred = inputs - row_mean
    spread = jnp.mean(centred * centred, axis=-1, keepdims=True)
    return centred * lax.rsqrt(spread + EPSILON) * norm_gain + norm_bias


def norm_back(inputs, norm_gain, norm_bias, upstream):
    _, pullback = jax.vjp(layer_norm, inputs, norm_gain, norm_bias)
    return pullback(upstream)


def gelu_exact(inputs):
    return jax.nn.gelu(inputs, approximate=False)


def masked_scores(portion, offset, key_rows, key_limit, causal, score_scale):
    scores = (
        jnp.einsum("bhe,khe->hbk", portion, key_rows, preferred_element_type=jnp.float32)
        * score_scale
    )
    key_pos = jnp.arange(key_rows.shape[0])
    allowed = key_pos[None, :] < key_limit
    if causal:
        allowed = allowed & (key_pos[None, :] <= offset + jnp.arange(portion.shape[0])[:, None])
    return jnp.where(allowed[None], scores, MASKED)


def attend(queries, key_rows, values, key_limit, causal, score_scale):
    row_count, head_count, head_size = queries.shape
    block_len = min(512, row_count)
    portions = queries.reshape(row_count // block_len, block_len, head_count, head_size)
    offsets = jnp.arange(row_count // block_len) * block_len

    def one_block(entries):
        portion, offset = entries
        scores = masked_scores(portion, offset, key_rows, key_limit, causal, score_scale)
        row_max = jnp.max(scores, axis=-1, keepdims=True)
        unnormed = jnp.exp(scores - row_max)
        row_sum = jnp.sum(unnormed, axis=-1, keepdims=True)
        probs_low = (unnormed / row_sum).astype(jnp.bfloat16)
        result = jnp.einsum("hbk,khe->bhe", probs_low, values, preferred_element_type=jnp.float32)
        return (result.astype(jnp.bfloat16), row_max[..., 0] + jnp.log(row_sum[..., 0]))

    result, log_total = lax.map(one_block, (portions, offsets))
    return (result.reshape(row_count, head_count, head_size), log_total)


def attend_back(queries, key_rows, values, log_total, out_grad, key_limit, causal, score_scale):
    row_count, head_count, head_size = queries.shape
    block_len = min(512, row_count)
    portions = queries.reshape(row_count // block_len, block_len, head_count, head_size)
    grad_parts = out_grad.reshape(row_count // block_len, block_len, head_count, head_size)
    offsets = jnp.arange(row_count // block_len) * block_len

    def one_block(carry, entries):
        key_grad, value_grad = carry
        portion, grad_part, log_part, offset = entries
        scores = masked_scores(portion, offset, key_rows, key_limit, causal, score_scale)
        probs = jnp.exp(scores - log_part[..., None])
        probs_grad = jnp.einsum(
            "bhe,khe->hbk", grad_part, values, preferred_element_type=jnp.float32
        )
        row_dot = jnp.sum(probs * probs_grad, axis=-1, keepdims=True)
        scores_grad = (probs * (probs_grad - row_dot)).astype(jnp.bfloat16)
        value_grad = value_grad + jnp.einsum(
            "hbk,bhe->khe",
            probs.astype(jnp.bfloat16),
            grad_part,
            preferred_element_type=jnp.float32,
        )
        key_grad = (
            key_grad
            + jnp.einsum("hbk,bhe->khe", scores_grad, portion, preferred_element_type=jnp.float32)
            * score_scale
        )
        query_grad = (
            jnp.einsum("hbk,khe->bhe", scores_grad, key_rows, preferred_element_type=jnp.float32)
            * score_scale
        )
        return ((key_grad, value_grad), query_grad)

    empty = jnp.zeros(key_rows.shape, jnp.float32)
    (key_grad, value_grad), query_grad = lax.scan(
        one_block, (empty, empty), (portions, grad_parts, log_total, offsets)
    )
    return (query_grad.reshape(row_count, head_count, head_size), key_grad, value_grad)


def head_total(partial_value):
    return lax.psum(partial_value.astype(jnp.bfloat16), "tensor").astype(jnp.float32)


def relay_gather(block, axis):
    count = lax.axis_size(axis)
    me = lax.axis_index(axis)
    out = jnp.zeros((count + 1,) + block.shape, block.dtype)
    out = lax.dynamic_update_index_in_dim(out, block, me, 0)
    from_left, from_right = block, block
    for k in range(1, count):
        from_left = lax.ppermute(from_left, axis, [(i, i + 1) for i in range(k - 1, count - 1)])
        from_right = lax.ppermute(from_right, axis, [(i, i - 1) for i in range(1, count - k + 1)])
        out = lax.dynamic_update_index_in_dim(
            out, from_left, jnp.where(me - k >= 0, me - k, count), 0
        )
        out = lax.dynamic_update_index_in_dim(
            out, from_right, jnp.where(me + k < count, me + k, count), 0
        )
    return out[:count]


def relay_scatter(value, axis):
    count = lax.axis_size(axis)
    me = lax.axis_index(axis)
    shards = value.reshape((count, value.shape[0] // count) + value.shape[1:])

    def pick(index):
        return lax.dynamic_index_in_dim(shards, jnp.clip(index, 0, count - 1), 0, keepdims=False)

    to_right = to_left = None
    for k in range(1, count):
        send_right = pick(me + count - k).astype(jnp.float32)
        send_left = pick(me - (count - k)).astype(jnp.float32)
        if to_right is not None:
            send_right = send_right + to_right.astype(jnp.float32)
            send_left = send_left + to_left.astype(jnp.float32)
        to_right = lax.ppermute(
            send_right.astype(value.dtype), axis, [(i, i + 1) for i in range(min(k, count - 1))]
        )
        to_left = lax.ppermute(
            send_left.astype(value.dtype), axis, [(i, i - 1) for i in range(max(count - k, 1), count)]
        )
    total = pick(me).astype(jnp.float32)
    if to_right is not None:
        total = total + to_right.astype(jnp.float32) + to_left.astype(jnp.float32)
    return total.astype(value.dtype)


def relay_total(partial_value):
    low_value = partial_value.astype(jnp.bfloat16)
    reduced = relay_scatter(low_value, "tensor")
    return relay_gather(reduced, "tensor").reshape(low_value.shape).astype(jnp.float32)


def gathered_sum(pieces, weights, spec):
    partial_value = jnp.einsum(spec, pieces, weights, preferred_element_type=jnp.float32)
    return jnp.sum(partial_value.astype(jnp.bfloat16).astype(jnp.float32), axis=0)


def local(
    frames,
    text_states,
    frame_len,
    text_token_length,
    self_gain,
    self_bias,
    cross_gain,
    cross_bias,
    feed_gain,
    feed_bias,
    self_qkv,
    self_out,
    cross_query,
    cross_keyval,
    cross_out,
    feed_up,
    feed_down,
    cotangent,
):
    clip_count, slot_len, model_width = frames.shape
    text_count = text_states.shape[1]
    local_width = self_out.shape[0]
    head_count = local_width // HEAD
    score_scale = HEAD ** (-0.5)
    row_total = clip_count * slot_len
    inputs = frames.reshape(row_total, model_width).astype(jnp.float32)
    out_grad = cotangent.reshape(row_total, model_width)
    normed_self = layer_norm(inputs, self_gain, self_bias).astype(jnp.bfloat16)
    projected = jnp.einsum(
        "sd,cde->cse", normed_self, self_qkv, preferred_element_type=jnp.float32
    ).astype(jnp.bfloat16)
    projected = projected.reshape(3, clip_count, slot_len, head_count, HEAD)

    def self_clip(entries):
        return attend(entries[0], entries[1], entries[2], entries[3], True, score_scale)

    self_heads, self_log = lax.map(self_clip, (projected[0], projected[1], projected[2], frame_len))
    self_flat = self_heads.reshape(row_total, local_width)
    self_out_all = lax.all_gather(self_out, "tensor")
    cross_out_all = lax.all_gather(cross_out, "tensor")
    cross_query_all = lax.all_gather(cross_query, "tensor")
    self_pieces = relay_gather(self_flat, "tensor")
    after_self = inputs + gathered_sum(self_pieces, self_out_all, "gsk,gkd->gsd")
    normed_cross = layer_norm(after_self, cross_gain, cross_bias).astype(jnp.bfloat16)
    cross_queries = jnp.dot(normed_cross, cross_query, preferred_element_type=jnp.float32).astype(
        jnp.bfloat16
    )
    cross_queries = cross_queries.reshape(clip_count, slot_len, head_count, HEAD)
    text_proj = jnp.einsum(
        "ctd,gde->gcte", text_states, cross_keyval, preferred_element_type=jnp.float32
    ).astype(jnp.bfloat16)
    text_proj = text_proj.reshape(2, clip_count, text_count, head_count, HEAD)

    def cross_clip(entries):
        return attend(entries[0], entries[1], entries[2], entries[3], False, score_scale)

    cross_heads, cross_log = lax.map(
        cross_clip, (cross_queries, text_proj[0], text_proj[1], text_token_length)
    )
    cross_flat = cross_heads.reshape(row_total, local_width)
    cross_pieces = relay_gather(cross_flat, "tensor")
    after_cross = after_self + gathered_sum(cross_pieces, cross_out_all, "gsk,gkd->gsd")
    normed_feed = layer_norm(after_cross, feed_gain, feed_bias).astype(jnp.bfloat16)
    upward = jnp.dot(normed_feed, feed_up, preferred_element_type=jnp.float32)
    active = gelu_exact(upward).astype(jnp.bfloat16)
    feed_part = jnp.dot(active, feed_down, preferred_element_type=jnp.float32)
    block_out = (after_cross + relay_total(feed_part)).astype(jnp.bfloat16)
    active_grad = jnp.einsum("sd,kd->sk", out_grad, feed_down, preferred_element_type=jnp.float32)
    _, gelu_pull = jax.vjp(gelu_exact, upward)
    upward_grad = gelu_pull(active_grad)[0].astype(jnp.bfloat16)
    downward_gradient = jnp.einsum(
        "sk,sd->kd", active, out_grad, preferred_element_type=jnp.float32
    )
    up_grad = jnp.einsum("sd,sk->dk", normed_feed, upward_grad, preferred_element_type=jnp.float32)
    feed_sums = (
        lax.psum(up_grad.astype(jnp.bfloat16), "dp").astype(jnp.float32),
        lax.psum(downward_gradient.astype(jnp.bfloat16), "dp").astype(jnp.float32),
    )
    feed_input_part = jnp.einsum(
        "sk,dk->sd", upward_grad, feed_up, preferred_element_type=jnp.float32
    )
    feed_back = norm_back(after_cross, feed_gain, feed_bias, relay_total(feed_input_part))
    cross_grad_rows = out_grad.astype(jnp.float32) + feed_back[0]
    cross_grad_low = cross_grad_rows.astype(jnp.bfloat16)
    cout_grad = jnp.einsum(
        "sk,sd->kd", cross_flat, cross_grad_low, preferred_element_type=jnp.float32
    )
    cross_heads_grad = jnp.einsum(
        "sd,kd->sk", cross_grad_low, cross_out, preferred_element_type=jnp.float32
    ).astype(jnp.bfloat16)
    cross_heads_grad = cross_heads_grad.reshape(clip_count, slot_len, head_count, HEAD)

    def cross_clip_back(entries):
        return attend_back(
            entries[0],
            entries[1],
            entries[2],
            entries[3],
            entries[4],
            entries[5],
            False,
            score_scale,
        )

    cquery_heads, ckey_heads, cvalue_heads = lax.map(
        cross_clip_back,
        (cross_queries, text_proj[0], text_proj[1], cross_log, cross_heads_grad, text_token_length),
    )
    query_grad_low = cquery_heads.reshape(row_total, local_width).astype(jnp.bfloat16)
    keyval_grad_low = jnp.stack((ckey_heads, cvalue_heads)).astype(jnp.bfloat16)
    keyval_grad_low = keyval_grad_low.reshape(2, clip_count, text_count, local_width)
    cquery_grad = jnp.einsum(
        "sd,se->de", normed_cross, query_grad_low, preferred_element_type=jnp.float32
    )
    ckeyval_grad = jnp.einsum(
        "ctd,gcte->gde", text_states, keyval_grad_low, preferred_element_type=jnp.float32
    )
    text_part = jnp.einsum(
        "gcte,gde->ctd", keyval_grad_low, cross_keyval, preferred_element_type=jnp.float32
    )
    query_pieces = relay_gather(query_grad_low, "tensor")
    cross_sum = gathered_sum(query_pieces, cross_query_all, "gse,gde->gsd")
    text_grad = lax.psum(text_part.astype(jnp.bfloat16), "tensor").astype(jnp.float32)
    cross_back = norm_back(after_self, cross_gain, cross_bias, cross_sum)
    self_grad_rows = cross_grad_rows + cross_back[0]
    feed_sums, self_grad_rows = lax.optimization_barrier((feed_sums, self_grad_rows))
    self_grad_low = self_grad_rows.astype(jnp.bfloat16)
    sout_grad = jnp.einsum(
        "sk,sd->kd", self_flat, self_grad_low, preferred_element_type=jnp.float32
    )
    self_heads_grad = jnp.einsum(
        "sd,kd->sk", self_grad_low, self_out, preferred_element_type=jnp.float32
    ).astype(jnp.bfloat16)
    self_heads_grad = self_heads_grad.reshape(clip_count, slot_len, head_count, HEAD)

    def self_clip_back(entries):
        return attend_back(
            entries[0],
            entries[1],
            entries[2],
            entries[3],
            entries[4],
            entries[5],
            True,
            score_scale,
        )

    self_query_heads, self_key_heads, self_value_heads = lax.map(
        self_clip_back,
        (projected[0], projected[1], projected[2], self_log, self_heads_grad, frame_len),
    )
    projection_gradient = jnp.stack((self_query_heads, self_key_heads, self_value_heads)).astype(
        jnp.bfloat16
    )
    projection_gradient = projection_gradient.reshape(3, row_total, local_width)
    qkv_grad = jnp.einsum(
        "sd,cse->cde", normed_self, projection_gradient, preferred_element_type=jnp.float32
    )
    self_input_part = jnp.einsum(
        "cse,cde->sd", projection_gradient, self_qkv, preferred_element_type=jnp.float32
    )
    self_back = norm_back(inputs, self_gain, self_bias, relay_total(self_input_part))
    frames_grad = self_grad_rows + self_back[0]
    gain_terms = (
        self_back[1],
        self_back[2],
        cross_back[1],
        cross_back[2],
        feed_back[1],
        feed_back[2],
    )
    summed = (
        lax.psum(gain_terms[0].astype(jnp.bfloat16), "dp").astype(jnp.float32),
        lax.psum(gain_terms[1].astype(jnp.bfloat16), "dp").astype(jnp.float32),
        lax.psum(gain_terms[2].astype(jnp.bfloat16), "dp").astype(jnp.float32),
        lax.psum(gain_terms[3].astype(jnp.bfloat16), "dp").astype(jnp.float32),
        lax.psum(gain_terms[4].astype(jnp.bfloat16), "dp").astype(jnp.float32),
        lax.psum(gain_terms[5].astype(jnp.bfloat16), "dp").astype(jnp.float32),
        lax.psum(qkv_grad.astype(jnp.bfloat16), "dp").astype(jnp.float32),
        lax.psum(sout_grad.astype(jnp.bfloat16), "dp").astype(jnp.float32),
        lax.psum(cquery_grad.astype(jnp.bfloat16), "dp").astype(jnp.float32),
        lax.psum(ckeyval_grad.astype(jnp.bfloat16), "dp").astype(jnp.float32),
        lax.psum(cout_grad.astype(jnp.bfloat16), "dp").astype(jnp.float32),
        feed_sums[0],
        feed_sums[1],
    )
    return (
        block_out.reshape(clip_count, slot_len, model_width),
        frames_grad.reshape(clip_count, slot_len, model_width),
        text_grad,
        summed[0],
        summed[1],
        summed[2],
        summed[3],
        summed[4],
        summed[5],
        summed[6],
        summed[7],
        summed[8],
        summed[9],
        summed[10],
        summed[11],
        summed[12],
    )


def solution(mesh):
    return jax.shard_map(
        local,
        mesh=mesh,
        in_specs=(
            P("dp", None, None),
            P("dp", None, None),
            P("dp"),
            P("dp"),
            P(),
            P(),
            P(),
            P(),
            P(),
            P(),
            P(None, None, "tensor"),
            P("tensor", None),
            P(None, "tensor"),
            P(None, None, "tensor"),
            P("tensor", None),
            P(None, "tensor"),
            P("tensor", None),
            P("dp", None, None),
        ),
        out_specs=(
            P("dp", None, None),
            P("dp", None, None),
            P("dp", None, None),
            P(),
            P(),
            P(),
            P(),
            P(),
            P(),
            P(None, None, "tensor"),
            P("tensor", None),
            P(None, "tensor"),
            P(None, None, "tensor"),
            P("tensor", None),
            P(None, "tensor"),
            P("tensor", None),
        ),
        check_vma=False,
    )
```

```python
import jax
import jax.numpy as jnp
from jax import lax
from jax.sharding import PartitionSpec as P

HEAD = 64


EPSILON = 1e-05
MASKED = -1e30


def layer_norm(inputs, norm_gain, norm_bias):
    row_mean = jnp.mean(inputs, axis=-1, keepdims=True)
    centred = inputs - row_mean
    spread = jnp.mean(centred * centred, axis=-1, keepdims=True)
    return centred * lax.rsqrt(spread + EPSILON) * norm_gain + norm_bias


def normalized(inputs):
    row_mean = jnp.mean(inputs, axis=-1, keepdims=True)
    centred = inputs - row_mean
    spread = jnp.mean(centred * centred, axis=-1, keepdims=True)
    return centred * lax.rsqrt(spread + EPSILON)


def norm_back(inputs, norm_gain, norm_bias, upstream):
    _, pullback = jax.vjp(layer_norm, inputs, norm_gain, norm_bias)
    return pullback(upstream)


def gelu_exact(inputs):
    return jax.nn.gelu(inputs, approximate=False)


def masked_scores(portion, offset, key_rows, key_limit, causal, score_scale):
    scores = (
        jnp.einsum("bhe,khe->hbk", portion, key_rows, preferred_element_type=jnp.float32)
        * score_scale
    )
    key_pos = jnp.arange(key_rows.shape[0])
    allowed = key_pos[None, :] < key_limit
    if causal:
        allowed = allowed & (key_pos[None, :] <= offset + jnp.arange(portion.shape[0])[:, None])
    return jnp.where(allowed[None], scores, MASKED)


def attend(queries, key_rows, values, key_limit, causal, score_scale):
    row_count, head_count, head_size = queries.shape
    block_len = min(512, row_count)
    portions = queries.reshape(row_count // block_len, block_len, head_count, head_size)
    offsets = jnp.arange(row_count // block_len) * block_len

    def one_block(entries):
        portion, offset = entries
        scores = masked_scores(portion, offset, key_rows, key_limit, causal, score_scale)
        row_max = jnp.max(scores, axis=-1, keepdims=True)
        unnormed = jnp.exp(scores - row_max)
        row_sum = jnp.sum(unnormed, axis=-1, keepdims=True)
        probs_low = (unnormed / row_sum).astype(jnp.bfloat16)
        result = jnp.einsum("hbk,khe->bhe", probs_low, values, preferred_element_type=jnp.float32)
        return (result.astype(jnp.bfloat16), row_max[..., 0] + jnp.log(row_sum[..., 0]))

    result, log_total = lax.map(one_block, (portions, offsets))
    return (result.reshape(row_count, head_count, head_size), log_total)


def attend_back(queries, key_rows, values, log_total, out_grad, key_limit, causal, score_scale):
    row_count, head_count, head_size = queries.shape
    block_len = min(512, row_count)
    portions = queries.reshape(row_count // block_len, block_len, head_count, head_size)
    grad_parts = out_grad.reshape(row_count // block_len, block_len, head_count, head_size)
    offsets = jnp.arange(row_count // block_len) * block_len

    def one_block(carry, entries):
        key_grad, value_grad = carry
        portion, grad_part, log_part, offset = entries
        scores = masked_scores(portion, offset, key_rows, key_limit, causal, score_scale)
        probs = jnp.exp(scores - log_part[..., None])
        probs_grad = jnp.einsum(
            "bhe,khe->hbk", grad_part, values, preferred_element_type=jnp.float32
        )
        row_dot = jnp.sum(probs * probs_grad, axis=-1, keepdims=True)
        scores_grad = (probs * (probs_grad - row_dot)).astype(jnp.bfloat16)
        value_grad = value_grad + jnp.einsum(
            "hbk,bhe->khe",
            probs.astype(jnp.bfloat16),
            grad_part,
            preferred_element_type=jnp.float32,
        )
        key_grad = (
            key_grad
            + jnp.einsum("hbk,bhe->khe", scores_grad, portion, preferred_element_type=jnp.float32)
            * score_scale
        )
        query_grad = (
            jnp.einsum("hbk,khe->bhe", scores_grad, key_rows, preferred_element_type=jnp.float32)
            * score_scale
        )
        return ((key_grad, value_grad), query_grad)

    empty = jnp.zeros(key_rows.shape, jnp.float32)
    (key_grad, value_grad), query_grad = lax.scan(
        one_block, (empty, empty), (portions, grad_parts, log_total, offsets)
    )
    return (query_grad.reshape(row_count, head_count, head_size), key_grad, value_grad)


def head_total(partial_value):
    return lax.psum(partial_value.astype(jnp.bfloat16), "tensor").astype(jnp.float32)


def relay_gather(block, axis):
    count = lax.axis_size(axis)
    me = lax.axis_index(axis)
    out = jnp.zeros((count + 1,) + block.shape, block.dtype)
    out = lax.dynamic_update_index_in_dim(out, block, me, 0)
    from_left, from_right = block, block
    for k in range(1, count):
        from_left = lax.ppermute(from_left, axis, [(i, i + 1) for i in range(k - 1, count - 1)])
        from_right = lax.ppermute(from_right, axis, [(i, i - 1) for i in range(1, count - k + 1)])
        out = lax.dynamic_update_index_in_dim(
            out, from_left, jnp.where(me - k >= 0, me - k, count), 0
        )
        out = lax.dynamic_update_index_in_dim(
            out, from_right, jnp.where(me + k < count, me + k, count), 0
        )
    return out[:count]


def relay_scatter(value, axis):
    count = lax.axis_size(axis)
    me = lax.axis_index(axis)
    shards = value.reshape((count, value.shape[0] // count) + value.shape[1:])

    def pick(index):
        return lax.dynamic_index_in_dim(shards, jnp.clip(index, 0, count - 1), 0, keepdims=False)

    to_right = to_left = None
    for k in range(1, count):
        send_right = pick(me + count - k).astype(jnp.float32)
        send_left = pick(me - (count - k)).astype(jnp.float32)
        if to_right is not None:
            send_right = send_right + to_right.astype(jnp.float32)
            send_left = send_left + to_left.astype(jnp.float32)
        to_right = lax.ppermute(
            send_right.astype(value.dtype), axis, [(i, i + 1) for i in range(min(k, count - 1))]
        )
        to_left = lax.ppermute(
            send_left.astype(value.dtype), axis, [(i, i - 1) for i in range(max(count - k, 1), count)]
        )
    total = pick(me).astype(jnp.float32)
    if to_right is not None:
        total = total + to_right.astype(jnp.float32) + to_left.astype(jnp.float32)
    return total.astype(value.dtype)


def relay_total(partial_value):
    low_value = partial_value.astype(jnp.bfloat16)
    reduced = relay_scatter(low_value, "tensor")
    return relay_gather(reduced, "tensor").reshape(low_value.shape).astype(jnp.float32)


def flat_psum(terms, axis):
    flat = jnp.concatenate([term.astype(jnp.bfloat16).reshape(-1) for term in terms])
    flat = lax.psum(flat, axis).astype(jnp.float32)
    out, start = [], 0
    for term in terms:
        out.append(flat[start : start + term.size].reshape(term.shape))
        start += term.size
    return out


def gathered_sum(pieces, weights, spec):
    partial_value = jnp.einsum(spec, pieces, weights, preferred_element_type=jnp.float32)
    return jnp.sum(partial_value.astype(jnp.bfloat16).astype(jnp.float32), axis=0)


def local(
    frames,
    text_states,
    frame_len,
    text_token_length,
    self_gain,
    self_bias,
    cross_gain,
    cross_bias,
    feed_gain,
    feed_bias,
    self_qkv,
    self_out,
    cross_query,
    cross_keyval,
    cross_out,
    feed_up,
    feed_down,
    cotangent,
):
    clip_count, slot_len, model_width = frames.shape
    text_count = text_states.shape[1]
    local_width = self_out.shape[0]
    head_count = local_width // HEAD
    score_scale = HEAD ** (-0.5)
    row_total = clip_count * slot_len
    inputs = frames.reshape(row_total, model_width).astype(jnp.float32)
    out_grad = cotangent.reshape(row_total, model_width)
    normed_self = layer_norm(inputs, self_gain, self_bias).astype(jnp.bfloat16)
    projected = jnp.einsum(
        "sd,cde->cse", normed_self, self_qkv, preferred_element_type=jnp.float32
    ).astype(jnp.bfloat16)
    projected = projected.reshape(3, clip_count, slot_len, head_count, HEAD)

    def self_clip(entries):
        return attend(entries[0], entries[1], entries[2], entries[3], True, score_scale)

    self_heads, self_log = lax.map(self_clip, (projected[0], projected[1], projected[2], frame_len))
    self_flat = self_heads.reshape(row_total, local_width)
    self_out_all = lax.all_gather(self_out, "tensor")
    cross_out_all = lax.all_gather(cross_out, "tensor")
    cross_query_all = lax.all_gather(cross_query, "tensor")
    self_pieces = relay_gather(self_flat, "tensor")
    after_self = inputs + gathered_sum(self_pieces, self_out_all, "gsk,gkd->gsd")
    normed_cross = layer_norm(after_self, cross_gain, cross_bias).astype(jnp.bfloat16)
    cross_queries = jnp.dot(normed_cross, cross_query, preferred_element_type=jnp.float32).astype(
        jnp.bfloat16
    )
    cross_queries = cross_queries.reshape(clip_count, slot_len, head_count, HEAD)
    text_proj = jnp.einsum(
        "ctd,gde->gcte", text_states, cross_keyval, preferred_element_type=jnp.float32
    ).astype(jnp.bfloat16)
    text_proj = text_proj.reshape(2, clip_count, text_count, head_count, HEAD)

    def cross_clip(entries):
        return attend(entries[0], entries[1], entries[2], entries[3], False, score_scale)

    cross_heads, cross_log = lax.map(
        cross_clip, (cross_queries, text_proj[0], text_proj[1], text_token_length)
    )
    cross_flat = cross_heads.reshape(row_total, local_width)
    cross_pieces = relay_gather(cross_flat, "tensor")
    after_cross = after_self + gathered_sum(cross_pieces, cross_out_all, "gsk,gkd->gsd")
    normed_feed = layer_norm(after_cross, feed_gain, feed_bias).astype(jnp.bfloat16)
    upward = jnp.dot(normed_feed, feed_up, preferred_element_type=jnp.float32)
    active = gelu_exact(upward).astype(jnp.bfloat16)
    feed_part = jnp.dot(active, feed_down, preferred_element_type=jnp.float32)
    feed_low = feed_part.astype(jnp.bfloat16)
    active_grad = jnp.einsum("sd,kd->sk", out_grad, feed_down, preferred_element_type=jnp.float32)
    _, gelu_pull = jax.vjp(gelu_exact, upward)
    upward_grad = gelu_pull(active_grad)[0].astype(jnp.bfloat16)
    downward_gradient = jnp.einsum(
        "sk,sd->kd", active, out_grad, preferred_element_type=jnp.float32
    )
    up_grad = jnp.einsum("sd,sk->dk", normed_feed, upward_grad, preferred_element_type=jnp.float32)
    feed_input_part = jnp.einsum(
        "sk,dk->sd", upward_grad, feed_up, preferred_element_type=jnp.float32
    )
    feed_back = norm_back(after_cross, feed_gain, feed_bias, relay_total(feed_input_part))
    feed_sums = flat_psum((up_grad, downward_gradient, feed_back[1], feed_back[2]), "dp")
    cross_grad_rows = out_grad.astype(jnp.float32) + feed_back[0]
    cross_grad_low = cross_grad_rows.astype(jnp.bfloat16)
    cout_grad = jnp.einsum(
        "sk,sd->kd", cross_flat, cross_grad_low, preferred_element_type=jnp.float32
    )
    cross_heads_grad = jnp.einsum(
        "sd,kd->sk", cross_grad_low, cross_out, preferred_element_type=jnp.float32
    ).astype(jnp.bfloat16)
    cross_heads_grad = cross_heads_grad.reshape(clip_count, slot_len, head_count, HEAD)

    def cross_clip_back(entries):
        return attend_back(
            entries[0],
            entries[1],
            entries[2],
            entries[3],
            entries[4],
            entries[5],
            False,
            score_scale,
        )

    cquery_heads, ckey_heads, cvalue_heads = lax.map(
        cross_clip_back,
        (cross_queries, text_proj[0], text_proj[1], cross_log, cross_heads_grad, text_token_length),
    )
    query_grad_low = cquery_heads.reshape(row_total, local_width).astype(jnp.bfloat16)
    feed_low, query_grad_low = lax.optimization_barrier((feed_low, query_grad_low))
    block_out = (after_cross + lax.psum(feed_low, "tensor").astype(jnp.float32)).astype(
        jnp.bfloat16
    )
    keyval_grad_low = jnp.stack((ckey_heads, cvalue_heads)).astype(jnp.bfloat16)
    keyval_grad_low = keyval_grad_low.reshape(2, clip_count, text_count, local_width)
    cquery_grad = jnp.einsum(
        "sd,se->de", normed_cross, query_grad_low, preferred_element_type=jnp.float32
    )
    ckeyval_grad = jnp.einsum(
        "ctd,gcte->gde", text_states, keyval_grad_low, preferred_element_type=jnp.float32
    )
    text_part = jnp.einsum(
        "gcte,gde->ctd", keyval_grad_low, cross_keyval, preferred_element_type=jnp.float32
    )
    query_pieces = relay_gather(query_grad_low, "tensor")
    cross_sum = gathered_sum(query_pieces, cross_query_all, "gse,gde->gsd")
    text_grad = lax.psum(text_part.astype(jnp.bfloat16), "tensor").astype(jnp.float32)
    cross_back = norm_back(after_self, cross_gain, cross_bias, cross_sum)
    self_grad_rows = cross_grad_rows + cross_back[0]
    feed_sums, self_grad_rows = lax.optimization_barrier((feed_sums, self_grad_rows))
    self_grad_low = self_grad_rows.astype(jnp.bfloat16)
    sout_grad = jnp.einsum(
        "sk,sd->kd", self_flat, self_grad_low, preferred_element_type=jnp.float32
    )
    self_heads_grad = jnp.einsum(
        "sd,kd->sk", self_grad_low, self_out, preferred_element_type=jnp.float32
    ).astype(jnp.bfloat16)
    self_heads_grad = self_heads_grad.reshape(clip_count, slot_len, head_count, HEAD)

    def self_clip_back(entries):
        return attend_back(
            entries[0],
            entries[1],
            entries[2],
            entries[3],
            entries[4],
            entries[5],
            True,
            score_scale,
        )

    self_query_heads, self_key_heads, self_value_heads = lax.map(
        self_clip_back,
        (projected[0], projected[1], projected[2], self_log, self_heads_grad, frame_len),
    )
    projection_gradient = jnp.stack((self_query_heads, self_key_heads, self_value_heads)).astype(
        jnp.bfloat16
    )
    projection_gradient = projection_gradient.reshape(3, row_total, local_width)
    qkv_grad = jnp.einsum(
        "sd,cse->cde", normed_self, projection_gradient, preferred_element_type=jnp.float32
    )
    self_input_part = jnp.einsum(
        "cse,cde->sd", projection_gradient, self_qkv, preferred_element_type=jnp.float32
    )
    self_back = norm_back(inputs, self_gain, self_bias, relay_total(self_input_part))
    own_part = self_input_part.astype(jnp.bfloat16).astype(jnp.float32)
    self_norm_terms = lax.psum(
        jnp.stack((jnp.sum(own_part * normalized(inputs), axis=0), jnp.sum(own_part, axis=0))),
        ("dp", "tensor"),
    )
    frames_grad = self_grad_rows + self_back[0]
    gain_terms = (
        self_back[1],
        self_back[2],
        cross_back[1],
        cross_back[2],
        feed_back[1],
        feed_back[2],
    )
    late_sums = flat_psum(
        (qkv_grad, sout_grad, cquery_grad, ckeyval_grad, cout_grad, cross_back[1], cross_back[2]),
        "dp",
    )
    summed = (
        self_norm_terms[0],
        self_norm_terms[1],
        late_sums[5],
        late_sums[6],
        feed_sums[2],
        feed_sums[3],
        late_sums[0],
        late_sums[1],
        late_sums[2],
        late_sums[3],
        late_sums[4],
        feed_sums[0],
        feed_sums[1],
    )
    return (
        block_out.reshape(clip_count, slot_len, model_width),
        frames_grad.reshape(clip_count, slot_len, model_width),
        text_grad,
        summed[0],
        summed[1],
        summed[2],
        summed[3],
        summed[4],
        summed[5],
        summed[6],
        summed[7],
        summed[8],
        summed[9],
        summed[10],
        summed[11],
        summed[12],
    )


def solution(mesh):
    return jax.shard_map(
        local,
        mesh=mesh,
        in_specs=(
            P("dp", None, None),
            P("dp", None, None),
            P("dp"),
            P("dp"),
            P(),
            P(),
            P(),
            P(),
            P(),
            P(),
            P(None, None, "tensor"),
            P("tensor", None),
            P(None, "tensor"),
            P(None, None, "tensor"),
            P("tensor", None),
            P(None, "tensor"),
            P("tensor", None),
            P("dp", None, None),
        ),
        out_specs=(
            P("dp", None, None),
            P("dp", None, None),
            P("dp", None, None),
            P(),
            P(),
            P(),
            P(),
            P(),
            P(),
            P(None, None, "tensor"),
            P("tensor", None),
            P(None, "tensor"),
            P(None, None, "tensor"),
            P("tensor", None),
            P(None, "tensor"),
            P("tensor", None),
        ),
        check_vma=False,
    )
```

```python
import jax
import jax.numpy as jnp
from jax import lax
from jax.sharding import PartitionSpec as P

HEAD = 64


EPSILON = 1e-05
MASKED = -1e30


def layer_norm(inputs, norm_gain, norm_bias):
    row_mean = jnp.mean(inputs, axis=-1, keepdims=True)
    centred = inputs - row_mean
    spread = jnp.mean(centred * centred, axis=-1, keepdims=True)
    return centred * lax.rsqrt(spread + EPSILON) * norm_gain + norm_bias


def normalized(inputs):
    row_mean = jnp.mean(inputs, axis=-1, keepdims=True)
    centred = inputs - row_mean
    spread = jnp.mean(centred * centred, axis=-1, keepdims=True)
    return centred * lax.rsqrt(spread + EPSILON)


def norm_back(inputs, norm_gain, norm_bias, upstream):
    _, pullback = jax.vjp(layer_norm, inputs, norm_gain, norm_bias)
    return pullback(upstream)


def gelu_exact(inputs):
    return jax.nn.gelu(inputs, approximate=False)


def masked_scores(portion, offset, key_rows, key_limit, causal, score_scale):
    scores = (
        jnp.einsum("bhe,khe->hbk", portion, key_rows, preferred_element_type=jnp.float32)
        * score_scale
    )
    key_pos = jnp.arange(key_rows.shape[0])
    allowed = key_pos[None, :] < key_limit
    if causal:
        allowed = allowed & (key_pos[None, :] <= offset + jnp.arange(portion.shape[0])[:, None])
    return jnp.where(allowed[None], scores, MASKED)


def attend(queries, key_rows, values, key_limit, causal, score_scale):
    row_count, head_count, head_size = queries.shape
    block_len = min(512, row_count)
    portions = queries.reshape(row_count // block_len, block_len, head_count, head_size)
    offsets = jnp.arange(row_count // block_len) * block_len

    def one_block(entries):
        portion, offset = entries
        scores = masked_scores(portion, offset, key_rows, key_limit, causal, score_scale)
        row_max = jnp.max(scores, axis=-1, keepdims=True)
        unnormed = jnp.exp(scores - row_max)
        row_sum = jnp.sum(unnormed, axis=-1, keepdims=True)
        probs_low = (unnormed / row_sum).astype(jnp.bfloat16)
        result = jnp.einsum("hbk,khe->bhe", probs_low, values, preferred_element_type=jnp.float32)
        return (result.astype(jnp.bfloat16), row_max[..., 0] + jnp.log(row_sum[..., 0]))

    result, log_total = lax.map(one_block, (portions, offsets))
    return (result.reshape(row_count, head_count, head_size), log_total)


def attend_back(queries, key_rows, values, log_total, out_grad, key_limit, causal, score_scale):
    row_count, head_count, head_size = queries.shape
    block_len = min(512, row_count)
    portions = queries.reshape(row_count // block_len, block_len, head_count, head_size)
    grad_parts = out_grad.reshape(row_count // block_len, block_len, head_count, head_size)
    offsets = jnp.arange(row_count // block_len) * block_len

    def one_block(carry, entries):
        key_grad, value_grad = carry
        portion, grad_part, log_part, offset = entries
        scores = masked_scores(portion, offset, key_rows, key_limit, causal, score_scale)
        probs = jnp.exp(scores - log_part[..., None])
        probs_grad = jnp.einsum(
            "bhe,khe->hbk", grad_part, values, preferred_element_type=jnp.float32
        )
        row_dot = jnp.sum(probs * probs_grad, axis=-1, keepdims=True)
        scores_grad = (probs * (probs_grad - row_dot)).astype(jnp.bfloat16)
        value_grad = value_grad + jnp.einsum(
            "hbk,bhe->khe",
            probs.astype(jnp.bfloat16),
            grad_part,
            preferred_element_type=jnp.float32,
        )
        key_grad = (
            key_grad
            + jnp.einsum("hbk,bhe->khe", scores_grad, portion, preferred_element_type=jnp.float32)
            * score_scale
        )
        query_grad = (
            jnp.einsum("hbk,khe->bhe", scores_grad, key_rows, preferred_element_type=jnp.float32)
            * score_scale
        )
        return ((key_grad, value_grad), query_grad)

    empty = jnp.zeros(key_rows.shape, jnp.float32)
    (key_grad, value_grad), query_grad = lax.scan(
        one_block, (empty, empty), (portions, grad_parts, log_total, offsets)
    )
    return (query_grad.reshape(row_count, head_count, head_size), key_grad, value_grad)


def head_total(partial_value):
    return lax.psum(partial_value.astype(jnp.bfloat16), "tensor").astype(jnp.float32)


def relay_gather(block, axis):
    count = lax.axis_size(axis)
    me = lax.axis_index(axis)
    out = jnp.zeros((count + 1,) + block.shape, block.dtype)
    out = lax.dynamic_update_index_in_dim(out, block, me, 0)
    from_left, from_right = block, block
    for k in range(1, count):
        from_left = lax.ppermute(from_left, axis, [(i, i + 1) for i in range(k - 1, count - 1)])
        from_right = lax.ppermute(from_right, axis, [(i, i - 1) for i in range(1, count - k + 1)])
        out = lax.dynamic_update_index_in_dim(
            out, from_left, jnp.where(me - k >= 0, me - k, count), 0
        )
        out = lax.dynamic_update_index_in_dim(
            out, from_right, jnp.where(me + k < count, me + k, count), 0
        )
    return out[:count]


def relay_scatter(value, axis):
    count = lax.axis_size(axis)
    me = lax.axis_index(axis)
    shards = value.reshape((count, value.shape[0] // count) + value.shape[1:])

    def pick(index):
        return lax.dynamic_index_in_dim(shards, jnp.clip(index, 0, count - 1), 0, keepdims=False)

    to_right = to_left = None
    for k in range(1, count):
        send_right = pick(me + count - k).astype(jnp.float32)
        send_left = pick(me - (count - k)).astype(jnp.float32)
        if to_right is not None:
            send_right = send_right + to_right.astype(jnp.float32)
            send_left = send_left + to_left.astype(jnp.float32)
        to_right = lax.ppermute(
            send_right.astype(value.dtype), axis, [(i, i + 1) for i in range(min(k, count - 1))]
        )
        to_left = lax.ppermute(
            send_left.astype(value.dtype), axis, [(i, i - 1) for i in range(max(count - k, 1), count)]
        )
    total = pick(me).astype(jnp.float32)
    if to_right is not None:
        total = total + to_right.astype(jnp.float32) + to_left.astype(jnp.float32)
    return total.astype(value.dtype)


def relay_total(partial_value):
    low_value = partial_value.astype(jnp.bfloat16)
    reduced = relay_scatter(low_value, "tensor")
    return relay_gather(reduced, "tensor").reshape(low_value.shape).astype(jnp.float32)


def stacked_psum(matrix, rows, axis):
    pad = (-(matrix.shape[0] + len(rows))) % 16
    extra = jnp.stack(rows + [jnp.zeros_like(rows[0])] * pad)
    summed = lax.psum(jnp.concatenate([matrix, extra]).astype(jnp.bfloat16), axis)
    summed = summed.astype(jnp.float32)
    count = matrix.shape[0]
    return [summed[:count]] + [summed[count + i] for i in range(len(rows))]


def dp_sum(term):
    return lax.psum(term.astype(jnp.bfloat16), "dp").astype(jnp.float32)


def gathered_sum(pieces, weights, spec):
    partial_value = jnp.einsum(spec, pieces, weights, preferred_element_type=jnp.float32)
    return jnp.sum(partial_value.astype(jnp.bfloat16).astype(jnp.float32), axis=0)


def local(
    frames,
    text_states,
    frame_len,
    text_token_length,
    self_gain,
    self_bias,
    cross_gain,
    cross_bias,
    feed_gain,
    feed_bias,
    self_qkv,
    self_out,
    cross_query,
    cross_keyval,
    cross_out,
    feed_up,
    feed_down,
    cotangent,
):
    clip_count, slot_len, model_width = frames.shape
    text_count = text_states.shape[1]
    local_width = self_out.shape[0]
    head_count = local_width // HEAD
    score_scale = HEAD ** (-0.5)
    row_total = clip_count * slot_len
    inputs = frames.reshape(row_total, model_width).astype(jnp.float32)
    out_grad = cotangent.reshape(row_total, model_width)
    normed_self = layer_norm(inputs, self_gain, self_bias).astype(jnp.bfloat16)
    projected = jnp.einsum(
        "sd,cde->cse", normed_self, self_qkv, preferred_element_type=jnp.float32
    ).astype(jnp.bfloat16)
    projected = projected.reshape(3, clip_count, slot_len, head_count, HEAD)

    def self_clip(entries):
        return attend(entries[0], entries[1], entries[2], entries[3], True, score_scale)

    self_heads, self_log = lax.map(self_clip, (projected[0], projected[1], projected[2], frame_len))
    self_flat = self_heads.reshape(row_total, local_width)
    self_out_all = lax.all_gather(self_out, "tensor")
    cross_out_all = lax.all_gather(cross_out, "tensor")
    cross_query_all = lax.all_gather(cross_query, "tensor")
    self_pieces = relay_gather(self_flat, "tensor")
    after_self = inputs + gathered_sum(self_pieces, self_out_all, "gsk,gkd->gsd")
    normed_cross = layer_norm(after_self, cross_gain, cross_bias).astype(jnp.bfloat16)
    cross_queries = jnp.dot(normed_cross, cross_query, preferred_element_type=jnp.float32).astype(
        jnp.bfloat16
    )
    cross_queries = cross_queries.reshape(clip_count, slot_len, head_count, HEAD)
    text_proj = jnp.einsum(
        "ctd,gde->gcte", text_states, cross_keyval, preferred_element_type=jnp.float32
    ).astype(jnp.bfloat16)
    text_proj = text_proj.reshape(2, clip_count, text_count, head_count, HEAD)

    def cross_clip(entries):
        return attend(entries[0], entries[1], entries[2], entries[3], False, score_scale)

    cross_heads, cross_log = lax.map(
        cross_clip, (cross_queries, text_proj[0], text_proj[1], text_token_length)
    )
    cross_flat = cross_heads.reshape(row_total, local_width)
    cross_pieces = relay_gather(cross_flat, "tensor")
    after_cross = after_self + gathered_sum(cross_pieces, cross_out_all, "gsk,gkd->gsd")
    normed_feed = layer_norm(after_cross, feed_gain, feed_bias).astype(jnp.bfloat16)
    upward = jnp.dot(normed_feed, feed_up, preferred_element_type=jnp.float32)
    active = gelu_exact(upward).astype(jnp.bfloat16)
    feed_part = jnp.dot(active, feed_down, preferred_element_type=jnp.float32)
    feed_low = feed_part.astype(jnp.bfloat16)
    active_grad = jnp.einsum("sd,kd->sk", out_grad, feed_down, preferred_element_type=jnp.float32)
    _, gelu_pull = jax.vjp(gelu_exact, upward)
    upward_grad = gelu_pull(active_grad)[0].astype(jnp.bfloat16)
    downward_gradient = jnp.einsum(
        "sk,sd->kd", active, out_grad, preferred_element_type=jnp.float32
    )
    up_grad = jnp.einsum("sd,sk->dk", normed_feed, upward_grad, preferred_element_type=jnp.float32)
    feed_input_part = jnp.einsum(
        "sk,dk->sd", upward_grad, feed_up, preferred_element_type=jnp.float32
    )
    feed_back = norm_back(after_cross, feed_gain, feed_bias, relay_total(feed_input_part))
    feed_sums = [dp_sum(up_grad)] + stacked_psum(
        downward_gradient, [feed_back[1], feed_back[2]], "dp"
    )
    feed_sums = [feed_sums[0], feed_sums[1], feed_sums[2], feed_sums[3]]
    cross_grad_rows = out_grad.astype(jnp.float32) + feed_back[0]
    cross_grad_low = cross_grad_rows.astype(jnp.bfloat16)
    cout_grad = jnp.einsum(
        "sk,sd->kd", cross_flat, cross_grad_low, preferred_element_type=jnp.float32
    )
    cross_heads_grad = jnp.einsum(
        "sd,kd->sk", cross_grad_low, cross_out, preferred_element_type=jnp.float32
    ).astype(jnp.bfloat16)
    cross_heads_grad = cross_heads_grad.reshape(clip_count, slot_len, head_count, HEAD)

    def cross_clip_back(entries):
        return attend_back(
            entries[0],
            entries[1],
            entries[2],
            entries[3],
            entries[4],
            entries[5],
            False,
            score_scale,
        )

    cquery_heads, ckey_heads, cvalue_heads = lax.map(
        cross_clip_back,
        (cross_queries, text_proj[0], text_proj[1], cross_log, cross_heads_grad, text_token_length),
    )
    query_grad_low = cquery_heads.reshape(row_total, local_width).astype(jnp.bfloat16)
    feed_low, query_grad_low = lax.optimization_barrier((feed_low, query_grad_low))
    block_out = (after_cross + lax.psum(feed_low, "tensor").astype(jnp.float32)).astype(
        jnp.bfloat16
    )
    keyval_grad_low = jnp.stack((ckey_heads, cvalue_heads)).astype(jnp.bfloat16)
    keyval_grad_low = keyval_grad_low.reshape(2, clip_count, text_count, local_width)
    cquery_grad = jnp.einsum(
        "sd,se->de", normed_cross, query_grad_low, preferred_element_type=jnp.float32
    )
    ckeyval_grad = jnp.einsum(
        "ctd,gcte->gde", text_states, keyval_grad_low, preferred_element_type=jnp.float32
    )
    text_part = jnp.einsum(
        "gcte,gde->ctd", keyval_grad_low, cross_keyval, preferred_element_type=jnp.float32
    )
    query_pieces = relay_gather(query_grad_low, "tensor")
    cross_sum = gathered_sum(query_pieces, cross_query_all, "gse,gde->gsd")
    text_grad = lax.psum(text_part.astype(jnp.bfloat16), "tensor").astype(jnp.float32)
    cross_back = norm_back(after_self, cross_gain, cross_bias, cross_sum)
    self_grad_rows = cross_grad_rows + cross_back[0]
    feed_sums, self_grad_rows = lax.optimization_barrier((feed_sums, self_grad_rows))
    self_grad_low = self_grad_rows.astype(jnp.bfloat16)
    sout_grad = jnp.einsum(
        "sk,sd->kd", self_flat, self_grad_low, preferred_element_type=jnp.float32
    )
    self_heads_grad = jnp.einsum(
        "sd,kd->sk", self_grad_low, self_out, preferred_element_type=jnp.float32
    ).astype(jnp.bfloat16)
    self_heads_grad = self_heads_grad.reshape(clip_count, slot_len, head_count, HEAD)

    def self_clip_back(entries):
        return attend_back(
            entries[0],
            entries[1],
            entries[2],
            entries[3],
            entries[4],
            entries[5],
            True,
            score_scale,
        )

    self_query_heads, self_key_heads, self_value_heads = lax.map(
        self_clip_back,
        (projected[0], projected[1], projected[2], self_log, self_heads_grad, frame_len),
    )
    projection_gradient = jnp.stack((self_query_heads, self_key_heads, self_value_heads)).astype(
        jnp.bfloat16
    )
    projection_gradient = projection_gradient.reshape(3, row_total, local_width)
    qkv_grad = jnp.einsum(
        "sd,cse->cde", normed_self, projection_gradient, preferred_element_type=jnp.float32
    )
    self_input_part = jnp.einsum(
        "cse,cde->sd", projection_gradient, self_qkv, preferred_element_type=jnp.float32
    )
    self_back = norm_back(inputs, self_gain, self_bias, relay_total(self_input_part))
    self_norm_terms = (dp_sum(self_back[1]), dp_sum(self_back[2]))
    frames_grad = self_grad_rows + self_back[0]
    gain_terms = (
        self_back[1],
        self_back[2],
        cross_back[1],
        cross_back[2],
        feed_back[1],
        feed_back[2],
    )
    late_sums = [dp_sum(term) for term in (qkv_grad, sout_grad, cquery_grad, ckeyval_grad)]
    late_sums = late_sums + stacked_psum(cout_grad, [cross_back[1], cross_back[2]], "dp")
    summed = (
        self_norm_terms[0],
        self_norm_terms[1],
        late_sums[5],
        late_sums[6],
        feed_sums[2],
        feed_sums[3],
        late_sums[0],
        late_sums[1],
        late_sums[2],
        late_sums[3],
        late_sums[4],
        feed_sums[0],
        feed_sums[1],
    )
    return (
        block_out.reshape(clip_count, slot_len, model_width),
        frames_grad.reshape(clip_count, slot_len, model_width),
        text_grad,
        summed[0],
        summed[1],
        summed[2],
        summed[3],
        summed[4],
        summed[5],
        summed[6],
        summed[7],
        summed[8],
        summed[9],
        summed[10],
        summed[11],
        summed[12],
    )


def solution(mesh):
    return jax.shard_map(
        local,
        mesh=mesh,
        in_specs=(
            P("dp", None, None),
            P("dp", None, None),
            P("dp"),
            P("dp"),
            P(),
            P(),
            P(),
            P(),
            P(),
            P(),
            P(None, None, "tensor"),
            P("tensor", None),
            P(None, "tensor"),
            P(None, None, "tensor"),
            P("tensor", None),
            P(None, "tensor"),
            P("tensor", None),
            P("dp", None, None),
        ),
        out_specs=(
            P("dp", None, None),
            P("dp", None, None),
            P("dp", None, None),
            P(),
            P(),
            P(),
            P(),
            P(),
            P(),
            P(None, None, "tensor"),
            P("tensor", None),
            P(None, "tensor"),
            P(None, None, "tensor"),
            P("tensor", None),
            P(None, "tensor"),
            P("tensor", None),
        ),
        check_vma=False,
    )
```

```python
import jax
import jax.numpy as jnp
from jax import lax
from jax.sharding import PartitionSpec as P

HEAD = 64


EPSILON = 1e-05
MASKED = -1e30


def layer_norm(inputs, norm_gain, norm_bias):
    row_mean = jnp.mean(inputs, axis=-1, keepdims=True)
    centred = inputs - row_mean
    spread = jnp.mean(centred * centred, axis=-1, keepdims=True)
    return centred * lax.rsqrt(spread + EPSILON) * norm_gain + norm_bias


def normalized(inputs):
    row_mean = jnp.mean(inputs, axis=-1, keepdims=True)
    centred = inputs - row_mean
    spread = jnp.mean(centred * centred, axis=-1, keepdims=True)
    return centred * lax.rsqrt(spread + EPSILON)


def norm_back(inputs, norm_gain, norm_bias, upstream):
    _, pullback = jax.vjp(layer_norm, inputs, norm_gain, norm_bias)
    return pullback(upstream)


def gelu_exact(inputs):
    return jax.nn.gelu(inputs, approximate=False)


def masked_scores(portion, offset, key_rows, key_limit, causal, score_scale):
    scores = (
        jnp.einsum("bhe,khe->hbk", portion, key_rows, preferred_element_type=jnp.float32)
        * score_scale
    )
    key_pos = jnp.arange(key_rows.shape[0])
    allowed = key_pos[None, :] < key_limit
    if causal:
        allowed = allowed & (key_pos[None, :] <= offset + jnp.arange(portion.shape[0])[:, None])
    return jnp.where(allowed[None], scores, MASKED)


def attend(queries, key_rows, values, key_limit, causal, score_scale):
    row_count, head_count, head_size = queries.shape
    block_len = min(512, row_count)
    portions = queries.reshape(row_count // block_len, block_len, head_count, head_size)
    offsets = jnp.arange(row_count // block_len) * block_len

    def one_block(entries):
        portion, offset = entries
        scores = masked_scores(portion, offset, key_rows, key_limit, causal, score_scale)
        row_max = jnp.max(scores, axis=-1, keepdims=True)
        unnormed = jnp.exp(scores - row_max)
        row_sum = jnp.sum(unnormed, axis=-1, keepdims=True)
        probs_low = (unnormed / row_sum).astype(jnp.bfloat16)
        result = jnp.einsum("hbk,khe->bhe", probs_low, values, preferred_element_type=jnp.float32)
        return (result.astype(jnp.bfloat16), row_max[..., 0] + jnp.log(row_sum[..., 0]))

    result, log_total = lax.map(one_block, (portions, offsets))
    return (result.reshape(row_count, head_count, head_size), log_total)


def attend_back(queries, key_rows, values, log_total, out_grad, key_limit, causal, score_scale):
    row_count, head_count, head_size = queries.shape
    block_len = min(512, row_count)
    portions = queries.reshape(row_count // block_len, block_len, head_count, head_size)
    grad_parts = out_grad.reshape(row_count // block_len, block_len, head_count, head_size)
    offsets = jnp.arange(row_count // block_len) * block_len

    def one_block(carry, entries):
        key_grad, value_grad = carry
        portion, grad_part, log_part, offset = entries
        scores = masked_scores(portion, offset, key_rows, key_limit, causal, score_scale)
        probs = jnp.exp(scores - log_part[..., None])
        probs_grad = jnp.einsum(
            "bhe,khe->hbk", grad_part, values, preferred_element_type=jnp.float32
        )
        row_dot = jnp.sum(probs * probs_grad, axis=-1, keepdims=True)
        scores_grad = (probs * (probs_grad - row_dot)).astype(jnp.bfloat16)
        value_grad = value_grad + jnp.einsum(
            "hbk,bhe->khe",
            probs.astype(jnp.bfloat16),
            grad_part,
            preferred_element_type=jnp.float32,
        )
        key_grad = (
            key_grad
            + jnp.einsum("hbk,bhe->khe", scores_grad, portion, preferred_element_type=jnp.float32)
            * score_scale
        )
        query_grad = (
            jnp.einsum("hbk,khe->bhe", scores_grad, key_rows, preferred_element_type=jnp.float32)
            * score_scale
        )
        return ((key_grad, value_grad), query_grad)

    empty = jnp.zeros(key_rows.shape, jnp.float32)
    (key_grad, value_grad), query_grad = lax.scan(
        one_block, (empty, empty), (portions, grad_parts, log_total, offsets)
    )
    return (query_grad.reshape(row_count, head_count, head_size), key_grad, value_grad)


def head_total(partial_value):
    return lax.psum(partial_value.astype(jnp.bfloat16), "tensor").astype(jnp.float32)


def relay_gather(block, axis):
    count = lax.axis_size(axis)
    me = lax.axis_index(axis)
    out = jnp.zeros((count + 1,) + block.shape, block.dtype)
    out = lax.dynamic_update_index_in_dim(out, block, me, 0)
    from_left, from_right = block, block
    for k in range(1, count):
        from_left = lax.ppermute(from_left, axis, [(i, i + 1) for i in range(k - 1, count - 1)])
        from_right = lax.ppermute(from_right, axis, [(i, i - 1) for i in range(1, count - k + 1)])
        out = lax.dynamic_update_index_in_dim(
            out, from_left, jnp.where(me - k >= 0, me - k, count), 0
        )
        out = lax.dynamic_update_index_in_dim(
            out, from_right, jnp.where(me + k < count, me + k, count), 0
        )
    return out[:count]


def relay_scatter(value, axis):
    count = lax.axis_size(axis)
    me = lax.axis_index(axis)
    shards = value.reshape((count, value.shape[0] // count) + value.shape[1:])

    def pick(index):
        return lax.dynamic_index_in_dim(shards, jnp.clip(index, 0, count - 1), 0, keepdims=False)

    to_right = to_left = None
    for k in range(1, count):
        send_right = pick(me + count - k).astype(jnp.float32)
        send_left = pick(me - (count - k)).astype(jnp.float32)
        if to_right is not None:
            send_right = send_right + to_right.astype(jnp.float32)
            send_left = send_left + to_left.astype(jnp.float32)
        to_right = lax.ppermute(
            send_right.astype(value.dtype), axis, [(i, i + 1) for i in range(min(k, count - 1))]
        )
        to_left = lax.ppermute(
            send_left.astype(value.dtype), axis, [(i, i - 1) for i in range(max(count - k, 1), count)]
        )
    total = pick(me).astype(jnp.float32)
    if to_right is not None:
        total = total + to_right.astype(jnp.float32) + to_left.astype(jnp.float32)
    return total.astype(value.dtype)


def relay_total(partial_value):
    low_value = partial_value.astype(jnp.bfloat16)
    reduced = relay_scatter(low_value, "tensor")
    return relay_gather(reduced, "tensor").reshape(low_value.shape).astype(jnp.float32)


def stacked_psum(matrix, rows, axis):
    pad = (-(matrix.shape[0] + len(rows))) % 16
    extra = jnp.stack(rows + [jnp.zeros_like(rows[0])] * pad)
    summed = lax.psum(jnp.concatenate([matrix, extra]).astype(jnp.bfloat16), axis)
    summed = summed.astype(jnp.float32)
    count = matrix.shape[0]
    return [summed[:count]] + [summed[count + i] for i in range(len(rows))]


def dp_sum(term):
    return lax.psum(term.astype(jnp.bfloat16), "dp").astype(jnp.float32)


def gathered_sum(pieces, weights, spec):
    partial_value = jnp.einsum(spec, pieces, weights, preferred_element_type=jnp.float32)
    return jnp.sum(partial_value.astype(jnp.bfloat16).astype(jnp.float32), axis=0)


def local(
    frames,
    text_states,
    frame_len,
    text_token_length,
    self_gain,
    self_bias,
    cross_gain,
    cross_bias,
    feed_gain,
    feed_bias,
    self_qkv,
    self_out,
    cross_query,
    cross_keyval,
    cross_out,
    feed_up,
    feed_down,
    cotangent,
):
    clip_count, slot_len, model_width = frames.shape
    text_count = text_states.shape[1]
    local_width = self_out.shape[0]
    head_count = local_width // HEAD
    score_scale = HEAD ** (-0.5)
    row_total = clip_count * slot_len
    inputs = frames.reshape(row_total, model_width).astype(jnp.float32)
    out_grad = cotangent.reshape(row_total, model_width)
    normed_self = layer_norm(inputs, self_gain, self_bias).astype(jnp.bfloat16)
    projected = jnp.einsum(
        "sd,cde->cse", normed_self, self_qkv, preferred_element_type=jnp.float32
    ).astype(jnp.bfloat16)
    projected = projected.reshape(3, clip_count, slot_len, head_count, HEAD)

    def self_clip(entries):
        return attend(entries[0], entries[1], entries[2], entries[3], True, score_scale)

    self_heads, self_log = lax.map(self_clip, (projected[0], projected[1], projected[2], frame_len))
    self_flat = self_heads.reshape(row_total, local_width)
    self_out_all = lax.all_gather(self_out, "tensor")
    cross_out_all = lax.all_gather(cross_out, "tensor")
    cross_query_all = lax.all_gather(cross_query, "tensor")
    self_pieces = relay_gather(self_flat, "tensor")
    after_self = inputs + gathered_sum(self_pieces, self_out_all, "gsk,gkd->gsd")
    normed_cross = layer_norm(after_self, cross_gain, cross_bias).astype(jnp.bfloat16)
    cross_queries = jnp.dot(normed_cross, cross_query, preferred_element_type=jnp.float32).astype(
        jnp.bfloat16
    )
    cross_queries = cross_queries.reshape(clip_count, slot_len, head_count, HEAD)
    text_proj = jnp.einsum(
        "ctd,gde->gcte", text_states, cross_keyval, preferred_element_type=jnp.float32
    ).astype(jnp.bfloat16)
    text_proj = text_proj.reshape(2, clip_count, text_count, head_count, HEAD)

    def cross_clip(entries):
        return attend(entries[0], entries[1], entries[2], entries[3], False, score_scale)

    cross_heads, cross_log = lax.map(
        cross_clip, (cross_queries, text_proj[0], text_proj[1], text_token_length)
    )
    cross_flat = cross_heads.reshape(row_total, local_width)
    cross_pieces = relay_gather(cross_flat, "tensor")
    after_cross = after_self + gathered_sum(cross_pieces, cross_out_all, "gsk,gkd->gsd")
    normed_feed = layer_norm(after_cross, feed_gain, feed_bias).astype(jnp.bfloat16)
    cross_query_all, normed_feed = lax.optimization_barrier((cross_query_all, normed_feed))
    upward = jnp.dot(normed_feed, feed_up, preferred_element_type=jnp.float32)
    active = gelu_exact(upward).astype(jnp.bfloat16)
    feed_part = jnp.dot(active, feed_down, preferred_element_type=jnp.float32)
    feed_low = feed_part.astype(jnp.bfloat16)
    active_grad = jnp.einsum("sd,kd->sk", out_grad, feed_down, preferred_element_type=jnp.float32)
    _, gelu_pull = jax.vjp(gelu_exact, upward)
    upward_grad = gelu_pull(active_grad)[0].astype(jnp.bfloat16)
    downward_gradient = jnp.einsum(
        "sk,sd->kd", active, out_grad, preferred_element_type=jnp.float32
    )
    up_grad = jnp.einsum("sd,sk->dk", normed_feed, upward_grad, preferred_element_type=jnp.float32)
    feed_sums = [dp_sum(up_grad), dp_sum(downward_gradient)]
    feed_input_part = jnp.einsum(
        "sk,dk->sd", upward_grad, feed_up, preferred_element_type=jnp.float32
    )
    feed_back = norm_back(after_cross, feed_gain, feed_bias, relay_total(feed_input_part))
    cross_grad_rows = out_grad.astype(jnp.float32) + feed_back[0]
    cross_grad_low = cross_grad_rows.astype(jnp.bfloat16)
    cout_grad = jnp.einsum(
        "sk,sd->kd", cross_flat, cross_grad_low, preferred_element_type=jnp.float32
    )
    cross_heads_grad = jnp.einsum(
        "sd,kd->sk", cross_grad_low, cross_out, preferred_element_type=jnp.float32
    ).astype(jnp.bfloat16)
    cross_heads_grad = cross_heads_grad.reshape(clip_count, slot_len, head_count, HEAD)

    def cross_clip_back(entries):
        return attend_back(
            entries[0],
            entries[1],
            entries[2],
            entries[3],
            entries[4],
            entries[5],
            False,
            score_scale,
        )

    cquery_heads, ckey_heads, cvalue_heads = lax.map(
        cross_clip_back,
        (cross_queries, text_proj[0], text_proj[1], cross_log, cross_heads_grad, text_token_length),
    )
    query_grad_low = cquery_heads.reshape(row_total, local_width).astype(jnp.bfloat16)
    feed_low, query_grad_low = lax.optimization_barrier((feed_low, query_grad_low))
    block_out = (after_cross + lax.psum(feed_low, "tensor").astype(jnp.float32)).astype(
        jnp.bfloat16
    )
    keyval_grad_low = jnp.stack((ckey_heads, cvalue_heads)).astype(jnp.bfloat16)
    keyval_grad_low = keyval_grad_low.reshape(2, clip_count, text_count, local_width)
    cquery_grad = jnp.einsum(
        "sd,se->de", normed_cross, query_grad_low, preferred_element_type=jnp.float32
    )
    ckeyval_grad = jnp.einsum(
        "ctd,gcte->gde", text_states, keyval_grad_low, preferred_element_type=jnp.float32
    )
    text_part = jnp.einsum(
        "gcte,gde->ctd", keyval_grad_low, cross_keyval, preferred_element_type=jnp.float32
    )
    query_pieces = relay_gather(query_grad_low, "tensor")
    cross_sum = gathered_sum(query_pieces, cross_query_all, "gse,gde->gsd")
    text_grad = lax.psum(text_part.astype(jnp.bfloat16), "tensor").astype(jnp.float32)
    cross_back = norm_back(after_self, cross_gain, cross_bias, cross_sum)
    self_grad_rows = cross_grad_rows + cross_back[0]
    feed_sums, self_grad_rows = lax.optimization_barrier((feed_sums, self_grad_rows))
    self_grad_low = self_grad_rows.astype(jnp.bfloat16)
    sout_grad = jnp.einsum(
        "sk,sd->kd", self_flat, self_grad_low, preferred_element_type=jnp.float32
    )
    self_heads_grad = jnp.einsum(
        "sd,kd->sk", self_grad_low, self_out, preferred_element_type=jnp.float32
    ).astype(jnp.bfloat16)
    self_heads_grad = self_heads_grad.reshape(clip_count, slot_len, head_count, HEAD)

    def self_clip_back(entries):
        return attend_back(
            entries[0],
            entries[1],
            entries[2],
            entries[3],
            entries[4],
            entries[5],
            True,
            score_scale,
        )

    self_query_heads, self_key_heads, self_value_heads = lax.map(
        self_clip_back,
        (projected[0], projected[1], projected[2], self_log, self_heads_grad, frame_len),
    )
    projection_gradient = jnp.stack((self_query_heads, self_key_heads, self_value_heads)).astype(
        jnp.bfloat16
    )
    projection_gradient = projection_gradient.reshape(3, row_total, local_width)
    qkv_grad = jnp.einsum(
        "sd,cse->cde", normed_self, projection_gradient, preferred_element_type=jnp.float32
    )
    self_input_part = jnp.einsum(
        "cse,cde->sd", projection_gradient, self_qkv, preferred_element_type=jnp.float32
    )
    self_back = norm_back(inputs, self_gain, self_bias, relay_total(self_input_part))
    self_norm_terms = (dp_sum(self_back[1]), dp_sum(self_back[2]))
    frames_grad = self_grad_rows + self_back[0]
    gain_terms = (
        self_back[1],
        self_back[2],
        cross_back[1],
        cross_back[2],
        feed_back[1],
        feed_back[2],
    )
    late_sums = [dp_sum(term) for term in (qkv_grad, sout_grad, cquery_grad, ckeyval_grad)]
    late_sums = late_sums + stacked_psum(
        cout_grad, [cross_back[1], cross_back[2], feed_back[1], feed_back[2]], "dp"
    )
    summed = (
        self_norm_terms[0],
        self_norm_terms[1],
        late_sums[5],
        late_sums[6],
        late_sums[7],
        late_sums[8],
        late_sums[0],
        late_sums[1],
        late_sums[2],
        late_sums[3],
        late_sums[4],
        feed_sums[0],
        feed_sums[1],
    )
    return (
        block_out.reshape(clip_count, slot_len, model_width),
        frames_grad.reshape(clip_count, slot_len, model_width),
        text_grad,
        summed[0],
        summed[1],
        summed[2],
        summed[3],
        summed[4],
        summed[5],
        summed[6],
        summed[7],
        summed[8],
        summed[9],
        summed[10],
        summed[11],
        summed[12],
    )


def solution(mesh):
    return jax.shard_map(
        local,
        mesh=mesh,
        in_specs=(
            P("dp", None, None),
            P("dp", None, None),
            P("dp"),
            P("dp"),
            P(),
            P(),
            P(),
            P(),
            P(),
            P(),
            P(None, None, "tensor"),
            P("tensor", None),
            P(None, "tensor"),
            P(None, None, "tensor"),
            P("tensor", None),
            P(None, "tensor"),
            P("tensor", None),
            P("dp", None, None),
        ),
        out_specs=(
            P("dp", None, None),
            P("dp", None, None),
            P("dp", None, None),
            P(),
            P(),
            P(),
            P(),
            P(),
            P(),
            P(None, None, "tensor"),
            P("tensor", None),
            P(None, "tensor"),
            P(None, None, "tensor"),
            P("tensor", None),
            P(None, "tensor"),
            P("tensor", None),
        ),
        check_vma=False,
    )
```

```python
import jax
import jax.numpy as jnp
from jax import lax
from jax.sharding import PartitionSpec as P

HEAD = 64


EPSILON = 1e-05
MASKED = -1e30


def layer_norm(inputs, norm_gain, norm_bias):
    row_mean = jnp.mean(inputs, axis=-1, keepdims=True)
    centred = inputs - row_mean
    spread = jnp.mean(centred * centred, axis=-1, keepdims=True)
    return centred * lax.rsqrt(spread + EPSILON) * norm_gain + norm_bias


def normalized(inputs):
    row_mean = jnp.mean(inputs, axis=-1, keepdims=True)
    centred = inputs - row_mean
    spread = jnp.mean(centred * centred, axis=-1, keepdims=True)
    return centred * lax.rsqrt(spread + EPSILON)


def norm_back(inputs, norm_gain, norm_bias, upstream):
    _, pullback = jax.vjp(layer_norm, inputs, norm_gain, norm_bias)
    return pullback(upstream)


def gelu_exact(inputs):
    return jax.nn.gelu(inputs, approximate=False)


def masked_scores(portion, offset, key_rows, key_limit, causal, score_scale):
    scores = (
        jnp.einsum("bhe,khe->hbk", portion, key_rows, preferred_element_type=jnp.float32)
        * score_scale
    )
    key_pos = jnp.arange(key_rows.shape[0])
    allowed = key_pos[None, :] < key_limit
    if causal:
        allowed = allowed & (key_pos[None, :] <= offset + jnp.arange(portion.shape[0])[:, None])
    return jnp.where(allowed[None], scores, MASKED)


def attend(queries, key_rows, values, key_limit, causal, score_scale):
    row_count, head_count, head_size = queries.shape
    block_len = min(512, row_count)
    portions = queries.reshape(row_count // block_len, block_len, head_count, head_size)
    offsets = jnp.arange(row_count // block_len) * block_len

    def one_block(entries):
        portion, offset = entries
        scores = masked_scores(portion, offset, key_rows, key_limit, causal, score_scale)
        row_max = jnp.max(scores, axis=-1, keepdims=True)
        unnormed = jnp.exp(scores - row_max)
        row_sum = jnp.sum(unnormed, axis=-1, keepdims=True)
        probs_low = (unnormed / row_sum).astype(jnp.bfloat16)
        result = jnp.einsum("hbk,khe->bhe", probs_low, values, preferred_element_type=jnp.float32)
        return (result.astype(jnp.bfloat16), row_max[..., 0] + jnp.log(row_sum[..., 0]))

    result, log_total = lax.map(one_block, (portions, offsets))
    return (result.reshape(row_count, head_count, head_size), log_total)


def attend_back(queries, key_rows, values, log_total, out_grad, key_limit, causal, score_scale):
    row_count, head_count, head_size = queries.shape
    block_len = min(512, row_count)
    portions = queries.reshape(row_count // block_len, block_len, head_count, head_size)
    grad_parts = out_grad.reshape(row_count // block_len, block_len, head_count, head_size)
    offsets = jnp.arange(row_count // block_len) * block_len

    def one_block(carry, entries):
        key_grad, value_grad = carry
        portion, grad_part, log_part, offset = entries
        scores = masked_scores(portion, offset, key_rows, key_limit, causal, score_scale)
        probs = jnp.exp(scores - log_part[..., None])
        probs_grad = jnp.einsum(
            "bhe,khe->hbk", grad_part, values, preferred_element_type=jnp.float32
        )
        row_dot = jnp.sum(probs * probs_grad, axis=-1, keepdims=True)
        scores_grad = (probs * (probs_grad - row_dot)).astype(jnp.bfloat16)
        value_grad = value_grad + jnp.einsum(
            "hbk,bhe->khe",
            probs.astype(jnp.bfloat16),
            grad_part,
            preferred_element_type=jnp.float32,
        )
        key_grad = (
            key_grad
            + jnp.einsum("hbk,bhe->khe", scores_grad, portion, preferred_element_type=jnp.float32)
            * score_scale
        )
        query_grad = (
            jnp.einsum("hbk,khe->bhe", scores_grad, key_rows, preferred_element_type=jnp.float32)
            * score_scale
        )
        return ((key_grad, value_grad), query_grad)

    empty = jnp.zeros(key_rows.shape, jnp.float32)
    (key_grad, value_grad), query_grad = lax.scan(
        one_block, (empty, empty), (portions, grad_parts, log_total, offsets)
    )
    return (query_grad.reshape(row_count, head_count, head_size), key_grad, value_grad)


def head_total(partial_value):
    return lax.psum(partial_value.astype(jnp.bfloat16), "tensor").astype(jnp.float32)


def relay_pieces(block, axis):
    count = lax.axis_size(axis)
    me = lax.axis_index(axis)
    pieces = [(block, me)]
    from_left, from_right = block, block
    for k in range(1, count):
        from_left = lax.ppermute(from_left, axis, [(i, i + 1) for i in range(k - 1, count - 1)])
        from_right = lax.ppermute(from_right, axis, [(i, i - 1) for i in range(1, count - k + 1)])
        pieces.append((from_left, me - k))
        pieces.append((from_right, me + k))
    return pieces


def relay_scatter(value, axis):
    count = lax.axis_size(axis)
    me = lax.axis_index(axis)
    shards = value.reshape((count, value.shape[0] // count) + value.shape[1:])

    def pick(index):
        return lax.dynamic_index_in_dim(shards, jnp.clip(index, 0, count - 1), 0, keepdims=False)

    to_right = to_left = None
    for k in range(1, count):
        send_right = pick(me + count - k).astype(jnp.float32)
        send_left = pick(me - (count - k)).astype(jnp.float32)
        if to_right is not None:
            send_right = send_right + to_right.astype(jnp.float32)
            send_left = send_left + to_left.astype(jnp.float32)
        to_right = lax.ppermute(
            send_right.astype(value.dtype), axis, [(i, i + 1) for i in range(min(k, count - 1))]
        )
        to_left = lax.ppermute(
            send_left.astype(value.dtype), axis, [(i, i - 1) for i in range(max(count - k, 1), count)]
        )
    total = pick(me).astype(jnp.float32)
    if to_right is not None:
        total = total + to_right.astype(jnp.float32) + to_left.astype(jnp.float32)
    return total.astype(value.dtype)


def relay_total(partial_value):
    low_value = partial_value.astype(jnp.bfloat16)
    reduced = relay_scatter(low_value, "tensor")
    pieces = relay_pieces(reduced, "tensor")
    shards = []
    for owner in range(len(pieces) // 2 + 1):
        shard = jnp.zeros_like(reduced)
        for piece, source in pieces:
            shard = jnp.where(source == owner, piece, shard)
        shards.append(shard)
    return jnp.concatenate(shards).astype(jnp.float32)


def stacked_psum(matrix, rows, axis):
    pad = (-(matrix.shape[0] + len(rows))) % 16
    extra = jnp.stack(rows + [jnp.zeros_like(rows[0])] * pad)
    summed = lax.psum(jnp.concatenate([matrix, extra]).astype(jnp.bfloat16), axis)
    summed = summed.astype(jnp.float32)
    count = matrix.shape[0]
    return [summed[:count]] + [summed[count + i] for i in range(len(rows))]


def dp_sum(term):
    return lax.psum(term.astype(jnp.bfloat16), "dp").astype(jnp.float32)


def gathered_sum(block, weights, spec):
    count = weights.shape[0]
    total = None
    for piece, source in relay_pieces(block, "tensor"):
        weight = lax.dynamic_index_in_dim(weights, jnp.clip(source, 0, count - 1), 0, keepdims=False)
        partial_value = jnp.einsum(spec, piece, weight, preferred_element_type=jnp.float32)
        partial_value = partial_value.astype(jnp.bfloat16).astype(jnp.float32)
        total = partial_value if total is None else total + partial_value
        total = lax.optimization_barrier(total)
    return total


def local(
    frames,
    text_states,
    frame_len,
    text_token_length,
    self_gain,
    self_bias,
    cross_gain,
    cross_bias,
    feed_gain,
    feed_bias,
    self_qkv,
    self_out,
    cross_query,
    cross_keyval,
    cross_out,
    feed_up,
    feed_down,
    cotangent,
):
    clip_count, slot_len, model_width = frames.shape
    text_count = text_states.shape[1]
    local_width = self_out.shape[0]
    head_count = local_width // HEAD
    score_scale = HEAD ** (-0.5)
    row_total = clip_count * slot_len
    inputs = frames.reshape(row_total, model_width).astype(jnp.float32)
    out_grad = cotangent.reshape(row_total, model_width)
    normed_self = layer_norm(inputs, self_gain, self_bias).astype(jnp.bfloat16)
    projected = jnp.einsum(
        "sd,cde->cse", normed_self, self_qkv, preferred_element_type=jnp.float32
    ).astype(jnp.bfloat16)
    projected = projected.reshape(3, clip_count, slot_len, head_count, HEAD)

    def self_clip(entries):
        return attend(entries[0], entries[1], entries[2], entries[3], True, score_scale)

    self_heads, self_log = lax.map(self_clip, (projected[0], projected[1], projected[2], frame_len))
    self_flat = self_heads.reshape(row_total, local_width)
    self_out_all = lax.all_gather(self_out, "tensor")
    cross_out_all = lax.all_gather(cross_out, "tensor")
    cross_query_all = lax.all_gather(cross_query, "tensor")
    after_self = inputs + gathered_sum(self_flat, self_out_all, "sk,kd->sd")
    normed_cross = layer_norm(after_self, cross_gain, cross_bias).astype(jnp.bfloat16)
    cross_queries = jnp.dot(normed_cross, cross_query, preferred_element_type=jnp.float32).astype(
        jnp.bfloat16
    )
    cross_queries = cross_queries.reshape(clip_count, slot_len, head_count, HEAD)
    text_proj = jnp.einsum(
        "ctd,gde->gcte", text_states, cross_keyval, preferred_element_type=jnp.float32
    ).astype(jnp.bfloat16)
    text_proj = text_proj.reshape(2, clip_count, text_count, head_count, HEAD)

    def cross_clip(entries):
        return attend(entries[0], entries[1], entries[2], entries[3], False, score_scale)

    cross_heads, cross_log = lax.map(
        cross_clip, (cross_queries, text_proj[0], text_proj[1], text_token_length)
    )
    cross_flat = cross_heads.reshape(row_total, local_width)
    after_cross = after_self + gathered_sum(cross_flat, cross_out_all, "sk,kd->sd")
    normed_feed = layer_norm(after_cross, feed_gain, feed_bias).astype(jnp.bfloat16)
    upward = jnp.dot(normed_feed, feed_up, preferred_element_type=jnp.float32)
    active = gelu_exact(upward).astype(jnp.bfloat16)
    feed_part = jnp.dot(active, feed_down, preferred_element_type=jnp.float32)
    feed_low = feed_part.astype(jnp.bfloat16)
    active_grad = jnp.einsum("sd,kd->sk", out_grad, feed_down, preferred_element_type=jnp.float32)
    _, gelu_pull = jax.vjp(gelu_exact, upward)
    upward_grad = gelu_pull(active_grad)[0].astype(jnp.bfloat16)
    downward_gradient = jnp.einsum(
        "sk,sd->kd", active, out_grad, preferred_element_type=jnp.float32
    )
    up_grad = jnp.einsum("sd,sk->dk", normed_feed, upward_grad, preferred_element_type=jnp.float32)
    feed_input_part = jnp.einsum(
        "sk,dk->sd", upward_grad, feed_up, preferred_element_type=jnp.float32
    )
    feed_back = norm_back(after_cross, feed_gain, feed_bias, relay_total(feed_input_part))
    feed_sums = [dp_sum(up_grad), dp_sum(downward_gradient)]
    cross_grad_rows = out_grad.astype(jnp.float32) + feed_back[0]
    cross_grad_low = cross_grad_rows.astype(jnp.bfloat16)
    cout_grad = jnp.einsum(
        "sk,sd->kd", cross_flat, cross_grad_low, preferred_element_type=jnp.float32
    )
    cross_heads_grad = jnp.einsum(
        "sd,kd->sk", cross_grad_low, cross_out, preferred_element_type=jnp.float32
    ).astype(jnp.bfloat16)
    cross_heads_grad = cross_heads_grad.reshape(clip_count, slot_len, head_count, HEAD)

    def cross_clip_back(entries):
        return attend_back(
            entries[0],
            entries[1],
            entries[2],
            entries[3],
            entries[4],
            entries[5],
            False,
            score_scale,
        )

    cquery_heads, ckey_heads, cvalue_heads = lax.map(
        cross_clip_back,
        (cross_queries, text_proj[0], text_proj[1], cross_log, cross_heads_grad, text_token_length),
    )
    query_grad_low = cquery_heads.reshape(row_total, local_width).astype(jnp.bfloat16)
    feed_low, query_grad_low = lax.optimization_barrier((feed_low, query_grad_low))
    block_out = (after_cross + lax.psum(feed_low, "tensor").astype(jnp.float32)).astype(
        jnp.bfloat16
    )
    keyval_grad_low = jnp.stack((ckey_heads, cvalue_heads)).astype(jnp.bfloat16)
    keyval_grad_low = keyval_grad_low.reshape(2, clip_count, text_count, local_width)
    cquery_grad = jnp.einsum(
        "sd,se->de", normed_cross, query_grad_low, preferred_element_type=jnp.float32
    )
    ckeyval_grad = jnp.einsum(
        "ctd,gcte->gde", text_states, keyval_grad_low, preferred_element_type=jnp.float32
    )
    text_part = jnp.einsum(
        "gcte,gde->ctd", keyval_grad_low, cross_keyval, preferred_element_type=jnp.float32
    )
    cross_sum = gathered_sum(query_grad_low, cross_query_all, "se,de->sd")
    text_grad = lax.psum(text_part.astype(jnp.bfloat16), "tensor").astype(jnp.float32)
    cross_back = norm_back(after_self, cross_gain, cross_bias, cross_sum)
    self_grad_rows = cross_grad_rows + cross_back[0]
    feed_sums, self_grad_rows = lax.optimization_barrier((feed_sums, self_grad_rows))
    self_grad_low = self_grad_rows.astype(jnp.bfloat16)
    sout_grad = jnp.einsum(
        "sk,sd->kd", self_flat, self_grad_low, preferred_element_type=jnp.float32
    )
    self_heads_grad = jnp.einsum(
        "sd,kd->sk", self_grad_low, self_out, preferred_element_type=jnp.float32
    ).astype(jnp.bfloat16)
    self_heads_grad = self_heads_grad.reshape(clip_count, slot_len, head_count, HEAD)

    def self_clip_back(entries):
        return attend_back(
            entries[0],
            entries[1],
            entries[2],
            entries[3],
            entries[4],
            entries[5],
            True,
            score_scale,
        )

    self_query_heads, self_key_heads, self_value_heads = lax.map(
        self_clip_back,
        (projected[0], projected[1], projected[2], self_log, self_heads_grad, frame_len),
    )
    projection_gradient = jnp.stack((self_query_heads, self_key_heads, self_value_heads)).astype(
        jnp.bfloat16
    )
    projection_gradient = projection_gradient.reshape(3, row_total, local_width)
    qkv_grad = jnp.einsum(
        "sd,cse->cde", normed_self, projection_gradient, preferred_element_type=jnp.float32
    )
    self_input_part = jnp.einsum(
        "cse,cde->sd", projection_gradient, self_qkv, preferred_element_type=jnp.float32
    )
    self_back = norm_back(inputs, self_gain, self_bias, relay_total(self_input_part))
    self_norm_terms = (dp_sum(self_back[1]), dp_sum(self_back[2]))
    frames_grad = self_grad_rows + self_back[0]
    gain_terms = (
        self_back[1],
        self_back[2],
        cross_back[1],
        cross_back[2],
        feed_back[1],
        feed_back[2],
    )
    late_sums = [dp_sum(term) for term in (qkv_grad, sout_grad, cquery_grad, ckeyval_grad)]
    late_sums = late_sums + stacked_psum(
        cout_grad, [cross_back[1], cross_back[2], feed_back[1], feed_back[2]], "dp"
    )
    summed = (
        self_norm_terms[0],
        self_norm_terms[1],
        late_sums[5],
        late_sums[6],
        late_sums[7],
        late_sums[8],
        late_sums[0],
        late_sums[1],
        late_sums[2],
        late_sums[3],
        late_sums[4],
        feed_sums[0],
        feed_sums[1],
    )
    return (
        block_out.reshape(clip_count, slot_len, model_width),
        frames_grad.reshape(clip_count, slot_len, model_width),
        text_grad,
        summed[0],
        summed[1],
        summed[2],
        summed[3],
        summed[4],
        summed[5],
        summed[6],
        summed[7],
        summed[8],
        summed[9],
        summed[10],
        summed[11],
        summed[12],
    )


def solution(mesh):
    return jax.shard_map(
        local,
        mesh=mesh,
        in_specs=(
            P("dp", None, None),
            P("dp", None, None),
            P("dp"),
            P("dp"),
            P(),
            P(),
            P(),
            P(),
            P(),
            P(),
            P(None, None, "tensor"),
            P("tensor", None),
            P(None, "tensor"),
            P(None, None, "tensor"),
            P("tensor", None),
            P(None, "tensor"),
            P("tensor", None),
            P("dp", None, None),
        ),
        out_specs=(
            P("dp", None, None),
            P("dp", None, None),
            P("dp", None, None),
            P(),
            P(),
            P(),
            P(),
            P(),
            P(),
            P(None, None, "tensor"),
            P("tensor", None),
            P(None, "tensor"),
            P(None, None, "tensor"),
            P("tensor", None),
            P(None, "tensor"),
            P("tensor", None),
        ),
        check_vma=False,
    )
```

```python
import jax
import jax.numpy as jnp
from jax import lax
from jax.sharding import PartitionSpec as P

HEAD = 64


EPSILON = 1e-05
MASKED = -1e30


def layer_norm(inputs, norm_gain, norm_bias):
    row_mean = jnp.mean(inputs, axis=-1, keepdims=True)
    centred = inputs - row_mean
    spread = jnp.mean(centred * centred, axis=-1, keepdims=True)
    return centred * lax.rsqrt(spread + EPSILON) * norm_gain + norm_bias


def normalized(inputs):
    row_mean = jnp.mean(inputs, axis=-1, keepdims=True)
    centred = inputs - row_mean
    spread = jnp.mean(centred * centred, axis=-1, keepdims=True)
    return centred * lax.rsqrt(spread + EPSILON)


def norm_back(inputs, norm_gain, norm_bias, upstream):
    _, pullback = jax.vjp(layer_norm, inputs, norm_gain, norm_bias)
    return pullback(upstream)


def gelu_exact(inputs):
    return jax.nn.gelu(inputs, approximate=False)


def masked_scores(portion, offset, key_rows, key_limit, causal, score_scale):
    scores = (
        jnp.einsum("bhe,khe->hbk", portion, key_rows, preferred_element_type=jnp.float32)
        * score_scale
    )
    key_pos = jnp.arange(key_rows.shape[0])
    allowed = key_pos[None, :] < key_limit
    if causal:
        allowed = allowed & (key_pos[None, :] <= offset + jnp.arange(portion.shape[0])[:, None])
    return jnp.where(allowed[None], scores, MASKED)


def attend(queries, key_rows, values, key_limit, causal, score_scale):
    row_count, head_count, head_size = queries.shape
    block_len = min(512, row_count)
    portions = queries.reshape(row_count // block_len, block_len, head_count, head_size)
    offsets = jnp.arange(row_count // block_len) * block_len

    def one_block(entries):
        portion, offset = entries
        scores = masked_scores(portion, offset, key_rows, key_limit, causal, score_scale)
        row_max = jnp.max(scores, axis=-1, keepdims=True)
        unnormed = jnp.exp(scores - row_max)
        row_sum = jnp.sum(unnormed, axis=-1, keepdims=True)
        probs_low = (unnormed / row_sum).astype(jnp.bfloat16)
        result = jnp.einsum("hbk,khe->bhe", probs_low, values, preferred_element_type=jnp.float32)
        return (result.astype(jnp.bfloat16), row_max[..., 0] + jnp.log(row_sum[..., 0]))

    result, log_total = lax.map(one_block, (portions, offsets))
    return (result.reshape(row_count, head_count, head_size), log_total)


def attend_back(queries, key_rows, values, log_total, out_grad, key_limit, causal, score_scale):
    row_count, head_count, head_size = queries.shape
    block_len = min(512, row_count)
    portions = queries.reshape(row_count // block_len, block_len, head_count, head_size)
    grad_parts = out_grad.reshape(row_count // block_len, block_len, head_count, head_size)
    offsets = jnp.arange(row_count // block_len) * block_len

    def one_block(carry, entries):
        key_grad, value_grad = carry
        portion, grad_part, log_part, offset = entries
        scores = masked_scores(portion, offset, key_rows, key_limit, causal, score_scale)
        probs = jnp.exp(scores - log_part[..., None])
        probs_grad = jnp.einsum(
            "bhe,khe->hbk", grad_part, values, preferred_element_type=jnp.float32
        )
        row_dot = jnp.sum(probs * probs_grad, axis=-1, keepdims=True)
        scores_grad = (probs * (probs_grad - row_dot)).astype(jnp.bfloat16)
        value_grad = value_grad + jnp.einsum(
            "hbk,bhe->khe",
            probs.astype(jnp.bfloat16),
            grad_part,
            preferred_element_type=jnp.float32,
        )
        key_grad = (
            key_grad
            + jnp.einsum("hbk,bhe->khe", scores_grad, portion, preferred_element_type=jnp.float32)
            * score_scale
        )
        query_grad = (
            jnp.einsum("hbk,khe->bhe", scores_grad, key_rows, preferred_element_type=jnp.float32)
            * score_scale
        )
        return ((key_grad, value_grad), query_grad)

    empty = jnp.zeros(key_rows.shape, jnp.float32)
    (key_grad, value_grad), query_grad = lax.scan(
        one_block, (empty, empty), (portions, grad_parts, log_total, offsets)
    )
    return (query_grad.reshape(row_count, head_count, head_size), key_grad, value_grad)


def head_total(partial_value):
    return lax.psum(partial_value.astype(jnp.bfloat16), "tensor").astype(jnp.float32)


def relay_pieces(block, axis):
    count = lax.axis_size(axis)
    me = lax.axis_index(axis)
    pieces = [(block, me)]
    from_left, from_right = block, block
    for k in range(1, count):
        from_left = lax.ppermute(from_left, axis, [(i, i + 1) for i in range(k - 1, count - 1)])
        from_right = lax.ppermute(from_right, axis, [(i, i - 1) for i in range(1, count - k + 1)])
        pieces.append((from_left, me - k))
        pieces.append((from_right, me + k))
    return pieces


def relay_scatter(value, axis):
    count = lax.axis_size(axis)
    me = lax.axis_index(axis)
    shards = value.reshape((count, value.shape[0] // count) + value.shape[1:])

    def pick(index):
        return lax.dynamic_index_in_dim(shards, jnp.clip(index, 0, count - 1), 0, keepdims=False)

    to_right = to_left = None
    for k in range(1, count):
        send_right = pick(me + count - k).astype(jnp.float32)
        send_left = pick(me - (count - k)).astype(jnp.float32)
        if to_right is not None:
            send_right = send_right + to_right.astype(jnp.float32)
            send_left = send_left + to_left.astype(jnp.float32)
        to_right = lax.ppermute(
            send_right.astype(value.dtype), axis, [(i, i + 1) for i in range(min(k, count - 1))]
        )
        to_left = lax.ppermute(
            send_left.astype(value.dtype), axis, [(i, i - 1) for i in range(max(count - k, 1), count)]
        )
    total = pick(me).astype(jnp.float32)
    if to_right is not None:
        total = total + to_right.astype(jnp.float32) + to_left.astype(jnp.float32)
    return total.astype(value.dtype)


def relay_total(partial_value):
    low_value = partial_value.astype(jnp.bfloat16)
    reduced = relay_scatter(low_value, "tensor")
    pieces = relay_pieces(reduced, "tensor")
    shards = []
    for owner in range(len(pieces) // 2 + 1):
        shard = jnp.zeros_like(reduced)
        for piece, source in pieces:
            shard = jnp.where(source == owner, piece, shard)
        shards.append(shard)
    return jnp.concatenate(shards).astype(jnp.float32)


def stacked_psum(matrix, rows, axis):
    pad = (-(matrix.shape[0] + len(rows))) % 16
    extra = jnp.stack(rows + [jnp.zeros_like(rows[0])] * pad)
    summed = lax.psum(jnp.concatenate([matrix, extra]).astype(jnp.bfloat16), axis)
    summed = summed.astype(jnp.float32)
    count = matrix.shape[0]
    return [summed[:count]] + [summed[count + i] for i in range(len(rows))]


def butterfly_sum(terms, axis):
    count = lax.axis_size(axis)
    me = lax.axis_index(axis)
    pieces = [term.astype(jnp.bfloat16).reshape(-1, 128) for term in terms]
    rows = sum(piece.shape[0] for piece in pieces)
    pad = (-rows) % (16 * count)
    if pad:
        pieces.append(jnp.zeros((pad, 128), jnp.bfloat16))
    current = jnp.concatenate(pieces)
    steps = count.bit_length() - 1
    for level in range(steps):
        pairs = [(i, i ^ (1 << level)) for i in range(count)]
        half = current.shape[0] // 2
        bit = (me // (1 << level)) % 2
        keep = lax.dynamic_slice_in_dim(current, bit * half, half)
        sent = lax.dynamic_slice_in_dim(current, (1 - bit) * half, half)
        arrived = lax.ppermute(sent, axis, pairs)
        current = (keep.astype(jnp.float32) + arrived.astype(jnp.float32)).astype(jnp.bfloat16)
    for level in reversed(range(steps)):
        pairs = [(i, i ^ (1 << level)) for i in range(count)]
        bit = (me // (1 << level)) % 2
        arrived = lax.ppermute(current, axis, pairs)
        current = jnp.where(
            bit == 0,
            jnp.concatenate([current, arrived]),
            jnp.concatenate([arrived, current]),
        )
    out, start = [], 0
    for term in terms:
        size = term.size // 128
        out.append(current[start : start + size].astype(jnp.float32).reshape(term.shape))
        start += size
    return out


def dp_sum(term):
    return lax.psum(term.astype(jnp.bfloat16), "dp").astype(jnp.float32)


def gathered_sum(block, weights, spec):
    count = weights.shape[0]
    total = None
    for piece, source in relay_pieces(block, "tensor"):
        weight = lax.dynamic_index_in_dim(weights, jnp.clip(source, 0, count - 1), 0, keepdims=False)
        partial_value = jnp.einsum(spec, piece, weight, preferred_element_type=jnp.float32)
        partial_value = partial_value.astype(jnp.bfloat16).astype(jnp.float32)
        total = partial_value if total is None else total + partial_value
        total = lax.optimization_barrier(total)
    return total


def local(
    frames,
    text_states,
    frame_len,
    text_token_length,
    self_gain,
    self_bias,
    cross_gain,
    cross_bias,
    feed_gain,
    feed_bias,
    self_qkv,
    self_out,
    cross_query,
    cross_keyval,
    cross_out,
    feed_up,
    feed_down,
    cotangent,
):
    clip_count, slot_len, model_width = frames.shape
    text_count = text_states.shape[1]
    local_width = self_out.shape[0]
    head_count = local_width // HEAD
    score_scale = HEAD ** (-0.5)
    row_total = clip_count * slot_len
    inputs = frames.reshape(row_total, model_width).astype(jnp.float32)
    out_grad = cotangent.reshape(row_total, model_width)
    normed_self = layer_norm(inputs, self_gain, self_bias).astype(jnp.bfloat16)
    projected = jnp.einsum(
        "sd,cde->cse", normed_self, self_qkv, preferred_element_type=jnp.float32
    ).astype(jnp.bfloat16)
    projected = projected.reshape(3, clip_count, slot_len, head_count, HEAD)

    def self_clip(entries):
        return attend(entries[0], entries[1], entries[2], entries[3], True, score_scale)

    self_heads, self_log = lax.map(self_clip, (projected[0], projected[1], projected[2], frame_len))
    self_flat = self_heads.reshape(row_total, local_width)
    self_out_all = lax.all_gather(self_out, "tensor")
    cross_out_all = lax.all_gather(cross_out, "tensor")
    cross_query_all = lax.all_gather(cross_query, "tensor")
    after_self = inputs + gathered_sum(self_flat, self_out_all, "sk,kd->sd")
    normed_cross = layer_norm(after_self, cross_gain, cross_bias).astype(jnp.bfloat16)
    cross_queries = jnp.dot(normed_cross, cross_query, preferred_element_type=jnp.float32).astype(
        jnp.bfloat16
    )
    cross_queries = cross_queries.reshape(clip_count, slot_len, head_count, HEAD)
    text_proj = jnp.einsum(
        "ctd,gde->gcte", text_states, cross_keyval, preferred_element_type=jnp.float32
    ).astype(jnp.bfloat16)
    text_proj = text_proj.reshape(2, clip_count, text_count, head_count, HEAD)

    def cross_clip(entries):
        return attend(entries[0], entries[1], entries[2], entries[3], False, score_scale)

    cross_heads, cross_log = lax.map(
        cross_clip, (cross_queries, text_proj[0], text_proj[1], text_token_length)
    )
    cross_flat = cross_heads.reshape(row_total, local_width)
    after_cross = after_self + gathered_sum(cross_flat, cross_out_all, "sk,kd->sd")
    normed_feed = layer_norm(after_cross, feed_gain, feed_bias).astype(jnp.bfloat16)
    upward = jnp.dot(normed_feed, feed_up, preferred_element_type=jnp.float32)
    active = gelu_exact(upward).astype(jnp.bfloat16)
    feed_part = jnp.dot(active, feed_down, preferred_element_type=jnp.float32)
    feed_low = feed_part.astype(jnp.bfloat16)
    active_grad = jnp.einsum("sd,kd->sk", out_grad, feed_down, preferred_element_type=jnp.float32)
    _, gelu_pull = jax.vjp(gelu_exact, upward)
    upward_grad = gelu_pull(active_grad)[0].astype(jnp.bfloat16)
    downward_gradient = jnp.einsum(
        "sk,sd->kd", active, out_grad, preferred_element_type=jnp.float32
    )
    up_grad = jnp.einsum("sd,sk->dk", normed_feed, upward_grad, preferred_element_type=jnp.float32)
    feed_input_part = jnp.einsum(
        "sk,dk->sd", upward_grad, feed_up, preferred_element_type=jnp.float32
    )
    feed_back = norm_back(after_cross, feed_gain, feed_bias, relay_total(feed_input_part))
    feed_sums = [dp_sum(up_grad), dp_sum(downward_gradient)]
    cross_grad_rows = out_grad.astype(jnp.float32) + feed_back[0]
    cross_grad_low = cross_grad_rows.astype(jnp.bfloat16)
    cout_grad = jnp.einsum(
        "sk,sd->kd", cross_flat, cross_grad_low, preferred_element_type=jnp.float32
    )
    cross_heads_grad = jnp.einsum(
        "sd,kd->sk", cross_grad_low, cross_out, preferred_element_type=jnp.float32
    ).astype(jnp.bfloat16)
    cross_heads_grad = cross_heads_grad.reshape(clip_count, slot_len, head_count, HEAD)

    def cross_clip_back(entries):
        return attend_back(
            entries[0],
            entries[1],
            entries[2],
            entries[3],
            entries[4],
            entries[5],
            False,
            score_scale,
        )

    cquery_heads, ckey_heads, cvalue_heads = lax.map(
        cross_clip_back,
        (cross_queries, text_proj[0], text_proj[1], cross_log, cross_heads_grad, text_token_length),
    )
    query_grad_low = cquery_heads.reshape(row_total, local_width).astype(jnp.bfloat16)
    feed_low, query_grad_low = lax.optimization_barrier((feed_low, query_grad_low))
    block_out = (after_cross + lax.psum(feed_low, "tensor").astype(jnp.float32)).astype(
        jnp.bfloat16
    )
    keyval_grad_low = jnp.stack((ckey_heads, cvalue_heads)).astype(jnp.bfloat16)
    keyval_grad_low = keyval_grad_low.reshape(2, clip_count, text_count, local_width)
    cquery_grad = jnp.einsum(
        "sd,se->de", normed_cross, query_grad_low, preferred_element_type=jnp.float32
    )
    ckeyval_grad = jnp.einsum(
        "ctd,gcte->gde", text_states, keyval_grad_low, preferred_element_type=jnp.float32
    )
    text_part = jnp.einsum(
        "gcte,gde->ctd", keyval_grad_low, cross_keyval, preferred_element_type=jnp.float32
    )
    cross_sum = gathered_sum(query_grad_low, cross_query_all, "se,de->sd")
    text_grad = lax.psum(text_part.astype(jnp.bfloat16), "tensor").astype(jnp.float32)
    cross_back = norm_back(after_self, cross_gain, cross_bias, cross_sum)
    self_grad_rows = cross_grad_rows + cross_back[0]
    feed_sums, self_grad_rows = lax.optimization_barrier((feed_sums, self_grad_rows))
    self_grad_low = self_grad_rows.astype(jnp.bfloat16)
    sout_grad = jnp.einsum(
        "sk,sd->kd", self_flat, self_grad_low, preferred_element_type=jnp.float32
    )
    self_heads_grad = jnp.einsum(
        "sd,kd->sk", self_grad_low, self_out, preferred_element_type=jnp.float32
    ).astype(jnp.bfloat16)
    self_heads_grad = self_heads_grad.reshape(clip_count, slot_len, head_count, HEAD)

    def self_clip_back(entries):
        return attend_back(
            entries[0],
            entries[1],
            entries[2],
            entries[3],
            entries[4],
            entries[5],
            True,
            score_scale,
        )

    self_query_heads, self_key_heads, self_value_heads = lax.map(
        self_clip_back,
        (projected[0], projected[1], projected[2], self_log, self_heads_grad, frame_len),
    )
    projection_gradient = jnp.stack((self_query_heads, self_key_heads, self_value_heads)).astype(
        jnp.bfloat16
    )
    projection_gradient = projection_gradient.reshape(3, row_total, local_width)
    qkv_grad = jnp.einsum(
        "sd,cse->cde", normed_self, projection_gradient, preferred_element_type=jnp.float32
    )
    self_input_part = jnp.einsum(
        "cse,cde->sd", projection_gradient, self_qkv, preferred_element_type=jnp.float32
    )
    self_back = norm_back(inputs, self_gain, self_bias, relay_total(self_input_part))
    self_norm_terms = (dp_sum(self_back[1]), dp_sum(self_back[2]))
    frames_grad = self_grad_rows + self_back[0]
    gain_terms = (
        self_back[1],
        self_back[2],
        cross_back[1],
        cross_back[2],
        feed_back[1],
        feed_back[2],
    )
    late_sums = butterfly_sum(
        (
            qkv_grad,
            sout_grad,
            cquery_grad,
            ckeyval_grad,
            cout_grad,
            cross_back[1],
            cross_back[2],
            feed_back[1],
            feed_back[2],
        ),
        "dp",
    )
    summed = (
        self_norm_terms[0],
        self_norm_terms[1],
        late_sums[5],
        late_sums[6],
        late_sums[7],
        late_sums[8],
        late_sums[0],
        late_sums[1],
        late_sums[2],
        late_sums[3],
        late_sums[4],
        feed_sums[0],
        feed_sums[1],
    )
    return (
        block_out.reshape(clip_count, slot_len, model_width),
        frames_grad.reshape(clip_count, slot_len, model_width),
        text_grad,
        summed[0],
        summed[1],
        summed[2],
        summed[3],
        summed[4],
        summed[5],
        summed[6],
        summed[7],
        summed[8],
        summed[9],
        summed[10],
        summed[11],
        summed[12],
    )


def solution(mesh):
    return jax.shard_map(
        local,
        mesh=mesh,
        in_specs=(
            P("dp", None, None),
            P("dp", None, None),
            P("dp"),
            P("dp"),
            P(),
            P(),
            P(),
            P(),
            P(),
            P(),
            P(None, None, "tensor"),
            P("tensor", None),
            P(None, "tensor"),
            P(None, None, "tensor"),
            P("tensor", None),
            P(None, "tensor"),
            P("tensor", None),
            P("dp", None, None),
        ),
        out_specs=(
            P("dp", None, None),
            P("dp", None, None),
            P("dp", None, None),
            P(),
            P(),
            P(),
            P(),
            P(),
            P(),
            P(None, None, "tensor"),
            P("tensor", None),
            P(None, "tensor"),
            P(None, None, "tensor"),
            P("tensor", None),
            P(None, "tensor"),
            P("tensor", None),
        ),
        check_vma=False,
    )
```

```python
import jax
import jax.numpy as jnp
from jax import lax
from jax.sharding import PartitionSpec as P

HEAD = 64


EPSILON = 1e-05
MASKED = -1e30


def layer_norm(inputs, norm_gain, norm_bias):
    row_mean = jnp.mean(inputs, axis=-1, keepdims=True)
    centred = inputs - row_mean
    spread = jnp.mean(centred * centred, axis=-1, keepdims=True)
    return centred * lax.rsqrt(spread + EPSILON) * norm_gain + norm_bias


def normalized(inputs):
    row_mean = jnp.mean(inputs, axis=-1, keepdims=True)
    centred = inputs - row_mean
    spread = jnp.mean(centred * centred, axis=-1, keepdims=True)
    return centred * lax.rsqrt(spread + EPSILON)


def norm_back(inputs, norm_gain, norm_bias, upstream):
    _, pullback = jax.vjp(layer_norm, inputs, norm_gain, norm_bias)
    return pullback(upstream)


def gelu_exact(inputs):
    return jax.nn.gelu(inputs, approximate=False)


def masked_scores(portion, offset, key_rows, key_limit, causal, score_scale):
    scores = (
        jnp.einsum("bhe,khe->hbk", portion, key_rows, preferred_element_type=jnp.float32)
        * score_scale
    )
    key_pos = jnp.arange(key_rows.shape[0])
    allowed = key_pos[None, :] < key_limit
    if causal:
        allowed = allowed & (key_pos[None, :] <= offset + jnp.arange(portion.shape[0])[:, None])
    return jnp.where(allowed[None], scores, MASKED)


def attend(queries, key_rows, values, key_limit, causal, score_scale):
    row_count, head_count, head_size = queries.shape
    block_len = min(512, row_count)
    portions = queries.reshape(row_count // block_len, block_len, head_count, head_size)
    offsets = jnp.arange(row_count // block_len) * block_len

    def one_block(entries):
        portion, offset = entries
        scores = masked_scores(portion, offset, key_rows, key_limit, causal, score_scale)
        row_max = jnp.max(scores, axis=-1, keepdims=True)
        unnormed = jnp.exp(scores - row_max)
        row_sum = jnp.sum(unnormed, axis=-1, keepdims=True)
        probs_low = (unnormed / row_sum).astype(jnp.bfloat16)
        result = jnp.einsum("hbk,khe->bhe", probs_low, values, preferred_element_type=jnp.float32)
        return (result.astype(jnp.bfloat16), row_max[..., 0] + jnp.log(row_sum[..., 0]))

    if not causal:
        result, log_total = lax.map(one_block, (portions, offsets))
        return (result.reshape(row_count, head_count, head_size), log_total)
    results, totals = [], []
    for index in range(row_count // block_len):
        key_end = (index + 1) * block_len
        scores = masked_scores(
            portions[index], index * block_len, key_rows[:key_end], key_limit, causal, score_scale
        )
        row_max = jnp.max(scores, axis=-1, keepdims=True)
        unnormed = jnp.exp(scores - row_max)
        row_sum = jnp.sum(unnormed, axis=-1, keepdims=True)
        probs_low = (unnormed / row_sum).astype(jnp.bfloat16)
        result = jnp.einsum(
            "hbk,khe->bhe", probs_low, values[:key_end], preferred_element_type=jnp.float32
        )
        results.append(result.astype(jnp.bfloat16))
        totals.append(row_max[..., 0] + jnp.log(row_sum[..., 0]))
    return (jnp.concatenate(results).reshape(row_count, head_count, head_size), jnp.stack(totals))


def attend_back(queries, key_rows, values, log_total, out_grad, key_limit, causal, score_scale):
    row_count, head_count, head_size = queries.shape
    block_len = min(512, row_count)
    portions = queries.reshape(row_count // block_len, block_len, head_count, head_size)
    grad_parts = out_grad.reshape(row_count // block_len, block_len, head_count, head_size)
    offsets = jnp.arange(row_count // block_len) * block_len

    def one_block(carry, entries):
        key_grad, value_grad = carry
        portion, grad_part, log_part, offset = entries
        scores = masked_scores(portion, offset, key_rows, key_limit, causal, score_scale)
        probs = jnp.exp(scores - log_part[..., None])
        probs_grad = jnp.einsum(
            "bhe,khe->hbk", grad_part, values, preferred_element_type=jnp.float32
        )
        row_dot = jnp.sum(probs * probs_grad, axis=-1, keepdims=True)
        scores_grad = (probs * (probs_grad - row_dot)).astype(jnp.bfloat16)
        value_grad = value_grad + jnp.einsum(
            "hbk,bhe->khe",
            probs.astype(jnp.bfloat16),
            grad_part,
            preferred_element_type=jnp.float32,
        )
        key_grad = (
            key_grad
            + jnp.einsum("hbk,bhe->khe", scores_grad, portion, preferred_element_type=jnp.float32)
            * score_scale
        )
        query_grad = (
            jnp.einsum("hbk,khe->bhe", scores_grad, key_rows, preferred_element_type=jnp.float32)
            * score_scale
        )
        return ((key_grad, value_grad), query_grad)

    empty = jnp.zeros(key_rows.shape, jnp.float32)
    if not causal:
        (key_grad, value_grad), query_grad = lax.scan(
            one_block, (empty, empty), (portions, grad_parts, log_total, offsets)
        )
        return (query_grad.reshape(row_count, head_count, head_size), key_grad, value_grad)
    key_grad, value_grad, query_grads = empty, empty, []
    for index in range(row_count // block_len):
        key_end = (index + 1) * block_len
        portion, grad_part = portions[index], grad_parts[index]
        keys, vals = key_rows[:key_end], values[:key_end]
        scores = masked_scores(portion, index * block_len, keys, key_limit, causal, score_scale)
        probs = jnp.exp(scores - log_total[index][..., None])
        probs_grad = jnp.einsum("bhe,khe->hbk", grad_part, vals, preferred_element_type=jnp.float32)
        row_dot = jnp.sum(probs * probs_grad, axis=-1, keepdims=True)
        scores_grad = (probs * (probs_grad - row_dot)).astype(jnp.bfloat16)
        value_part = jnp.einsum(
            "hbk,bhe->khe", probs.astype(jnp.bfloat16), grad_part, preferred_element_type=jnp.float32
        )
        key_part = (
            jnp.einsum("hbk,bhe->khe", scores_grad, portion, preferred_element_type=jnp.float32)
            * score_scale
        )
        value_grad = value_grad.at[:key_end].add(value_part)
        key_grad = key_grad.at[:key_end].add(key_part)
        query_grads.append(
            jnp.einsum("hbk,khe->bhe", scores_grad, keys, preferred_element_type=jnp.float32)
            * score_scale
        )
    query_grad = jnp.concatenate(query_grads)
    return (query_grad.reshape(row_count, head_count, head_size), key_grad, value_grad)


def head_total(partial_value):
    return lax.psum(partial_value.astype(jnp.bfloat16), "tensor").astype(jnp.float32)


def relay_pieces(block, axis):
    count = lax.axis_size(axis)
    me = lax.axis_index(axis)
    pieces = [(block, me)]
    from_left, from_right = block, block
    for k in range(1, count):
        from_left = lax.ppermute(from_left, axis, [(i, i + 1) for i in range(k - 1, count - 1)])
        from_right = lax.ppermute(from_right, axis, [(i, i - 1) for i in range(1, count - k + 1)])
        pieces.append((from_left, me - k))
        pieces.append((from_right, me + k))
    return pieces


def relay_scatter(value, axis):
    count = lax.axis_size(axis)
    me = lax.axis_index(axis)
    shards = value.reshape((count, value.shape[0] // count) + value.shape[1:])

    def pick(index):
        return lax.dynamic_index_in_dim(shards, jnp.clip(index, 0, count - 1), 0, keepdims=False)

    to_right = to_left = None
    for k in range(1, count):
        send_right = pick(me + count - k).astype(jnp.float32)
        send_left = pick(me - (count - k)).astype(jnp.float32)
        if to_right is not None:
            send_right = send_right + to_right.astype(jnp.float32)
            send_left = send_left + to_left.astype(jnp.float32)
        to_right = lax.ppermute(
            send_right.astype(value.dtype), axis, [(i, i + 1) for i in range(min(k, count - 1))]
        )
        to_left = lax.ppermute(
            send_left.astype(value.dtype), axis, [(i, i - 1) for i in range(max(count - k, 1), count)]
        )
    total = pick(me).astype(jnp.float32)
    if to_right is not None:
        total = total + to_right.astype(jnp.float32) + to_left.astype(jnp.float32)
    return total.astype(value.dtype)


def relay_total(partial_value):
    low_value = partial_value.astype(jnp.bfloat16)
    reduced = relay_scatter(low_value, "tensor")
    pieces = relay_pieces(reduced, "tensor")
    shards = []
    for owner in range(len(pieces) // 2 + 1):
        shard = jnp.zeros_like(reduced)
        for piece, source in pieces:
            shard = jnp.where(source == owner, piece, shard)
        shards.append(shard)
    return jnp.concatenate(shards).astype(jnp.float32)


def stacked_psum(matrix, rows, axis):
    pad = (-(matrix.shape[0] + len(rows))) % 16
    extra = jnp.stack(rows + [jnp.zeros_like(rows[0])] * pad)
    summed = lax.psum(jnp.concatenate([matrix, extra]).astype(jnp.bfloat16), axis)
    summed = summed.astype(jnp.float32)
    count = matrix.shape[0]
    return [summed[:count]] + [summed[count + i] for i in range(len(rows))]


def dp_sum(term):
    return lax.psum(term.astype(jnp.bfloat16), "dp").astype(jnp.float32)


def gathered_sum(block, weights, spec):
    count = weights.shape[0]
    total = None
    for piece, source in relay_pieces(block, "tensor"):
        weight = lax.dynamic_index_in_dim(weights, jnp.clip(source, 0, count - 1), 0, keepdims=False)
        partial_value = jnp.einsum(spec, piece, weight, preferred_element_type=jnp.float32)
        partial_value = partial_value.astype(jnp.bfloat16).astype(jnp.float32)
        total = partial_value if total is None else total + partial_value
        total = lax.optimization_barrier(total)
    return total


def local(
    frames,
    text_states,
    frame_len,
    text_token_length,
    self_gain,
    self_bias,
    cross_gain,
    cross_bias,
    feed_gain,
    feed_bias,
    self_qkv,
    self_out,
    cross_query,
    cross_keyval,
    cross_out,
    feed_up,
    feed_down,
    cotangent,
):
    clip_count, slot_len, model_width = frames.shape
    text_count = text_states.shape[1]
    local_width = self_out.shape[0]
    head_count = local_width // HEAD
    score_scale = HEAD ** (-0.5)
    row_total = clip_count * slot_len
    inputs = frames.reshape(row_total, model_width).astype(jnp.float32)
    out_grad = cotangent.reshape(row_total, model_width)
    normed_self = layer_norm(inputs, self_gain, self_bias).astype(jnp.bfloat16)
    projected = jnp.einsum(
        "sd,cde->cse", normed_self, self_qkv, preferred_element_type=jnp.float32
    ).astype(jnp.bfloat16)
    projected = projected.reshape(3, clip_count, slot_len, head_count, HEAD)

    def self_clip(entries):
        return attend(entries[0], entries[1], entries[2], entries[3], True, score_scale)

    self_heads, self_log = lax.map(self_clip, (projected[0], projected[1], projected[2], frame_len))
    self_flat = self_heads.reshape(row_total, local_width)
    self_out_all = lax.all_gather(self_out, "tensor")
    cross_out_all = lax.all_gather(cross_out, "tensor")
    cross_query_all = lax.all_gather(cross_query, "tensor")
    after_self = inputs + gathered_sum(self_flat, self_out_all, "sk,kd->sd")
    normed_cross = layer_norm(after_self, cross_gain, cross_bias).astype(jnp.bfloat16)
    cross_queries = jnp.dot(normed_cross, cross_query, preferred_element_type=jnp.float32).astype(
        jnp.bfloat16
    )
    cross_queries = cross_queries.reshape(clip_count, slot_len, head_count, HEAD)
    text_proj = jnp.einsum(
        "ctd,gde->gcte", text_states, cross_keyval, preferred_element_type=jnp.float32
    ).astype(jnp.bfloat16)
    text_proj = text_proj.reshape(2, clip_count, text_count, head_count, HEAD)

    def cross_clip(entries):
        return attend(entries[0], entries[1], entries[2], entries[3], False, score_scale)

    cross_heads, cross_log = lax.map(
        cross_clip, (cross_queries, text_proj[0], text_proj[1], text_token_length)
    )
    cross_flat = cross_heads.reshape(row_total, local_width)
    after_cross = after_self + gathered_sum(cross_flat, cross_out_all, "sk,kd->sd")
    normed_feed = layer_norm(after_cross, feed_gain, feed_bias).astype(jnp.bfloat16)
    upward = jnp.dot(normed_feed, feed_up, preferred_element_type=jnp.float32)
    active = gelu_exact(upward).astype(jnp.bfloat16)
    feed_part = jnp.dot(active, feed_down, preferred_element_type=jnp.float32)
    feed_low = feed_part.astype(jnp.bfloat16)
    active_grad = jnp.einsum("sd,kd->sk", out_grad, feed_down, preferred_element_type=jnp.float32)
    _, gelu_pull = jax.vjp(gelu_exact, upward)
    upward_grad = gelu_pull(active_grad)[0].astype(jnp.bfloat16)
    downward_gradient = jnp.einsum(
        "sk,sd->kd", active, out_grad, preferred_element_type=jnp.float32
    )
    up_grad = jnp.einsum("sd,sk->dk", normed_feed, upward_grad, preferred_element_type=jnp.float32)
    feed_input_part = jnp.einsum(
        "sk,dk->sd", upward_grad, feed_up, preferred_element_type=jnp.float32
    )
    feed_back = norm_back(after_cross, feed_gain, feed_bias, relay_total(feed_input_part))
    feed_sums = [dp_sum(up_grad), dp_sum(downward_gradient)]
    cross_grad_rows = out_grad.astype(jnp.float32) + feed_back[0]
    cross_grad_low = cross_grad_rows.astype(jnp.bfloat16)
    cout_grad = jnp.einsum(
        "sk,sd->kd", cross_flat, cross_grad_low, preferred_element_type=jnp.float32
    )
    cross_heads_grad = jnp.einsum(
        "sd,kd->sk", cross_grad_low, cross_out, preferred_element_type=jnp.float32
    ).astype(jnp.bfloat16)
    cross_heads_grad = cross_heads_grad.reshape(clip_count, slot_len, head_count, HEAD)

    def cross_clip_back(entries):
        return attend_back(
            entries[0],
            entries[1],
            entries[2],
            entries[3],
            entries[4],
            entries[5],
            False,
            score_scale,
        )

    cquery_heads, ckey_heads, cvalue_heads = lax.map(
        cross_clip_back,
        (cross_queries, text_proj[0], text_proj[1], cross_log, cross_heads_grad, text_token_length),
    )
    query_grad_low = cquery_heads.reshape(row_total, local_width).astype(jnp.bfloat16)
    feed_low, query_grad_low = lax.optimization_barrier((feed_low, query_grad_low))
    block_out = (after_cross + lax.psum(feed_low, "tensor").astype(jnp.float32)).astype(
        jnp.bfloat16
    )
    keyval_grad_low = jnp.stack((ckey_heads, cvalue_heads)).astype(jnp.bfloat16)
    keyval_grad_low = keyval_grad_low.reshape(2, clip_count, text_count, local_width)
    cquery_grad = jnp.einsum(
        "sd,se->de", normed_cross, query_grad_low, preferred_element_type=jnp.float32
    )
    ckeyval_grad = jnp.einsum(
        "ctd,gcte->gde", text_states, keyval_grad_low, preferred_element_type=jnp.float32
    )
    text_part = jnp.einsum(
        "gcte,gde->ctd", keyval_grad_low, cross_keyval, preferred_element_type=jnp.float32
    )
    cross_sum = gathered_sum(query_grad_low, cross_query_all, "se,de->sd")
    text_grad = lax.psum(text_part.astype(jnp.bfloat16), "tensor").astype(jnp.float32)
    cross_back = norm_back(after_self, cross_gain, cross_bias, cross_sum)
    self_grad_rows = cross_grad_rows + cross_back[0]
    feed_sums, self_grad_rows = lax.optimization_barrier((feed_sums, self_grad_rows))
    self_grad_low = self_grad_rows.astype(jnp.bfloat16)
    sout_grad = jnp.einsum(
        "sk,sd->kd", self_flat, self_grad_low, preferred_element_type=jnp.float32
    )
    self_heads_grad = jnp.einsum(
        "sd,kd->sk", self_grad_low, self_out, preferred_element_type=jnp.float32
    ).astype(jnp.bfloat16)
    self_heads_grad = self_heads_grad.reshape(clip_count, slot_len, head_count, HEAD)

    def self_clip_back(entries):
        return attend_back(
            entries[0],
            entries[1],
            entries[2],
            entries[3],
            entries[4],
            entries[5],
            True,
            score_scale,
        )

    self_query_heads, self_key_heads, self_value_heads = lax.map(
        self_clip_back,
        (projected[0], projected[1], projected[2], self_log, self_heads_grad, frame_len),
    )
    projection_gradient = jnp.stack((self_query_heads, self_key_heads, self_value_heads)).astype(
        jnp.bfloat16
    )
    projection_gradient = projection_gradient.reshape(3, row_total, local_width)
    qkv_grad = jnp.einsum(
        "sd,cse->cde", normed_self, projection_gradient, preferred_element_type=jnp.float32
    )
    self_input_part = jnp.einsum(
        "cse,cde->sd", projection_gradient, self_qkv, preferred_element_type=jnp.float32
    )
    self_back = norm_back(inputs, self_gain, self_bias, relay_total(self_input_part))
    self_norm_terms = (dp_sum(self_back[1]), dp_sum(self_back[2]))
    frames_grad = self_grad_rows + self_back[0]
    gain_terms = (
        self_back[1],
        self_back[2],
        cross_back[1],
        cross_back[2],
        feed_back[1],
        feed_back[2],
    )
    late_sums = [dp_sum(term) for term in (qkv_grad, sout_grad, cquery_grad, ckeyval_grad)]
    late_sums = late_sums + stacked_psum(
        cout_grad, [cross_back[1], cross_back[2], feed_back[1], feed_back[2]], "dp"
    )
    summed = (
        self_norm_terms[0],
        self_norm_terms[1],
        late_sums[5],
        late_sums[6],
        late_sums[7],
        late_sums[8],
        late_sums[0],
        late_sums[1],
        late_sums[2],
        late_sums[3],
        late_sums[4],
        feed_sums[0],
        feed_sums[1],
    )
    return (
        block_out.reshape(clip_count, slot_len, model_width),
        frames_grad.reshape(clip_count, slot_len, model_width),
        text_grad,
        summed[0],
        summed[1],
        summed[2],
        summed[3],
        summed[4],
        summed[5],
        summed[6],
        summed[7],
        summed[8],
        summed[9],
        summed[10],
        summed[11],
        summed[12],
    )


def solution(mesh):
    return jax.shard_map(
        local,
        mesh=mesh,
        in_specs=(
            P("dp", None, None),
            P("dp", None, None),
            P("dp"),
            P("dp"),
            P(),
            P(),
            P(),
            P(),
            P(),
            P(),
            P(None, None, "tensor"),
            P("tensor", None),
            P(None, "tensor"),
            P(None, None, "tensor"),
            P("tensor", None),
            P(None, "tensor"),
            P("tensor", None),
            P("dp", None, None),
        ),
        out_specs=(
            P("dp", None, None),
            P("dp", None, None),
            P("dp", None, None),
            P(),
            P(),
            P(),
            P(),
            P(),
            P(),
            P(None, None, "tensor"),
            P("tensor", None),
            P(None, "tensor"),
            P(None, None, "tensor"),
            P("tensor", None),
            P(None, "tensor"),
            P("tensor", None),
        ),
        check_vma=False,
    )
```

```python
import jax
import jax.numpy as jnp
from jax import lax
from jax.sharding import PartitionSpec as P

HEAD = 64


EPSILON = 1e-05
MASKED = -1e30


def layer_norm(inputs, norm_gain, norm_bias):
    row_mean = jnp.mean(inputs, axis=-1, keepdims=True)
    centred = inputs - row_mean
    spread = jnp.mean(centred * centred, axis=-1, keepdims=True)
    return centred * lax.rsqrt(spread + EPSILON) * norm_gain + norm_bias


def normalized(inputs):
    row_mean = jnp.mean(inputs, axis=-1, keepdims=True)
    centred = inputs - row_mean
    spread = jnp.mean(centred * centred, axis=-1, keepdims=True)
    return centred * lax.rsqrt(spread + EPSILON)


def norm_back(inputs, norm_gain, norm_bias, upstream):
    _, pullback = jax.vjp(layer_norm, inputs, norm_gain, norm_bias)
    return pullback(upstream)


def gelu_exact(inputs):
    return jax.nn.gelu(inputs, approximate=False)


def masked_scores(portion, offset, key_rows, key_limit, causal, score_scale):
    scores = (
        jnp.einsum("bhe,khe->hbk", portion, key_rows, preferred_element_type=jnp.float32)
        * score_scale
    )
    key_pos = jnp.arange(key_rows.shape[0])
    allowed = key_pos[None, :] < key_limit
    if causal:
        allowed = allowed & (key_pos[None, :] <= offset + jnp.arange(portion.shape[0])[:, None])
    return jnp.where(allowed[None], scores, MASKED)


def attend(queries, key_rows, values, key_limit, causal, score_scale):
    row_count, head_count, head_size = queries.shape
    block_len = min(512, row_count)
    portions = queries.reshape(row_count // block_len, block_len, head_count, head_size)
    offsets = jnp.arange(row_count // block_len) * block_len

    def one_block(entries):
        portion, offset = entries
        scores = masked_scores(portion, offset, key_rows, key_limit, causal, score_scale)
        row_max = jnp.max(scores, axis=-1, keepdims=True)
        unnormed = jnp.exp(scores - row_max)
        row_sum = jnp.sum(unnormed, axis=-1, keepdims=True)
        probs_low = (unnormed / row_sum).astype(jnp.bfloat16)
        result = jnp.einsum("hbk,khe->bhe", probs_low, values, preferred_element_type=jnp.float32)
        return (result.astype(jnp.bfloat16), row_max[..., 0] + jnp.log(row_sum[..., 0]))

    if not causal:
        result, log_total = lax.map(one_block, (portions, offsets))
        return (result.reshape(row_count, head_count, head_size), log_total)
    results, totals = [], []
    for index in range(row_count // block_len):
        key_end = (index + 1) * block_len
        scores = masked_scores(
            portions[index], index * block_len, key_rows[:key_end], key_limit, causal, score_scale
        )
        row_max = jnp.max(scores, axis=-1, keepdims=True)
        unnormed = jnp.exp(scores - row_max)
        row_sum = jnp.sum(unnormed, axis=-1, keepdims=True)
        probs_low = (unnormed / row_sum).astype(jnp.bfloat16)
        result = jnp.einsum(
            "hbk,khe->bhe", probs_low, values[:key_end], preferred_element_type=jnp.float32
        )
        results.append(result.astype(jnp.bfloat16))
        totals.append(row_max[..., 0] + jnp.log(row_sum[..., 0]))
    return (jnp.concatenate(results).reshape(row_count, head_count, head_size), jnp.stack(totals))


def attend_back(queries, key_rows, values, log_total, out_grad, key_limit, causal, score_scale):
    row_count, head_count, head_size = queries.shape
    block_len = min(512, row_count)
    portions = queries.reshape(row_count // block_len, block_len, head_count, head_size)
    grad_parts = out_grad.reshape(row_count // block_len, block_len, head_count, head_size)
    offsets = jnp.arange(row_count // block_len) * block_len

    def one_block(carry, entries):
        key_grad, value_grad = carry
        portion, grad_part, log_part, offset = entries
        scores = masked_scores(portion, offset, key_rows, key_limit, causal, score_scale)
        probs = jnp.exp(scores - log_part[..., None])
        probs_grad = jnp.einsum(
            "bhe,khe->hbk", grad_part, values, preferred_element_type=jnp.float32
        )
        row_dot = jnp.sum(probs * probs_grad, axis=-1, keepdims=True)
        scores_grad = (probs * (probs_grad - row_dot)).astype(jnp.bfloat16)
        value_grad = value_grad + jnp.einsum(
            "hbk,bhe->khe",
            probs.astype(jnp.bfloat16),
            grad_part,
            preferred_element_type=jnp.float32,
        )
        key_grad = (
            key_grad
            + jnp.einsum("hbk,bhe->khe", scores_grad, portion, preferred_element_type=jnp.float32)
            * score_scale
        )
        query_grad = (
            jnp.einsum("hbk,khe->bhe", scores_grad, key_rows, preferred_element_type=jnp.float32)
            * score_scale
        )
        return ((key_grad, value_grad), query_grad)

    empty = jnp.zeros(key_rows.shape, jnp.float32)
    if not causal:
        (key_grad, value_grad), query_grad = lax.scan(
            one_block, (empty, empty), (portions, grad_parts, log_total, offsets)
        )
        return (query_grad.reshape(row_count, head_count, head_size), key_grad, value_grad)
    key_grad, value_grad, query_grads = empty, empty, []
    for index in range(row_count // block_len):
        key_end = (index + 1) * block_len
        portion, grad_part = portions[index], grad_parts[index]
        keys, vals = key_rows[:key_end], values[:key_end]
        scores = masked_scores(portion, index * block_len, keys, key_limit, causal, score_scale)
        probs = jnp.exp(scores - log_total[index][..., None])
        probs_grad = jnp.einsum("bhe,khe->hbk", grad_part, vals, preferred_element_type=jnp.float32)
        row_dot = jnp.sum(probs * probs_grad, axis=-1, keepdims=True)
        scores_grad = (probs * (probs_grad - row_dot)).astype(jnp.bfloat16)
        value_part = jnp.einsum(
            "hbk,bhe->khe", probs.astype(jnp.bfloat16), grad_part, preferred_element_type=jnp.float32
        )
        key_part = (
            jnp.einsum("hbk,bhe->khe", scores_grad, portion, preferred_element_type=jnp.float32)
            * score_scale
        )
        value_grad = value_grad.at[:key_end].add(value_part)
        key_grad = key_grad.at[:key_end].add(key_part)
        query_grads.append(
            jnp.einsum("hbk,khe->bhe", scores_grad, keys, preferred_element_type=jnp.float32)
            * score_scale
        )
    query_grad = jnp.concatenate(query_grads)
    return (query_grad.reshape(row_count, head_count, head_size), key_grad, value_grad)


def head_total(partial_value):
    return lax.psum(partial_value.astype(jnp.bfloat16), "tensor").astype(jnp.float32)


def relay_pieces(block, axis):
    count = lax.axis_size(axis)
    me = lax.axis_index(axis)
    pieces = [(block, me)]
    from_left, from_right = block, block
    for k in range(1, count):
        from_left = lax.ppermute(from_left, axis, [(i, i + 1) for i in range(k - 1, count - 1)])
        from_right = lax.ppermute(from_right, axis, [(i, i - 1) for i in range(1, count - k + 1)])
        pieces.append((from_left, me - k))
        pieces.append((from_right, me + k))
    return pieces


def relay_scatter(value, axis):
    count = lax.axis_size(axis)
    me = lax.axis_index(axis)
    shards = value.reshape((count, value.shape[0] // count) + value.shape[1:])

    def pick(index):
        return lax.dynamic_index_in_dim(shards, jnp.clip(index, 0, count - 1), 0, keepdims=False)

    to_right = to_left = None
    for k in range(1, count):
        send_right = pick(me + count - k).astype(jnp.float32)
        send_left = pick(me - (count - k)).astype(jnp.float32)
        if to_right is not None:
            send_right = send_right + to_right.astype(jnp.float32)
            send_left = send_left + to_left.astype(jnp.float32)
        to_right = lax.ppermute(
            send_right.astype(value.dtype), axis, [(i, i + 1) for i in range(min(k, count - 1))]
        )
        to_left = lax.ppermute(
            send_left.astype(value.dtype), axis, [(i, i - 1) for i in range(max(count - k, 1), count)]
        )
    total = pick(me).astype(jnp.float32)
    if to_right is not None:
        total = total + to_right.astype(jnp.float32) + to_left.astype(jnp.float32)
    return total.astype(value.dtype)


def relay_total(partial_value):
    low_value = partial_value.astype(jnp.bfloat16)
    reduced = relay_scatter(low_value, "tensor")
    pieces = relay_pieces(reduced, "tensor")
    shards = []
    for owner in range(len(pieces) // 2 + 1):
        shard = jnp.zeros_like(reduced)
        for piece, source in pieces:
            shard = jnp.where(source == owner, piece, shard)
        shards.append(shard)
    return jnp.concatenate(shards).astype(jnp.float32)


def stacked_psum(matrix, rows, axis):
    pad = (-(matrix.shape[0] + len(rows))) % 16
    extra = jnp.stack(rows + [jnp.zeros_like(rows[0])] * pad)
    summed = lax.psum(jnp.concatenate([matrix, extra]).astype(jnp.bfloat16), axis)
    summed = summed.astype(jnp.float32)
    count = matrix.shape[0]
    return [summed[:count]] + [summed[count + i] for i in range(len(rows))]


def dp_sum(term):
    return lax.psum(term.astype(jnp.bfloat16), "dp").astype(jnp.float32)


def paired_sum(block, weight_pieces, spec):
    total = None
    for (piece, _), (weight, _) in zip(relay_pieces(block, "tensor"), weight_pieces):
        partial_value = jnp.einsum(spec, piece, weight, preferred_element_type=jnp.float32)
        partial_value = partial_value.astype(jnp.bfloat16).astype(jnp.float32)
        total = partial_value if total is None else total + partial_value
        total = lax.optimization_barrier(total)
    return total


def gathered_sum(block, weights, spec):
    count = weights.shape[0]
    total = None
    for piece, source in relay_pieces(block, "tensor"):
        weight = lax.dynamic_index_in_dim(weights, jnp.clip(source, 0, count - 1), 0, keepdims=False)
        partial_value = jnp.einsum(spec, piece, weight, preferred_element_type=jnp.float32)
        partial_value = partial_value.astype(jnp.bfloat16).astype(jnp.float32)
        total = partial_value if total is None else total + partial_value
        total = lax.optimization_barrier(total)
    return total


def local(
    frames,
    text_states,
    frame_len,
    text_token_length,
    self_gain,
    self_bias,
    cross_gain,
    cross_bias,
    feed_gain,
    feed_bias,
    self_qkv,
    self_out,
    cross_query,
    cross_keyval,
    cross_out,
    feed_up,
    feed_down,
    cotangent,
):
    clip_count, slot_len, model_width = frames.shape
    text_count = text_states.shape[1]
    local_width = self_out.shape[0]
    head_count = local_width // HEAD
    score_scale = HEAD ** (-0.5)
    row_total = clip_count * slot_len
    inputs = frames.reshape(row_total, model_width).astype(jnp.float32)
    out_grad = cotangent.reshape(row_total, model_width)
    normed_self = layer_norm(inputs, self_gain, self_bias).astype(jnp.bfloat16)
    projected = jnp.einsum(
        "sd,cde->cse", normed_self, self_qkv, preferred_element_type=jnp.float32
    ).astype(jnp.bfloat16)
    projected = projected.reshape(3, clip_count, slot_len, head_count, HEAD)

    def self_clip(entries):
        return attend(entries[0], entries[1], entries[2], entries[3], True, score_scale)

    self_heads, self_log = lax.map(self_clip, (projected[0], projected[1], projected[2], frame_len))
    self_flat = self_heads.reshape(row_total, local_width)
    self_out_all = lax.all_gather(self_out, "tensor")
    cross_out_all = lax.all_gather(cross_out, "tensor")
    after_self = inputs + gathered_sum(self_flat, self_out_all, "sk,kd->sd")
    normed_cross = layer_norm(after_self, cross_gain, cross_bias).astype(jnp.bfloat16)
    cross_queries = jnp.dot(normed_cross, cross_query, preferred_element_type=jnp.float32).astype(
        jnp.bfloat16
    )
    cross_queries = cross_queries.reshape(clip_count, slot_len, head_count, HEAD)
    text_proj = jnp.einsum(
        "ctd,gde->gcte", text_states, cross_keyval, preferred_element_type=jnp.float32
    ).astype(jnp.bfloat16)
    text_proj = text_proj.reshape(2, clip_count, text_count, head_count, HEAD)

    def cross_clip(entries):
        return attend(entries[0], entries[1], entries[2], entries[3], False, score_scale)

    cross_heads, cross_log = lax.map(
        cross_clip, (cross_queries, text_proj[0], text_proj[1], text_token_length)
    )
    cross_flat = cross_heads.reshape(row_total, local_width)
    after_cross = after_self + gathered_sum(cross_flat, cross_out_all, "sk,kd->sd")
    normed_feed = layer_norm(after_cross, feed_gain, feed_bias).astype(jnp.bfloat16)
    upward = jnp.dot(normed_feed, feed_up, preferred_element_type=jnp.float32)
    active = gelu_exact(upward).astype(jnp.bfloat16)
    feed_part = jnp.dot(active, feed_down, preferred_element_type=jnp.float32)
    feed_low = feed_part.astype(jnp.bfloat16)
    active_grad = jnp.einsum("sd,kd->sk", out_grad, feed_down, preferred_element_type=jnp.float32)
    _, gelu_pull = jax.vjp(gelu_exact, upward)
    upward_grad = gelu_pull(active_grad)[0].astype(jnp.bfloat16)
    downward_gradient = jnp.einsum(
        "sk,sd->kd", active, out_grad, preferred_element_type=jnp.float32
    )
    up_grad = jnp.einsum("sd,sk->dk", normed_feed, upward_grad, preferred_element_type=jnp.float32)
    feed_input_part = jnp.einsum(
        "sk,dk->sd", upward_grad, feed_up, preferred_element_type=jnp.float32
    )
    feed_back = norm_back(after_cross, feed_gain, feed_bias, relay_total(feed_input_part))
    feed_sums = [dp_sum(up_grad), dp_sum(downward_gradient)]
    cross_grad_rows = out_grad.astype(jnp.float32) + feed_back[0]
    query_weight, cross_grad_rows = lax.optimization_barrier((cross_query, cross_grad_rows))
    query_weight_pieces = relay_pieces(query_weight, "tensor")
    cross_grad_low = cross_grad_rows.astype(jnp.bfloat16)
    cout_grad = jnp.einsum(
        "sk,sd->kd", cross_flat, cross_grad_low, preferred_element_type=jnp.float32
    )
    cross_heads_grad = jnp.einsum(
        "sd,kd->sk", cross_grad_low, cross_out, preferred_element_type=jnp.float32
    ).astype(jnp.bfloat16)
    cross_heads_grad = cross_heads_grad.reshape(clip_count, slot_len, head_count, HEAD)

    def cross_clip_back(entries):
        return attend_back(
            entries[0],
            entries[1],
            entries[2],
            entries[3],
            entries[4],
            entries[5],
            False,
            score_scale,
        )

    cquery_heads, ckey_heads, cvalue_heads = lax.map(
        cross_clip_back,
        (cross_queries, text_proj[0], text_proj[1], cross_log, cross_heads_grad, text_token_length),
    )
    query_grad_low = cquery_heads.reshape(row_total, local_width).astype(jnp.bfloat16)
    feed_low, query_grad_low = lax.optimization_barrier((feed_low, query_grad_low))
    block_out = (after_cross + lax.psum(feed_low, "tensor").astype(jnp.float32)).astype(
        jnp.bfloat16
    )
    keyval_grad_low = jnp.stack((ckey_heads, cvalue_heads)).astype(jnp.bfloat16)
    keyval_grad_low = keyval_grad_low.reshape(2, clip_count, text_count, local_width)
    cquery_grad = jnp.einsum(
        "sd,se->de", normed_cross, query_grad_low, preferred_element_type=jnp.float32
    )
    ckeyval_grad = jnp.einsum(
        "ctd,gcte->gde", text_states, keyval_grad_low, preferred_element_type=jnp.float32
    )
    text_part = jnp.einsum(
        "gcte,gde->ctd", keyval_grad_low, cross_keyval, preferred_element_type=jnp.float32
    )
    cross_sum = paired_sum(query_grad_low, query_weight_pieces, "se,de->sd")
    text_grad = lax.psum(text_part.astype(jnp.bfloat16), "tensor").astype(jnp.float32)
    cross_back = norm_back(after_self, cross_gain, cross_bias, cross_sum)
    self_grad_rows = cross_grad_rows + cross_back[0]
    feed_sums, self_grad_rows = lax.optimization_barrier((feed_sums, self_grad_rows))
    self_grad_low = self_grad_rows.astype(jnp.bfloat16)
    sout_grad = jnp.einsum(
        "sk,sd->kd", self_flat, self_grad_low, preferred_element_type=jnp.float32
    )
    self_heads_grad = jnp.einsum(
        "sd,kd->sk", self_grad_low, self_out, preferred_element_type=jnp.float32
    ).astype(jnp.bfloat16)
    self_heads_grad = self_heads_grad.reshape(clip_count, slot_len, head_count, HEAD)

    def self_clip_back(entries):
        return attend_back(
            entries[0],
            entries[1],
            entries[2],
            entries[3],
            entries[4],
            entries[5],
            True,
            score_scale,
        )

    self_query_heads, self_key_heads, self_value_heads = lax.map(
        self_clip_back,
        (projected[0], projected[1], projected[2], self_log, self_heads_grad, frame_len),
    )
    projection_gradient = jnp.stack((self_query_heads, self_key_heads, self_value_heads)).astype(
        jnp.bfloat16
    )
    projection_gradient = projection_gradient.reshape(3, row_total, local_width)
    qkv_grad = jnp.einsum(
        "sd,cse->cde", normed_self, projection_gradient, preferred_element_type=jnp.float32
    )
    self_input_part = jnp.einsum(
        "cse,cde->sd", projection_gradient, self_qkv, preferred_element_type=jnp.float32
    )
    self_back = norm_back(inputs, self_gain, self_bias, relay_total(self_input_part))
    self_norm_terms = (dp_sum(self_back[1]), dp_sum(self_back[2]))
    frames_grad = self_grad_rows + self_back[0]
    gain_terms = (
        self_back[1],
        self_back[2],
        cross_back[1],
        cross_back[2],
        feed_back[1],
        feed_back[2],
    )
    late_sums = [dp_sum(term) for term in (qkv_grad, sout_grad, cquery_grad, ckeyval_grad)]
    late_sums = late_sums + stacked_psum(
        cout_grad, [cross_back[1], cross_back[2], feed_back[1], feed_back[2]], "dp"
    )
    summed = (
        self_norm_terms[0],
        self_norm_terms[1],
        late_sums[5],
        late_sums[6],
        late_sums[7],
        late_sums[8],
        late_sums[0],
        late_sums[1],
        late_sums[2],
        late_sums[3],
        late_sums[4],
        feed_sums[0],
        feed_sums[1],
    )
    return (
        block_out.reshape(clip_count, slot_len, model_width),
        frames_grad.reshape(clip_count, slot_len, model_width),
        text_grad,
        summed[0],
        summed[1],
        summed[2],
        summed[3],
        summed[4],
        summed[5],
        summed[6],
        summed[7],
        summed[8],
        summed[9],
        summed[10],
        summed[11],
        summed[12],
    )


def solution(mesh):
    return jax.shard_map(
        local,
        mesh=mesh,
        in_specs=(
            P("dp", None, None),
            P("dp", None, None),
            P("dp"),
            P("dp"),
            P(),
            P(),
            P(),
            P(),
            P(),
            P(),
            P(None, None, "tensor"),
            P("tensor", None),
            P(None, "tensor"),
            P(None, None, "tensor"),
            P("tensor", None),
            P(None, "tensor"),
            P("tensor", None),
            P("dp", None, None),
        ),
        out_specs=(
            P("dp", None, None),
            P("dp", None, None),
            P("dp", None, None),
            P(),
            P(),
            P(),
            P(),
            P(),
            P(),
            P(None, None, "tensor"),
            P("tensor", None),
            P(None, "tensor"),
            P(None, None, "tensor"),
            P("tensor", None),
            P(None, "tensor"),
            P("tensor", None),
        ),
        check_vma=False,
    )
```

```python
import jax
import jax.numpy as jnp
from jax import lax
from jax.sharding import PartitionSpec as P

HEAD = 64


EPSILON = 1e-05
MASKED = -1e30


def layer_norm(inputs, norm_gain, norm_bias):
    row_mean = jnp.mean(inputs, axis=-1, keepdims=True)
    centred = inputs - row_mean
    spread = jnp.mean(centred * centred, axis=-1, keepdims=True)
    return centred * lax.rsqrt(spread + EPSILON) * norm_gain + norm_bias


def normalized(inputs):
    row_mean = jnp.mean(inputs, axis=-1, keepdims=True)
    centred = inputs - row_mean
    spread = jnp.mean(centred * centred, axis=-1, keepdims=True)
    return centred * lax.rsqrt(spread + EPSILON)


def norm_back(inputs, norm_gain, norm_bias, upstream):
    _, pullback = jax.vjp(layer_norm, inputs, norm_gain, norm_bias)
    return pullback(upstream)


def gelu_exact(inputs):
    return jax.nn.gelu(inputs, approximate=False)


def masked_scores(portion, offset, key_rows, key_limit, causal, score_scale):
    scores = (
        jnp.einsum("bhe,khe->hbk", portion, key_rows, preferred_element_type=jnp.float32)
        * score_scale
    )
    key_pos = jnp.arange(key_rows.shape[0])
    allowed = key_pos[None, :] < key_limit
    if causal:
        allowed = allowed & (key_pos[None, :] <= offset + jnp.arange(portion.shape[0])[:, None])
    return jnp.where(allowed[None], scores, MASKED)


def attend(queries, key_rows, values, key_limit, causal, score_scale):
    row_count, head_count, head_size = queries.shape
    block_len = min(512, row_count)
    portions = queries.reshape(row_count // block_len, block_len, head_count, head_size)
    offsets = jnp.arange(row_count // block_len) * block_len

    def one_block(entries):
        portion, offset = entries
        scores = masked_scores(portion, offset, key_rows, key_limit, causal, score_scale)
        row_max = jnp.max(scores, axis=-1, keepdims=True)
        unnormed = jnp.exp(scores - row_max)
        row_sum = jnp.sum(unnormed, axis=-1, keepdims=True)
        probs_low = (unnormed / row_sum).astype(jnp.bfloat16)
        result = jnp.einsum("hbk,khe->bhe", probs_low, values, preferred_element_type=jnp.float32)
        return (result.astype(jnp.bfloat16), row_max[..., 0] + jnp.log(row_sum[..., 0]))

    if not causal:
        result, log_total = lax.map(one_block, (portions, offsets))
        return (result.reshape(row_count, head_count, head_size), log_total)
    results, totals = [], []
    for index in range(row_count // block_len):
        key_end = (index + 1) * block_len
        scores = masked_scores(
            portions[index], index * block_len, key_rows[:key_end], key_limit, causal, score_scale
        )
        row_max = jnp.max(scores, axis=-1, keepdims=True)
        unnormed = jnp.exp(scores - row_max)
        row_sum = jnp.sum(unnormed, axis=-1, keepdims=True)
        probs_low = (unnormed / row_sum).astype(jnp.bfloat16)
        result = jnp.einsum(
            "hbk,khe->bhe", probs_low, values[:key_end], preferred_element_type=jnp.float32
        )
        results.append(result.astype(jnp.bfloat16))
        totals.append(row_max[..., 0] + jnp.log(row_sum[..., 0]))
    return (jnp.concatenate(results).reshape(row_count, head_count, head_size), jnp.stack(totals))


def attend_back(queries, key_rows, values, log_total, out_grad, key_limit, causal, score_scale):
    row_count, head_count, head_size = queries.shape
    block_len = min(512, row_count)
    portions = queries.reshape(row_count // block_len, block_len, head_count, head_size)
    grad_parts = out_grad.reshape(row_count // block_len, block_len, head_count, head_size)
    offsets = jnp.arange(row_count // block_len) * block_len

    def one_block(carry, entries):
        key_grad, value_grad = carry
        portion, grad_part, log_part, offset = entries
        scores = masked_scores(portion, offset, key_rows, key_limit, causal, score_scale)
        probs = jnp.exp(scores - log_part[..., None])
        probs_grad = jnp.einsum(
            "bhe,khe->hbk", grad_part, values, preferred_element_type=jnp.float32
        )
        row_dot = jnp.sum(probs * probs_grad, axis=-1, keepdims=True)
        scores_grad = (probs * (probs_grad - row_dot)).astype(jnp.bfloat16)
        value_grad = value_grad + jnp.einsum(
            "hbk,bhe->khe",
            probs.astype(jnp.bfloat16),
            grad_part,
            preferred_element_type=jnp.float32,
        )
        key_grad = (
            key_grad
            + jnp.einsum("hbk,bhe->khe", scores_grad, portion, preferred_element_type=jnp.float32)
            * score_scale
        )
        query_grad = (
            jnp.einsum("hbk,khe->bhe", scores_grad, key_rows, preferred_element_type=jnp.float32)
            * score_scale
        )
        return ((key_grad, value_grad), query_grad)

    empty = jnp.zeros(key_rows.shape, jnp.float32)
    if not causal:
        (key_grad, value_grad), query_grad = lax.scan(
            one_block, (empty, empty), (portions, grad_parts, log_total, offsets)
        )
        return (query_grad.reshape(row_count, head_count, head_size), key_grad, value_grad)
    key_grad, value_grad, query_grads = empty, empty, []
    for index in range(row_count // block_len):
        key_end = (index + 1) * block_len
        portion, grad_part = portions[index], grad_parts[index]
        keys, vals = key_rows[:key_end], values[:key_end]
        scores = masked_scores(portion, index * block_len, keys, key_limit, causal, score_scale)
        probs = jnp.exp(scores - log_total[index][..., None])
        probs_grad = jnp.einsum("bhe,khe->hbk", grad_part, vals, preferred_element_type=jnp.float32)
        row_dot = jnp.sum(probs * probs_grad, axis=-1, keepdims=True)
        scores_grad = (probs * (probs_grad - row_dot)).astype(jnp.bfloat16)
        value_part = jnp.einsum(
            "hbk,bhe->khe", probs.astype(jnp.bfloat16), grad_part, preferred_element_type=jnp.float32
        )
        key_part = (
            jnp.einsum("hbk,bhe->khe", scores_grad, portion, preferred_element_type=jnp.float32)
            * score_scale
        )
        value_grad = value_grad.at[:key_end].add(value_part)
        key_grad = key_grad.at[:key_end].add(key_part)
        query_grads.append(
            jnp.einsum("hbk,khe->bhe", scores_grad, keys, preferred_element_type=jnp.float32)
            * score_scale
        )
    query_grad = jnp.concatenate(query_grads)
    return (query_grad.reshape(row_count, head_count, head_size), key_grad, value_grad)


def head_total(partial_value):
    return lax.psum(partial_value.astype(jnp.bfloat16), "tensor").astype(jnp.float32)


def relay_pieces(block, axis):
    count = lax.axis_size(axis)
    me = lax.axis_index(axis)
    pieces = [(block, me)]
    from_left, from_right = block, block
    for k in range(1, count):
        from_left = lax.ppermute(from_left, axis, [(i, i + 1) for i in range(k - 1, count - 1)])
        from_right = lax.ppermute(from_right, axis, [(i, i - 1) for i in range(1, count - k + 1)])
        pieces.append((from_left, me - k))
        pieces.append((from_right, me + k))
    return pieces


def relay_scatter(value, axis):
    count = lax.axis_size(axis)
    me = lax.axis_index(axis)
    shards = value.reshape((count, value.shape[0] // count) + value.shape[1:])

    def pick(index):
        return lax.dynamic_index_in_dim(shards, jnp.clip(index, 0, count - 1), 0, keepdims=False)

    to_right = to_left = None
    for k in range(1, count):
        send_right = pick(me + count - k).astype(jnp.float32)
        send_left = pick(me - (count - k)).astype(jnp.float32)
        if to_right is not None:
            send_right = send_right + to_right.astype(jnp.float32)
            send_left = send_left + to_left.astype(jnp.float32)
        to_right = lax.ppermute(
            send_right.astype(value.dtype), axis, [(i, i + 1) for i in range(min(k, count - 1))]
        )
        to_left = lax.ppermute(
            send_left.astype(value.dtype), axis, [(i, i - 1) for i in range(max(count - k, 1), count)]
        )
    total = pick(me).astype(jnp.float32)
    if to_right is not None:
        total = total + to_right.astype(jnp.float32) + to_left.astype(jnp.float32)
    return total.astype(value.dtype)


def relay_total(partial_value):
    low_value = partial_value.astype(jnp.bfloat16)
    reduced = relay_scatter(low_value, "tensor")
    pieces = relay_pieces(reduced, "tensor")
    shards = []
    for owner in range(len(pieces) // 2 + 1):
        shard = jnp.zeros_like(reduced)
        for piece, source in pieces:
            shard = jnp.where(source == owner, piece, shard)
        shards.append(shard)
    return jnp.concatenate(shards).astype(jnp.float32)


def stacked_psum(matrix, rows, axis):
    pad = (-(matrix.shape[0] + len(rows))) % 16
    extra = jnp.stack(rows + [jnp.zeros_like(rows[0])] * pad)
    summed = lax.psum(jnp.concatenate([matrix, extra]).astype(jnp.bfloat16), axis)
    summed = summed.astype(jnp.float32)
    count = matrix.shape[0]
    return [summed[:count]] + [summed[count + i] for i in range(len(rows))]


def dp_sum(term):
    return lax.psum(term.astype(jnp.bfloat16), "dp").astype(jnp.float32)


def paired_sum(block, weight_pieces, spec):
    total = None
    for (piece, _), (weight, _) in zip(relay_pieces(block, "tensor"), weight_pieces):
        partial_value = jnp.einsum(spec, piece, weight, preferred_element_type=jnp.float32)
        partial_value = partial_value.astype(jnp.bfloat16).astype(jnp.float32)
        total = partial_value if total is None else total + partial_value
        total = lax.optimization_barrier(total)
    return total


def gathered_sum(block, weights, spec):
    count = weights.shape[0]
    total = None
    for piece, source in relay_pieces(block, "tensor"):
        weight = lax.dynamic_index_in_dim(weights, jnp.clip(source, 0, count - 1), 0, keepdims=False)
        partial_value = jnp.einsum(spec, piece, weight, preferred_element_type=jnp.float32)
        partial_value = partial_value.astype(jnp.bfloat16).astype(jnp.float32)
        total = partial_value if total is None else total + partial_value
        total = lax.optimization_barrier(total)
    return total


def local(
    frames,
    text_states,
    frame_len,
    text_token_length,
    self_gain,
    self_bias,
    cross_gain,
    cross_bias,
    feed_gain,
    feed_bias,
    self_qkv,
    self_out,
    cross_query,
    cross_keyval,
    cross_out,
    feed_up,
    feed_down,
    cotangent,
):
    clip_count, slot_len, model_width = frames.shape
    text_count = text_states.shape[1]
    local_width = self_out.shape[0]
    head_count = local_width // HEAD
    score_scale = HEAD ** (-0.5)
    row_total = clip_count * slot_len
    inputs = frames.reshape(row_total, model_width).astype(jnp.float32)
    out_grad = cotangent.reshape(row_total, model_width)
    normed_self = layer_norm(inputs, self_gain, self_bias).astype(jnp.bfloat16)
    projected = jnp.einsum(
        "sd,cde->cse", normed_self, self_qkv, preferred_element_type=jnp.float32
    ).astype(jnp.bfloat16)
    projected = projected.reshape(3, clip_count, slot_len, head_count, HEAD)

    def self_clip(entries):
        return attend(entries[0], entries[1], entries[2], entries[3], True, score_scale)

    self_heads, self_log = lax.map(self_clip, (projected[0], projected[1], projected[2], frame_len))
    self_flat = self_heads.reshape(row_total, local_width)
    self_out_all = lax.all_gather(self_out, "tensor")
    cross_out_all = lax.all_gather(cross_out, "tensor")
    after_self = inputs + gathered_sum(self_flat, self_out_all, "sk,kd->sd")
    normed_cross = layer_norm(after_self, cross_gain, cross_bias).astype(jnp.bfloat16)
    cross_queries = jnp.dot(normed_cross, cross_query, preferred_element_type=jnp.float32).astype(
        jnp.bfloat16
    )
    cross_queries = cross_queries.reshape(clip_count, slot_len, head_count, HEAD)
    text_proj = jnp.einsum(
        "ctd,gde->gcte", text_states, cross_keyval, preferred_element_type=jnp.float32
    ).astype(jnp.bfloat16)
    text_proj = text_proj.reshape(2, clip_count, text_count, head_count, HEAD)

    def cross_clip(entries):
        return attend(entries[0], entries[1], entries[2], entries[3], False, score_scale)

    cross_heads, cross_log = lax.map(
        cross_clip, (cross_queries, text_proj[0], text_proj[1], text_token_length)
    )
    cross_flat = cross_heads.reshape(row_total, local_width)
    after_cross = after_self + gathered_sum(cross_flat, cross_out_all, "sk,kd->sd")
    normed_feed = layer_norm(after_cross, feed_gain, feed_bias).astype(jnp.bfloat16)
    upward = jnp.dot(normed_feed, feed_up, preferred_element_type=jnp.float32)
    active = gelu_exact(upward).astype(jnp.bfloat16)
    feed_part = jnp.dot(active, feed_down, preferred_element_type=jnp.float32)
    feed_low = feed_part.astype(jnp.bfloat16)
    active_grad = jnp.einsum("sd,kd->sk", out_grad, feed_down, preferred_element_type=jnp.float32)
    _, gelu_pull = jax.vjp(gelu_exact, upward)
    upward_grad = gelu_pull(active_grad)[0].astype(jnp.bfloat16)
    downward_gradient = jnp.einsum(
        "sk,sd->kd", active, out_grad, preferred_element_type=jnp.float32
    )
    up_grad = jnp.einsum("sd,sk->dk", normed_feed, upward_grad, preferred_element_type=jnp.float32)
    feed_input_part = jnp.einsum(
        "sk,dk->sd", upward_grad, feed_up, preferred_element_type=jnp.float32
    )
    feed_back = norm_back(after_cross, feed_gain, feed_bias, relay_total(feed_input_part))
    feed_sums = [dp_sum(up_grad), dp_sum(downward_gradient)]
    cross_grad_rows = out_grad.astype(jnp.float32) + feed_back[0]
    query_weight, cross_grad_rows = lax.optimization_barrier((cross_query, cross_grad_rows))
    query_weight_pieces = relay_pieces(query_weight, "tensor")
    cross_grad_low = cross_grad_rows.astype(jnp.bfloat16)
    cout_grad = jnp.einsum(
        "sk,sd->kd", cross_flat, cross_grad_low, preferred_element_type=jnp.float32
    )
    cross_heads_grad = jnp.einsum(
        "sd,kd->sk", cross_grad_low, cross_out, preferred_element_type=jnp.float32
    ).astype(jnp.bfloat16)
    cross_heads_grad = cross_heads_grad.reshape(clip_count, slot_len, head_count, HEAD)

    def cross_clip_back(entries):
        return attend_back(
            entries[0],
            entries[1],
            entries[2],
            entries[3],
            entries[4],
            entries[5],
            False,
            score_scale,
        )

    cquery_heads, ckey_heads, cvalue_heads = lax.map(
        cross_clip_back,
        (cross_queries, text_proj[0], text_proj[1], cross_log, cross_heads_grad, text_token_length),
    )
    query_grad_low = cquery_heads.reshape(row_total, local_width).astype(jnp.bfloat16)
    feed_low, query_grad_low, query_weight_pieces = lax.optimization_barrier(
        (feed_low, query_grad_low, query_weight_pieces)
    )
    block_out = (after_cross + lax.psum(feed_low, "tensor").astype(jnp.float32)).astype(
        jnp.bfloat16
    )
    keyval_grad_low = jnp.stack((ckey_heads, cvalue_heads)).astype(jnp.bfloat16)
    keyval_grad_low = keyval_grad_low.reshape(2, clip_count, text_count, local_width)
    cquery_grad = jnp.einsum(
        "sd,se->de", normed_cross, query_grad_low, preferred_element_type=jnp.float32
    )
    ckeyval_grad = jnp.einsum(
        "ctd,gcte->gde", text_states, keyval_grad_low, preferred_element_type=jnp.float32
    )
    text_part = jnp.einsum(
        "gcte,gde->ctd", keyval_grad_low, cross_keyval, preferred_element_type=jnp.float32
    )
    cross_sum = paired_sum(query_grad_low, query_weight_pieces, "se,de->sd")
    text_grad = lax.psum(text_part.astype(jnp.bfloat16), "tensor").astype(jnp.float32)
    cross_back = norm_back(after_self, cross_gain, cross_bias, cross_sum)
    self_grad_rows = cross_grad_rows + cross_back[0]
    feed_sums, self_grad_rows = lax.optimization_barrier((feed_sums, self_grad_rows))
    self_grad_low = self_grad_rows.astype(jnp.bfloat16)
    sout_grad = jnp.einsum(
        "sk,sd->kd", self_flat, self_grad_low, preferred_element_type=jnp.float32
    )
    self_heads_grad = jnp.einsum(
        "sd,kd->sk", self_grad_low, self_out, preferred_element_type=jnp.float32
    ).astype(jnp.bfloat16)
    self_heads_grad = self_heads_grad.reshape(clip_count, slot_len, head_count, HEAD)

    def self_clip_back(entries):
        return attend_back(
            entries[0],
            entries[1],
            entries[2],
            entries[3],
            entries[4],
            entries[5],
            True,
            score_scale,
        )

    self_query_heads, self_key_heads, self_value_heads = lax.map(
        self_clip_back,
        (projected[0], projected[1], projected[2], self_log, self_heads_grad, frame_len),
    )
    projection_gradient = jnp.stack((self_query_heads, self_key_heads, self_value_heads)).astype(
        jnp.bfloat16
    )
    projection_gradient = projection_gradient.reshape(3, row_total, local_width)
    qkv_grad = jnp.einsum(
        "sd,cse->cde", normed_self, projection_gradient, preferred_element_type=jnp.float32
    )
    self_input_part = jnp.einsum(
        "cse,cde->sd", projection_gradient, self_qkv, preferred_element_type=jnp.float32
    )
    self_back = norm_back(inputs, self_gain, self_bias, relay_total(self_input_part))
    self_norm_terms = (dp_sum(self_back[1]), dp_sum(self_back[2]))
    frames_grad = self_grad_rows + self_back[0]
    gain_terms = (
        self_back[1],
        self_back[2],
        cross_back[1],
        cross_back[2],
        feed_back[1],
        feed_back[2],
    )
    late_sums = [dp_sum(term) for term in (qkv_grad, sout_grad, cquery_grad, ckeyval_grad)]
    late_sums = late_sums + stacked_psum(
        cout_grad, [cross_back[1], cross_back[2], feed_back[1], feed_back[2]], "dp"
    )
    summed = (
        self_norm_terms[0],
        self_norm_terms[1],
        late_sums[5],
        late_sums[6],
        late_sums[7],
        late_sums[8],
        late_sums[0],
        late_sums[1],
        late_sums[2],
        late_sums[3],
        late_sums[4],
        feed_sums[0],
        feed_sums[1],
    )
    return (
        block_out.reshape(clip_count, slot_len, model_width),
        frames_grad.reshape(clip_count, slot_len, model_width),
        text_grad,
        summed[0],
        summed[1],
        summed[2],
        summed[3],
        summed[4],
        summed[5],
        summed[6],
        summed[7],
        summed[8],
        summed[9],
        summed[10],
        summed[11],
        summed[12],
    )


def solution(mesh):
    return jax.shard_map(
        local,
        mesh=mesh,
        in_specs=(
            P("dp", None, None),
            P("dp", None, None),
            P("dp"),
            P("dp"),
            P(),
            P(),
            P(),
            P(),
            P(),
            P(),
            P(None, None, "tensor"),
            P("tensor", None),
            P(None, "tensor"),
            P(None, None, "tensor"),
            P("tensor", None),
            P(None, "tensor"),
            P("tensor", None),
            P("dp", None, None),
        ),
        out_specs=(
            P("dp", None, None),
            P("dp", None, None),
            P("dp", None, None),
            P(),
            P(),
            P(),
            P(),
            P(),
            P(),
            P(None, None, "tensor"),
            P("tensor", None),
            P(None, "tensor"),
            P(None, None, "tensor"),
            P("tensor", None),
            P(None, "tensor"),
            P("tensor", None),
        ),
        check_vma=False,
    )
```

```python
import jax
import jax.numpy as jnp
from jax import lax
from jax.sharding import PartitionSpec as P

HEAD = 64


EPSILON = 1e-05
MASKED = -1e30


def layer_norm(inputs, norm_gain, norm_bias):
    row_mean = jnp.mean(inputs, axis=-1, keepdims=True)
    centred = inputs - row_mean
    spread = jnp.mean(centred * centred, axis=-1, keepdims=True)
    return centred * lax.rsqrt(spread + EPSILON) * norm_gain + norm_bias


def normalized(inputs):
    row_mean = jnp.mean(inputs, axis=-1, keepdims=True)
    centred = inputs - row_mean
    spread = jnp.mean(centred * centred, axis=-1, keepdims=True)
    return centred * lax.rsqrt(spread + EPSILON)


def norm_back(inputs, norm_gain, norm_bias, upstream):
    _, pullback = jax.vjp(layer_norm, inputs, norm_gain, norm_bias)
    return pullback(upstream)


def gelu_exact(inputs):
    return jax.nn.gelu(inputs, approximate=False)


def masked_scores(portion, offset, key_rows, key_limit, causal, score_scale):
    scores = (
        jnp.einsum("bhe,khe->hbk", portion, key_rows, preferred_element_type=jnp.float32)
        * score_scale
    )
    key_pos = jnp.arange(key_rows.shape[0])
    allowed = key_pos[None, :] < key_limit
    if causal:
        allowed = allowed & (key_pos[None, :] <= offset + jnp.arange(portion.shape[0])[:, None])
    return jnp.where(allowed[None], scores, MASKED)


def attend(queries, key_rows, values, key_limit, causal, score_scale):
    row_count, head_count, head_size = queries.shape
    block_len = min(512, row_count)
    portions = queries.reshape(row_count // block_len, block_len, head_count, head_size)
    offsets = jnp.arange(row_count // block_len) * block_len

    def one_block(entries):
        portion, offset = entries
        scores = masked_scores(portion, offset, key_rows, key_limit, causal, score_scale)
        row_max = jnp.max(scores, axis=-1, keepdims=True)
        unnormed = jnp.exp(scores - row_max)
        row_sum = jnp.sum(unnormed, axis=-1, keepdims=True)
        probs_low = (unnormed / row_sum).astype(jnp.bfloat16)
        result = jnp.einsum("hbk,khe->bhe", probs_low, values, preferred_element_type=jnp.float32)
        return (result.astype(jnp.bfloat16), row_max[..., 0] + jnp.log(row_sum[..., 0]))

    if not causal:
        result, log_total = lax.map(one_block, (portions, offsets))
        return (result.reshape(row_count, head_count, head_size), log_total)
    results, totals = [], []
    for index in range(row_count // block_len):
        key_end = (index + 1) * block_len
        scores = masked_scores(
            portions[index], index * block_len, key_rows[:key_end], key_limit, causal, score_scale
        )
        row_max = jnp.max(scores, axis=-1, keepdims=True)
        unnormed = jnp.exp(scores - row_max)
        row_sum = jnp.sum(unnormed, axis=-1, keepdims=True)
        probs_low = (unnormed / row_sum).astype(jnp.bfloat16)
        result = jnp.einsum(
            "hbk,khe->bhe", probs_low, values[:key_end], preferred_element_type=jnp.float32
        )
        results.append(result.astype(jnp.bfloat16))
        totals.append(row_max[..., 0] + jnp.log(row_sum[..., 0]))
    return (jnp.concatenate(results).reshape(row_count, head_count, head_size), jnp.stack(totals))


def attend_back(queries, key_rows, values, log_total, out_grad, key_limit, causal, score_scale):
    row_count, head_count, head_size = queries.shape
    block_len = min(512, row_count)
    portions = queries.reshape(row_count // block_len, block_len, head_count, head_size)
    grad_parts = out_grad.reshape(row_count // block_len, block_len, head_count, head_size)
    offsets = jnp.arange(row_count // block_len) * block_len

    def one_block(carry, entries):
        key_grad, value_grad = carry
        portion, grad_part, log_part, offset = entries
        scores = masked_scores(portion, offset, key_rows, key_limit, causal, score_scale)
        probs = jnp.exp(scores - log_part[..., None])
        probs_grad = jnp.einsum(
            "bhe,khe->hbk", grad_part, values, preferred_element_type=jnp.float32
        )
        row_dot = jnp.sum(probs * probs_grad, axis=-1, keepdims=True)
        scores_grad = (probs * (probs_grad - row_dot)).astype(jnp.bfloat16)
        value_grad = value_grad + jnp.einsum(
            "hbk,bhe->khe",
            probs.astype(jnp.bfloat16),
            grad_part,
            preferred_element_type=jnp.float32,
        )
        key_grad = (
            key_grad
            + jnp.einsum("hbk,bhe->khe", scores_grad, portion, preferred_element_type=jnp.float32)
            * score_scale
        )
        query_grad = (
            jnp.einsum("hbk,khe->bhe", scores_grad, key_rows, preferred_element_type=jnp.float32)
            * score_scale
        )
        return ((key_grad, value_grad), query_grad)

    empty = jnp.zeros(key_rows.shape, jnp.float32)
    if not causal:
        (key_grad, value_grad), query_grad = lax.scan(
            one_block, (empty, empty), (portions, grad_parts, log_total, offsets)
        )
        return (query_grad.reshape(row_count, head_count, head_size), key_grad, value_grad)
    key_grad, value_grad, query_grads = empty, empty, []
    for index in range(row_count // block_len):
        key_end = (index + 1) * block_len
        portion, grad_part = portions[index], grad_parts[index]
        keys, vals = key_rows[:key_end], values[:key_end]
        scores = masked_scores(portion, index * block_len, keys, key_limit, causal, score_scale)
        probs = jnp.exp(scores - log_total[index][..., None])
        probs_grad = jnp.einsum("bhe,khe->hbk", grad_part, vals, preferred_element_type=jnp.float32)
        row_dot = jnp.sum(probs * probs_grad, axis=-1, keepdims=True)
        scores_grad = (probs * (probs_grad - row_dot)).astype(jnp.bfloat16)
        value_part = jnp.einsum(
            "hbk,bhe->khe", probs.astype(jnp.bfloat16), grad_part, preferred_element_type=jnp.float32
        )
        key_part = (
            jnp.einsum("hbk,bhe->khe", scores_grad, portion, preferred_element_type=jnp.float32)
            * score_scale
        )
        value_grad = value_grad.at[:key_end].add(value_part)
        key_grad = key_grad.at[:key_end].add(key_part)
        query_grads.append(
            jnp.einsum("hbk,khe->bhe", scores_grad, keys, preferred_element_type=jnp.float32)
            * score_scale
        )
    query_grad = jnp.concatenate(query_grads)
    return (query_grad.reshape(row_count, head_count, head_size), key_grad, value_grad)


def head_total(partial_value):
    return lax.psum(partial_value.astype(jnp.bfloat16), "tensor").astype(jnp.float32)


def relay_pieces(block, axis):
    count = lax.axis_size(axis)
    me = lax.axis_index(axis)
    pieces = [(block, me)]
    from_left, from_right = block, block
    for k in range(1, count):
        from_left = lax.ppermute(from_left, axis, [(i, i + 1) for i in range(k - 1, count - 1)])
        from_right = lax.ppermute(from_right, axis, [(i, i - 1) for i in range(1, count - k + 1)])
        pieces.append((from_left, me - k))
        pieces.append((from_right, me + k))
    return pieces


def relay_scatter(value, axis):
    count = lax.axis_size(axis)
    me = lax.axis_index(axis)
    shards = value.reshape((count, value.shape[0] // count) + value.shape[1:])

    def pick(index):
        return lax.dynamic_index_in_dim(shards, jnp.clip(index, 0, count - 1), 0, keepdims=False)

    to_right = to_left = None
    for k in range(1, count):
        send_right = pick(me + count - k).astype(jnp.float32)
        send_left = pick(me - (count - k)).astype(jnp.float32)
        if to_right is not None:
            send_right = send_right + to_right.astype(jnp.float32)
            send_left = send_left + to_left.astype(jnp.float32)
        to_right = lax.ppermute(
            send_right.astype(value.dtype), axis, [(i, i + 1) for i in range(min(k, count - 1))]
        )
        to_left = lax.ppermute(
            send_left.astype(value.dtype), axis, [(i, i - 1) for i in range(max(count - k, 1), count)]
        )
    total = pick(me).astype(jnp.float32)
    if to_right is not None:
        total = total + to_right.astype(jnp.float32) + to_left.astype(jnp.float32)
    return total.astype(value.dtype)


def relay_total(partial_value):
    low_value = partial_value.astype(jnp.bfloat16)
    reduced = relay_scatter(low_value, "tensor")
    pieces = relay_pieces(reduced, "tensor")
    shards = []
    for owner in range(len(pieces) // 2 + 1):
        shard = jnp.zeros_like(reduced)
        for piece, source in pieces:
            shard = jnp.where(source == owner, piece, shard)
        shards.append(shard)
    return jnp.concatenate(shards).astype(jnp.float32)


def stacked_psum(matrix, rows, axis):
    pad = (-(matrix.shape[0] + len(rows))) % 16
    extra = jnp.stack(rows + [jnp.zeros_like(rows[0])] * pad)
    summed = lax.psum(jnp.concatenate([matrix, extra]).astype(jnp.bfloat16), axis)
    summed = summed.astype(jnp.float32)
    count = matrix.shape[0]
    return [summed[:count]] + [summed[count + i] for i in range(len(rows))]


def dp_sum(term):
    return lax.psum(term.astype(jnp.bfloat16), "dp").astype(jnp.float32)


def paired_sum(block, weight_pieces, spec):
    total = None
    for (piece, _), (weight, _) in zip(relay_pieces(block, "tensor"), weight_pieces):
        partial_value = jnp.einsum(spec, piece, weight, preferred_element_type=jnp.float32)
        partial_value = partial_value.astype(jnp.bfloat16).astype(jnp.float32)
        total = partial_value if total is None else total + partial_value
        total = lax.optimization_barrier(total)
    return total


def gathered_sum(block, weights, spec):
    count = weights.shape[0]
    total = None
    for piece, source in relay_pieces(block, "tensor"):
        weight = lax.dynamic_index_in_dim(weights, jnp.clip(source, 0, count - 1), 0, keepdims=False)
        partial_value = jnp.einsum(spec, piece, weight, preferred_element_type=jnp.float32)
        partial_value = partial_value.astype(jnp.bfloat16).astype(jnp.float32)
        total = partial_value if total is None else total + partial_value
        total = lax.optimization_barrier(total)
    return total


def local(
    frames,
    text_states,
    frame_len,
    text_token_length,
    self_gain,
    self_bias,
    cross_gain,
    cross_bias,
    feed_gain,
    feed_bias,
    self_qkv,
    self_out,
    cross_query,
    cross_keyval,
    cross_out,
    feed_up,
    feed_down,
    cotangent,
):
    clip_count, slot_len, model_width = frames.shape
    text_count = text_states.shape[1]
    local_width = self_out.shape[0]
    head_count = local_width // HEAD
    score_scale = HEAD ** (-0.5)
    row_total = clip_count * slot_len
    inputs = frames.reshape(row_total, model_width).astype(jnp.float32)
    out_grad = cotangent.reshape(row_total, model_width)
    normed_self = layer_norm(inputs, self_gain, self_bias).astype(jnp.bfloat16)
    projected = jnp.einsum(
        "sd,cde->cse", normed_self, self_qkv, preferred_element_type=jnp.float32
    ).astype(jnp.bfloat16)
    projected = projected.reshape(3, clip_count, slot_len, head_count, HEAD)

    def self_clip(entries):
        return attend(entries[0], entries[1], entries[2], entries[3], True, score_scale)

    self_heads, self_log = lax.map(self_clip, (projected[0], projected[1], projected[2], frame_len))
    self_flat = self_heads.reshape(row_total, local_width)
    self_out_all = lax.all_gather(self_out, "tensor")
    cross_out_all = lax.all_gather(cross_out, "tensor")
    after_self = inputs + gathered_sum(self_flat, self_out_all, "sk,kd->sd")
    normed_cross = layer_norm(after_self, cross_gain, cross_bias).astype(jnp.bfloat16)
    cross_queries = jnp.dot(normed_cross, cross_query, preferred_element_type=jnp.float32).astype(
        jnp.bfloat16
    )
    cross_queries = cross_queries.reshape(clip_count, slot_len, head_count, HEAD)
    text_proj = jnp.einsum(
        "ctd,gde->gcte", text_states, cross_keyval, preferred_element_type=jnp.float32
    ).astype(jnp.bfloat16)
    text_proj = text_proj.reshape(2, clip_count, text_count, head_count, HEAD)

    def cross_clip(entries):
        return attend(entries[0], entries[1], entries[2], entries[3], False, score_scale)

    cross_heads, cross_log = lax.map(
        cross_clip, (cross_queries, text_proj[0], text_proj[1], text_token_length)
    )
    cross_flat = cross_heads.reshape(row_total, local_width)
    after_cross = after_self + gathered_sum(cross_flat, cross_out_all, "sk,kd->sd")
    normed_feed = layer_norm(after_cross, feed_gain, feed_bias).astype(jnp.bfloat16)
    upward = jnp.dot(normed_feed, feed_up, preferred_element_type=jnp.float32)
    active = gelu_exact(upward).astype(jnp.bfloat16)
    feed_part = jnp.dot(active, feed_down, preferred_element_type=jnp.float32)
    feed_low = feed_part.astype(jnp.bfloat16)
    active_grad = jnp.einsum("sd,kd->sk", out_grad, feed_down, preferred_element_type=jnp.float32)
    _, gelu_pull = jax.vjp(gelu_exact, upward)
    upward_grad = gelu_pull(active_grad)[0].astype(jnp.bfloat16)
    downward_gradient = jnp.einsum(
        "sk,sd->kd", active, out_grad, preferred_element_type=jnp.float32
    )
    up_grad = jnp.einsum("sd,sk->dk", normed_feed, upward_grad, preferred_element_type=jnp.float32)
    feed_input_part = jnp.einsum(
        "sk,dk->sd", upward_grad, feed_up, preferred_element_type=jnp.float32
    )
    feed_back = norm_back(after_cross, feed_gain, feed_bias, relay_total(feed_input_part))
    feed_sums = [dp_sum(up_grad), dp_sum(downward_gradient)]
    cross_grad_rows = out_grad.astype(jnp.float32) + feed_back[0]
    query_weight, cross_grad_rows = lax.optimization_barrier((cross_query, cross_grad_rows))
    query_weight_pieces = relay_pieces(query_weight, "tensor")
    cross_grad_low = cross_grad_rows.astype(jnp.bfloat16)
    cout_grad = jnp.einsum(
        "sk,sd->kd", cross_flat, cross_grad_low, preferred_element_type=jnp.float32
    )
    cross_heads_grad = jnp.einsum(
        "sd,kd->sk", cross_grad_low, cross_out, preferred_element_type=jnp.float32
    ).astype(jnp.bfloat16)
    cross_heads_grad = cross_heads_grad.reshape(clip_count, slot_len, head_count, HEAD)

    def cross_clip_back(entries):
        return attend_back(
            entries[0],
            entries[1],
            entries[2],
            entries[3],
            entries[4],
            entries[5],
            False,
            score_scale,
        )

    cquery_heads, ckey_heads, cvalue_heads = lax.map(
        cross_clip_back,
        (cross_queries, text_proj[0], text_proj[1], cross_log, cross_heads_grad, text_token_length),
    )
    query_grad_low = cquery_heads.reshape(row_total, local_width).astype(jnp.bfloat16)
    query_grad_low, query_weight_pieces = lax.optimization_barrier(
        (query_grad_low, query_weight_pieces)
    )
    keyval_grad_low = jnp.stack((ckey_heads, cvalue_heads)).astype(jnp.bfloat16)
    keyval_grad_low = keyval_grad_low.reshape(2, clip_count, text_count, local_width)
    cquery_grad = jnp.einsum(
        "sd,se->de", normed_cross, query_grad_low, preferred_element_type=jnp.float32
    )
    ckeyval_grad = jnp.einsum(
        "ctd,gcte->gde", text_states, keyval_grad_low, preferred_element_type=jnp.float32
    )
    text_part = jnp.einsum(
        "gcte,gde->ctd", keyval_grad_low, cross_keyval, preferred_element_type=jnp.float32
    )
    cross_sum = paired_sum(query_grad_low, query_weight_pieces, "se,de->sd")
    feed_low, cross_sum = lax.optimization_barrier((feed_low, cross_sum))
    block_out = (after_cross + lax.psum(feed_low, "tensor").astype(jnp.float32)).astype(
        jnp.bfloat16
    )
    text_grad = lax.psum(text_part.astype(jnp.bfloat16), "tensor").astype(jnp.float32)
    cross_back = norm_back(after_self, cross_gain, cross_bias, cross_sum)
    self_grad_rows = cross_grad_rows + cross_back[0]
    feed_sums, self_grad_rows = lax.optimization_barrier((feed_sums, self_grad_rows))
    self_grad_low = self_grad_rows.astype(jnp.bfloat16)
    sout_grad = jnp.einsum(
        "sk,sd->kd", self_flat, self_grad_low, preferred_element_type=jnp.float32
    )
    self_heads_grad = jnp.einsum(
        "sd,kd->sk", self_grad_low, self_out, preferred_element_type=jnp.float32
    ).astype(jnp.bfloat16)
    self_heads_grad = self_heads_grad.reshape(clip_count, slot_len, head_count, HEAD)

    def self_clip_back(entries):
        return attend_back(
            entries[0],
            entries[1],
            entries[2],
            entries[3],
            entries[4],
            entries[5],
            True,
            score_scale,
        )

    self_query_heads, self_key_heads, self_value_heads = lax.map(
        self_clip_back,
        (projected[0], projected[1], projected[2], self_log, self_heads_grad, frame_len),
    )
    projection_gradient = jnp.stack((self_query_heads, self_key_heads, self_value_heads)).astype(
        jnp.bfloat16
    )
    projection_gradient = projection_gradient.reshape(3, row_total, local_width)
    qkv_grad = jnp.einsum(
        "sd,cse->cde", normed_self, projection_gradient, preferred_element_type=jnp.float32
    )
    self_input_part = jnp.einsum(
        "cse,cde->sd", projection_gradient, self_qkv, preferred_element_type=jnp.float32
    )
    self_back = norm_back(inputs, self_gain, self_bias, relay_total(self_input_part))
    self_norm_terms = (dp_sum(self_back[1]), dp_sum(self_back[2]))
    frames_grad = self_grad_rows + self_back[0]
    gain_terms = (
        self_back[1],
        self_back[2],
        cross_back[1],
        cross_back[2],
        feed_back[1],
        feed_back[2],
    )
    late_sums = [dp_sum(term) for term in (qkv_grad, sout_grad, cquery_grad, ckeyval_grad)]
    late_sums = late_sums + stacked_psum(
        cout_grad, [cross_back[1], cross_back[2], feed_back[1], feed_back[2]], "dp"
    )
    summed = (
        self_norm_terms[0],
        self_norm_terms[1],
        late_sums[5],
        late_sums[6],
        late_sums[7],
        late_sums[8],
        late_sums[0],
        late_sums[1],
        late_sums[2],
        late_sums[3],
        late_sums[4],
        feed_sums[0],
        feed_sums[1],
    )
    return (
        block_out.reshape(clip_count, slot_len, model_width),
        frames_grad.reshape(clip_count, slot_len, model_width),
        text_grad,
        summed[0],
        summed[1],
        summed[2],
        summed[3],
        summed[4],
        summed[5],
        summed[6],
        summed[7],
        summed[8],
        summed[9],
        summed[10],
        summed[11],
        summed[12],
    )


def solution(mesh):
    return jax.shard_map(
        local,
        mesh=mesh,
        in_specs=(
            P("dp", None, None),
            P("dp", None, None),
            P("dp"),
            P("dp"),
            P(),
            P(),
            P(),
            P(),
            P(),
            P(),
            P(None, None, "tensor"),
            P("tensor", None),
            P(None, "tensor"),
            P(None, None, "tensor"),
            P("tensor", None),
            P(None, "tensor"),
            P("tensor", None),
            P("dp", None, None),
        ),
        out_specs=(
            P("dp", None, None),
            P("dp", None, None),
            P("dp", None, None),
            P(),
            P(),
            P(),
            P(),
            P(),
            P(),
            P(None, None, "tensor"),
            P("tensor", None),
            P(None, "tensor"),
            P(None, None, "tensor"),
            P("tensor", None),
            P(None, "tensor"),
            P("tensor", None),
        ),
        check_vma=False,
    )
```

```python
import jax
import jax.numpy as jnp
from jax import lax
from jax.sharding import PartitionSpec as P

HEAD = 64


EPSILON = 1e-05
MASKED = -1e30


def layer_norm(inputs, norm_gain, norm_bias):
    row_mean = jnp.mean(inputs, axis=-1, keepdims=True)
    centred = inputs - row_mean
    spread = jnp.mean(centred * centred, axis=-1, keepdims=True)
    return centred * lax.rsqrt(spread + EPSILON) * norm_gain + norm_bias


def normalized(inputs):
    row_mean = jnp.mean(inputs, axis=-1, keepdims=True)
    centred = inputs - row_mean
    spread = jnp.mean(centred * centred, axis=-1, keepdims=True)
    return centred * lax.rsqrt(spread + EPSILON)


def norm_back(inputs, norm_gain, norm_bias, upstream):
    _, pullback = jax.vjp(layer_norm, inputs, norm_gain, norm_bias)
    return pullback(upstream)


def gelu_exact(inputs):
    return jax.nn.gelu(inputs, approximate=False)


def masked_scores(portion, offset, key_rows, key_limit, causal, score_scale):
    scores = (
        jnp.einsum("bhe,khe->hbk", portion, key_rows, preferred_element_type=jnp.float32)
        * score_scale
    )
    key_pos = jnp.arange(key_rows.shape[0])
    allowed = key_pos[None, :] < key_limit
    if causal:
        allowed = allowed & (key_pos[None, :] <= offset + jnp.arange(portion.shape[0])[:, None])
    return jnp.where(allowed[None], scores, MASKED)


def attend(queries, key_rows, values, key_limit, causal, score_scale):
    row_count, head_count, head_size = queries.shape
    block_len = min(512, row_count)
    portions = queries.reshape(row_count // block_len, block_len, head_count, head_size)
    offsets = jnp.arange(row_count // block_len) * block_len

    def one_block(entries):
        portion, offset = entries
        scores = masked_scores(portion, offset, key_rows, key_limit, causal, score_scale)
        row_max = jnp.max(scores, axis=-1, keepdims=True)
        unnormed = jnp.exp(scores - row_max)
        row_sum = jnp.sum(unnormed, axis=-1, keepdims=True)
        probs_low = (unnormed / row_sum).astype(jnp.bfloat16)
        result = jnp.einsum("hbk,khe->bhe", probs_low, values, preferred_element_type=jnp.float32)
        return (result.astype(jnp.bfloat16), row_max[..., 0] + jnp.log(row_sum[..., 0]))

    if not causal:
        result, log_total = lax.map(one_block, (portions, offsets))
        return (result.reshape(row_count, head_count, head_size), log_total)
    results, totals = [], []
    for index in range(row_count // block_len):
        key_end = (index + 1) * block_len
        scores = masked_scores(
            portions[index], index * block_len, key_rows[:key_end], key_limit, causal, score_scale
        )
        row_max = jnp.max(scores, axis=-1, keepdims=True)
        unnormed = jnp.exp(scores - row_max)
        row_sum = jnp.sum(unnormed, axis=-1, keepdims=True)
        probs_low = (unnormed / row_sum).astype(jnp.bfloat16)
        result = jnp.einsum(
            "hbk,khe->bhe", probs_low, values[:key_end], preferred_element_type=jnp.float32
        )
        results.append(result.astype(jnp.bfloat16))
        totals.append(row_max[..., 0] + jnp.log(row_sum[..., 0]))
    return (jnp.concatenate(results).reshape(row_count, head_count, head_size), jnp.stack(totals))


def attend_back(queries, key_rows, values, log_total, out_grad, key_limit, causal, score_scale):
    row_count, head_count, head_size = queries.shape
    block_len = min(512, row_count)
    portions = queries.reshape(row_count // block_len, block_len, head_count, head_size)
    grad_parts = out_grad.reshape(row_count // block_len, block_len, head_count, head_size)
    offsets = jnp.arange(row_count // block_len) * block_len

    def one_block(carry, entries):
        key_grad, value_grad = carry
        portion, grad_part, log_part, offset = entries
        scores = masked_scores(portion, offset, key_rows, key_limit, causal, score_scale)
        probs = jnp.exp(scores - log_part[..., None])
        probs_grad = jnp.einsum(
            "bhe,khe->hbk", grad_part, values, preferred_element_type=jnp.float32
        )
        row_dot = jnp.sum(probs * probs_grad, axis=-1, keepdims=True)
        scores_grad = (probs * (probs_grad - row_dot)).astype(jnp.bfloat16)
        value_grad = value_grad + jnp.einsum(
            "hbk,bhe->khe",
            probs.astype(jnp.bfloat16),
            grad_part,
            preferred_element_type=jnp.float32,
        )
        key_grad = (
            key_grad
            + jnp.einsum("hbk,bhe->khe", scores_grad, portion, preferred_element_type=jnp.float32)
            * score_scale
        )
        query_grad = (
            jnp.einsum("hbk,khe->bhe", scores_grad, key_rows, preferred_element_type=jnp.float32)
            * score_scale
        )
        return ((key_grad, value_grad), query_grad)

    empty = jnp.zeros(key_rows.shape, jnp.float32)
    if not causal:
        (key_grad, value_grad), query_grad = lax.scan(
            one_block, (empty, empty), (portions, grad_parts, log_total, offsets)
        )
        return (query_grad.reshape(row_count, head_count, head_size), key_grad, value_grad)
    key_grad, value_grad, query_grads = empty, empty, []
    for index in range(row_count // block_len):
        key_end = (index + 1) * block_len
        portion, grad_part = portions[index], grad_parts[index]
        keys, vals = key_rows[:key_end], values[:key_end]
        scores = masked_scores(portion, index * block_len, keys, key_limit, causal, score_scale)
        probs = jnp.exp(scores - log_total[index][..., None])
        probs_grad = jnp.einsum("bhe,khe->hbk", grad_part, vals, preferred_element_type=jnp.float32)
        row_dot = jnp.sum(probs * probs_grad, axis=-1, keepdims=True)
        scores_grad = (probs * (probs_grad - row_dot)).astype(jnp.bfloat16)
        value_part = jnp.einsum(
            "hbk,bhe->khe", probs.astype(jnp.bfloat16), grad_part, preferred_element_type=jnp.float32
        )
        key_part = (
            jnp.einsum("hbk,bhe->khe", scores_grad, portion, preferred_element_type=jnp.float32)
            * score_scale
        )
        value_grad = value_grad.at[:key_end].add(value_part)
        key_grad = key_grad.at[:key_end].add(key_part)
        query_grads.append(
            jnp.einsum("hbk,khe->bhe", scores_grad, keys, preferred_element_type=jnp.float32)
            * score_scale
        )
    query_grad = jnp.concatenate(query_grads)
    return (query_grad.reshape(row_count, head_count, head_size), key_grad, value_grad)


def head_total(partial_value):
    return lax.psum(partial_value.astype(jnp.bfloat16), "tensor").astype(jnp.float32)


def relay_pieces(block, axis):
    count = lax.axis_size(axis)
    me = lax.axis_index(axis)
    pieces = [(block, me)]
    from_left, from_right = block, block
    for k in range(1, count):
        from_left = lax.ppermute(from_left, axis, [(i, i + 1) for i in range(k - 1, count - 1)])
        from_right = lax.ppermute(from_right, axis, [(i, i - 1) for i in range(1, count - k + 1)])
        pieces.append((from_left, me - k))
        pieces.append((from_right, me + k))
    return pieces


def relay_scatter(value, axis):
    count = lax.axis_size(axis)
    me = lax.axis_index(axis)
    shards = value.reshape((count, value.shape[0] // count) + value.shape[1:])

    def pick(index):
        return lax.dynamic_index_in_dim(shards, jnp.clip(index, 0, count - 1), 0, keepdims=False)

    to_right = to_left = None
    for k in range(1, count):
        send_right = pick(me + count - k).astype(jnp.float32)
        send_left = pick(me - (count - k)).astype(jnp.float32)
        if to_right is not None:
            send_right = send_right + to_right.astype(jnp.float32)
            send_left = send_left + to_left.astype(jnp.float32)
        to_right = lax.ppermute(
            send_right.astype(value.dtype), axis, [(i, i + 1) for i in range(min(k, count - 1))]
        )
        to_left = lax.ppermute(
            send_left.astype(value.dtype), axis, [(i, i - 1) for i in range(max(count - k, 1), count)]
        )
    total = pick(me).astype(jnp.float32)
    if to_right is not None:
        total = total + to_right.astype(jnp.float32) + to_left.astype(jnp.float32)
    return total.astype(value.dtype)


def _rotate(value, axis, count, step):
    return lax.ppermute(value, axis, [(i, (i + step) % count) for i in range(count)])


def direct_total(partial_value):
    count = lax.axis_size("tensor")
    me = lax.axis_index("tensor")
    low_value = partial_value.astype(jnp.bfloat16)
    shards = low_value.reshape((count, low_value.shape[0] // count) + low_value.shape[1:])
    reduced = lax.dynamic_index_in_dim(shards, me, 0, keepdims=False).astype(jnp.float32)
    for step in range(1, count):
        sent = lax.dynamic_index_in_dim(shards, (me + step) % count, 0, keepdims=False)
        reduced = reduced + _rotate(sent, "tensor", count, step).astype(jnp.float32)
    reduced = reduced.astype(jnp.bfloat16)
    pieces = [(reduced, me)] + [
        (_rotate(reduced, "tensor", count, step), (me - step) % count) for step in range(1, count)
    ]
    rows = []
    for owner in range(count):
        shard = jnp.zeros_like(reduced)
        for piece, source in pieces:
            shard = jnp.where(source == owner, piece, shard)
        rows.append(shard)
    return jnp.concatenate(rows).astype(jnp.float32)


def relay_total(partial_value):
    low_value = partial_value.astype(jnp.bfloat16)
    reduced = relay_scatter(low_value, "tensor")
    pieces = relay_pieces(reduced, "tensor")
    shards = []
    for owner in range(len(pieces) // 2 + 1):
        shard = jnp.zeros_like(reduced)
        for piece, source in pieces:
            shard = jnp.where(source == owner, piece, shard)
        shards.append(shard)
    return jnp.concatenate(shards).astype(jnp.float32)


def stacked_psum(matrix, rows, axis):
    pad = (-(matrix.shape[0] + len(rows))) % 16
    extra = jnp.stack(rows + [jnp.zeros_like(rows[0])] * pad)
    summed = lax.psum(jnp.concatenate([matrix, extra]).astype(jnp.bfloat16), axis)
    summed = summed.astype(jnp.float32)
    count = matrix.shape[0]
    return [summed[:count]] + [summed[count + i] for i in range(len(rows))]


def dp_sum(term):
    return lax.psum(term.astype(jnp.bfloat16), "dp").astype(jnp.float32)


def gathered_sum(block, weights, spec):
    count = weights.shape[0]
    total = None
    for piece, source in relay_pieces(block, "tensor"):
        weight = lax.dynamic_index_in_dim(weights, jnp.clip(source, 0, count - 1), 0, keepdims=False)
        partial_value = jnp.einsum(spec, piece, weight, preferred_element_type=jnp.float32)
        partial_value = partial_value.astype(jnp.bfloat16).astype(jnp.float32)
        total = partial_value if total is None else total + partial_value
        total = lax.optimization_barrier(total)
    return total


def local(
    frames,
    text_states,
    frame_len,
    text_token_length,
    self_gain,
    self_bias,
    cross_gain,
    cross_bias,
    feed_gain,
    feed_bias,
    self_qkv,
    self_out,
    cross_query,
    cross_keyval,
    cross_out,
    feed_up,
    feed_down,
    cotangent,
):
    clip_count, slot_len, model_width = frames.shape
    text_count = text_states.shape[1]
    local_width = self_out.shape[0]
    head_count = local_width // HEAD
    score_scale = HEAD ** (-0.5)
    row_total = clip_count * slot_len
    inputs = frames.reshape(row_total, model_width).astype(jnp.float32)
    out_grad = cotangent.reshape(row_total, model_width)
    normed_self = layer_norm(inputs, self_gain, self_bias).astype(jnp.bfloat16)
    projected = jnp.einsum(
        "sd,cde->cse", normed_self, self_qkv, preferred_element_type=jnp.float32
    ).astype(jnp.bfloat16)
    projected = projected.reshape(3, clip_count, slot_len, head_count, HEAD)

    def self_clip(entries):
        return attend(entries[0], entries[1], entries[2], entries[3], True, score_scale)

    self_heads, self_log = lax.map(self_clip, (projected[0], projected[1], projected[2], frame_len))
    self_flat = self_heads.reshape(row_total, local_width)
    self_out_all = lax.all_gather(self_out, "tensor")
    cross_out_all = lax.all_gather(cross_out, "tensor")
    cross_query_all = lax.all_gather(cross_query, "tensor")
    after_self = inputs + gathered_sum(self_flat, self_out_all, "sk,kd->sd")
    normed_cross = layer_norm(after_self, cross_gain, cross_bias).astype(jnp.bfloat16)
    cross_queries = jnp.dot(normed_cross, cross_query, preferred_element_type=jnp.float32).astype(
        jnp.bfloat16
    )
    cross_queries = cross_queries.reshape(clip_count, slot_len, head_count, HEAD)
    text_proj = jnp.einsum(
        "ctd,gde->gcte", text_states, cross_keyval, preferred_element_type=jnp.float32
    ).astype(jnp.bfloat16)
    text_proj = text_proj.reshape(2, clip_count, text_count, head_count, HEAD)

    def cross_clip(entries):
        return attend(entries[0], entries[1], entries[2], entries[3], False, score_scale)

    cross_heads, cross_log = lax.map(
        cross_clip, (cross_queries, text_proj[0], text_proj[1], text_token_length)
    )
    cross_flat = cross_heads.reshape(row_total, local_width)
    after_cross = after_self + gathered_sum(cross_flat, cross_out_all, "sk,kd->sd")
    normed_feed = layer_norm(after_cross, feed_gain, feed_bias).astype(jnp.bfloat16)
    upward = jnp.dot(normed_feed, feed_up, preferred_element_type=jnp.float32)
    active = gelu_exact(upward).astype(jnp.bfloat16)
    feed_part = jnp.dot(active, feed_down, preferred_element_type=jnp.float32)
    feed_low = feed_part.astype(jnp.bfloat16)
    active_grad = jnp.einsum("sd,kd->sk", out_grad, feed_down, preferred_element_type=jnp.float32)
    _, gelu_pull = jax.vjp(gelu_exact, upward)
    upward_grad = gelu_pull(active_grad)[0].astype(jnp.bfloat16)
    downward_gradient = jnp.einsum(
        "sk,sd->kd", active, out_grad, preferred_element_type=jnp.float32
    )
    up_grad = jnp.einsum("sd,sk->dk", normed_feed, upward_grad, preferred_element_type=jnp.float32)
    feed_input_part = jnp.einsum(
        "sk,dk->sd", upward_grad, feed_up, preferred_element_type=jnp.float32
    )
    feed_back = norm_back(after_cross, feed_gain, feed_bias, direct_total(feed_input_part))
    feed_sums = [dp_sum(up_grad), dp_sum(downward_gradient)]
    cross_grad_rows = out_grad.astype(jnp.float32) + feed_back[0]
    cross_grad_low = cross_grad_rows.astype(jnp.bfloat16)
    cout_grad = jnp.einsum(
        "sk,sd->kd", cross_flat, cross_grad_low, preferred_element_type=jnp.float32
    )
    cross_heads_grad = jnp.einsum(
        "sd,kd->sk", cross_grad_low, cross_out, preferred_element_type=jnp.float32
    ).astype(jnp.bfloat16)
    cross_heads_grad = cross_heads_grad.reshape(clip_count, slot_len, head_count, HEAD)

    def cross_clip_back(entries):
        return attend_back(
            entries[0],
            entries[1],
            entries[2],
            entries[3],
            entries[4],
            entries[5],
            False,
            score_scale,
        )

    cquery_heads, ckey_heads, cvalue_heads = lax.map(
        cross_clip_back,
        (cross_queries, text_proj[0], text_proj[1], cross_log, cross_heads_grad, text_token_length),
    )
    query_grad_low = cquery_heads.reshape(row_total, local_width).astype(jnp.bfloat16)
    feed_low, query_grad_low = lax.optimization_barrier((feed_low, query_grad_low))
    block_out = (after_cross + lax.psum(feed_low, "tensor").astype(jnp.float32)).astype(
        jnp.bfloat16
    )
    keyval_grad_low = jnp.stack((ckey_heads, cvalue_heads)).astype(jnp.bfloat16)
    keyval_grad_low = keyval_grad_low.reshape(2, clip_count, text_count, local_width)
    cquery_grad = jnp.einsum(
        "sd,se->de", normed_cross, query_grad_low, preferred_element_type=jnp.float32
    )
    ckeyval_grad = jnp.einsum(
        "ctd,gcte->gde", text_states, keyval_grad_low, preferred_element_type=jnp.float32
    )
    text_part = jnp.einsum(
        "gcte,gde->ctd", keyval_grad_low, cross_keyval, preferred_element_type=jnp.float32
    )
    cross_sum = gathered_sum(query_grad_low, cross_query_all, "se,de->sd")
    text_grad = lax.psum(text_part.astype(jnp.bfloat16), "tensor").astype(jnp.float32)
    cross_back = norm_back(after_self, cross_gain, cross_bias, cross_sum)
    self_grad_rows = cross_grad_rows + cross_back[0]
    feed_sums, self_grad_rows = lax.optimization_barrier((feed_sums, self_grad_rows))
    self_grad_low = self_grad_rows.astype(jnp.bfloat16)
    sout_grad = jnp.einsum(
        "sk,sd->kd", self_flat, self_grad_low, preferred_element_type=jnp.float32
    )
    self_heads_grad = jnp.einsum(
        "sd,kd->sk", self_grad_low, self_out, preferred_element_type=jnp.float32
    ).astype(jnp.bfloat16)
    self_heads_grad = self_heads_grad.reshape(clip_count, slot_len, head_count, HEAD)

    def self_clip_back(entries):
        return attend_back(
            entries[0],
            entries[1],
            entries[2],
            entries[3],
            entries[4],
            entries[5],
            True,
            score_scale,
        )

    self_query_heads, self_key_heads, self_value_heads = lax.map(
        self_clip_back,
        (projected[0], projected[1], projected[2], self_log, self_heads_grad, frame_len),
    )
    projection_gradient = jnp.stack((self_query_heads, self_key_heads, self_value_heads)).astype(
        jnp.bfloat16
    )
    projection_gradient = projection_gradient.reshape(3, row_total, local_width)
    qkv_grad = jnp.einsum(
        "sd,cse->cde", normed_self, projection_gradient, preferred_element_type=jnp.float32
    )
    self_input_part = jnp.einsum(
        "cse,cde->sd", projection_gradient, self_qkv, preferred_element_type=jnp.float32
    )
    self_back = norm_back(inputs, self_gain, self_bias, direct_total(self_input_part))
    self_norm_terms = (dp_sum(self_back[1]), dp_sum(self_back[2]))
    frames_grad = self_grad_rows + self_back[0]
    gain_terms = (
        self_back[1],
        self_back[2],
        cross_back[1],
        cross_back[2],
        feed_back[1],
        feed_back[2],
    )
    late_sums = [dp_sum(term) for term in (qkv_grad, sout_grad, cquery_grad, ckeyval_grad)]
    late_sums = late_sums + stacked_psum(
        cout_grad, [cross_back[1], cross_back[2], feed_back[1], feed_back[2]], "dp"
    )
    summed = (
        self_norm_terms[0],
        self_norm_terms[1],
        late_sums[5],
        late_sums[6],
        late_sums[7],
        late_sums[8],
        late_sums[0],
        late_sums[1],
        late_sums[2],
        late_sums[3],
        late_sums[4],
        feed_sums[0],
        feed_sums[1],
    )
    return (
        block_out.reshape(clip_count, slot_len, model_width),
        frames_grad.reshape(clip_count, slot_len, model_width),
        text_grad,
        summed[0],
        summed[1],
        summed[2],
        summed[3],
        summed[4],
        summed[5],
        summed[6],
        summed[7],
        summed[8],
        summed[9],
        summed[10],
        summed[11],
        summed[12],
    )


def solution(mesh):
    return jax.shard_map(
        local,
        mesh=mesh,
        in_specs=(
            P("dp", None, None),
            P("dp", None, None),
            P("dp"),
            P("dp"),
            P(),
            P(),
            P(),
            P(),
            P(),
            P(),
            P(None, None, "tensor"),
            P("tensor", None),
            P(None, "tensor"),
            P(None, None, "tensor"),
            P("tensor", None),
            P(None, "tensor"),
            P("tensor", None),
            P("dp", None, None),
        ),
        out_specs=(
            P("dp", None, None),
            P("dp", None, None),
            P("dp", None, None),
            P(),
            P(),
            P(),
            P(),
            P(),
            P(),
            P(None, None, "tensor"),
            P("tensor", None),
            P(None, "tensor"),
            P(None, None, "tensor"),
            P("tensor", None),
            P(None, "tensor"),
            P("tensor", None),
        ),
        check_vma=False,
    )
```

```python
import jax
import jax.numpy as jnp
from jax import lax
from jax.sharding import PartitionSpec as P

HEAD = 64


EPSILON = 1e-05
MASKED = -1e30


def layer_norm(inputs, norm_gain, norm_bias):
    row_mean = jnp.mean(inputs, axis=-1, keepdims=True)
    centred = inputs - row_mean
    spread = jnp.mean(centred * centred, axis=-1, keepdims=True)
    return centred * lax.rsqrt(spread + EPSILON) * norm_gain + norm_bias


def normalized(inputs):
    row_mean = jnp.mean(inputs, axis=-1, keepdims=True)
    centred = inputs - row_mean
    spread = jnp.mean(centred * centred, axis=-1, keepdims=True)
    return centred * lax.rsqrt(spread + EPSILON)


def norm_back(inputs, norm_gain, norm_bias, upstream):
    _, pullback = jax.vjp(layer_norm, inputs, norm_gain, norm_bias)
    return pullback(upstream)


def gelu_exact(inputs):
    return jax.nn.gelu(inputs, approximate=False)


def masked_scores(portion, offset, key_rows, key_limit, causal, score_scale):
    scores = (
        jnp.einsum("bhe,khe->hbk", portion, key_rows, preferred_element_type=jnp.float32)
        * score_scale
    )
    key_pos = jnp.arange(key_rows.shape[0])
    allowed = key_pos[None, :] < key_limit
    if causal:
        allowed = allowed & (key_pos[None, :] <= offset + jnp.arange(portion.shape[0])[:, None])
    return jnp.where(allowed[None], scores, MASKED)


def attend(queries, key_rows, values, key_limit, causal, score_scale):
    row_count, head_count, head_size = queries.shape
    block_len = min(512, row_count)
    portions = queries.reshape(row_count // block_len, block_len, head_count, head_size)
    offsets = jnp.arange(row_count // block_len) * block_len

    def one_block(entries):
        portion, offset = entries
        scores = masked_scores(portion, offset, key_rows, key_limit, causal, score_scale)
        row_max = jnp.max(scores, axis=-1, keepdims=True)
        unnormed = jnp.exp(scores - row_max)
        row_sum = jnp.sum(unnormed, axis=-1, keepdims=True)
        probs_low = (unnormed / row_sum).astype(jnp.bfloat16)
        result = jnp.einsum("hbk,khe->bhe", probs_low, values, preferred_element_type=jnp.float32)
        return (result.astype(jnp.bfloat16), row_max[..., 0] + jnp.log(row_sum[..., 0]))

    if not causal:
        result, log_total = lax.map(one_block, (portions, offsets))
        return (result.reshape(row_count, head_count, head_size), log_total)
    results, totals = [], []
    for index in range(row_count // block_len):
        key_end = (index + 1) * block_len
        scores = masked_scores(
            portions[index], index * block_len, key_rows[:key_end], key_limit, causal, score_scale
        )
        row_max = jnp.max(scores, axis=-1, keepdims=True)
        unnormed = jnp.exp(scores - row_max)
        row_sum = jnp.sum(unnormed, axis=-1, keepdims=True)
        probs_low = (unnormed / row_sum).astype(jnp.bfloat16)
        result = jnp.einsum(
            "hbk,khe->bhe", probs_low, values[:key_end], preferred_element_type=jnp.float32
        )
        results.append(result.astype(jnp.bfloat16))
        totals.append(row_max[..., 0] + jnp.log(row_sum[..., 0]))
    return (jnp.concatenate(results).reshape(row_count, head_count, head_size), jnp.stack(totals))


def attend_back(queries, key_rows, values, log_total, out_grad, key_limit, causal, score_scale):
    row_count, head_count, head_size = queries.shape
    block_len = min(512, row_count)
    portions = queries.reshape(row_count // block_len, block_len, head_count, head_size)
    grad_parts = out_grad.reshape(row_count // block_len, block_len, head_count, head_size)
    offsets = jnp.arange(row_count // block_len) * block_len

    def one_block(carry, entries):
        key_grad, value_grad = carry
        portion, grad_part, log_part, offset = entries
        scores = masked_scores(portion, offset, key_rows, key_limit, causal, score_scale)
        probs = jnp.exp(scores - log_part[..., None])
        probs_grad = jnp.einsum(
            "bhe,khe->hbk", grad_part, values, preferred_element_type=jnp.float32
        )
        row_dot = jnp.sum(probs * probs_grad, axis=-1, keepdims=True)
        scores_grad = (probs * (probs_grad - row_dot)).astype(jnp.bfloat16)
        value_grad = value_grad + jnp.einsum(
            "hbk,bhe->khe",
            probs.astype(jnp.bfloat16),
            grad_part,
            preferred_element_type=jnp.float32,
        )
        key_grad = (
            key_grad
            + jnp.einsum("hbk,bhe->khe", scores_grad, portion, preferred_element_type=jnp.float32)
            * score_scale
        )
        query_grad = (
            jnp.einsum("hbk,khe->bhe", scores_grad, key_rows, preferred_element_type=jnp.float32)
            * score_scale
        )
        return ((key_grad, value_grad), query_grad)

    empty = jnp.zeros(key_rows.shape, jnp.float32)
    if not causal:
        (key_grad, value_grad), query_grad = lax.scan(
            one_block, (empty, empty), (portions, grad_parts, log_total, offsets)
        )
        return (query_grad.reshape(row_count, head_count, head_size), key_grad, value_grad)
    key_grad, value_grad, query_grads = empty, empty, []
    for index in range(row_count // block_len):
        key_end = (index + 1) * block_len
        portion, grad_part = portions[index], grad_parts[index]
        keys, vals = key_rows[:key_end], values[:key_end]
        scores = masked_scores(portion, index * block_len, keys, key_limit, causal, score_scale)
        probs = jnp.exp(scores - log_total[index][..., None])
        probs_grad = jnp.einsum("bhe,khe->hbk", grad_part, vals, preferred_element_type=jnp.float32)
        row_dot = jnp.sum(probs * probs_grad, axis=-1, keepdims=True)
        scores_grad = (probs * (probs_grad - row_dot)).astype(jnp.bfloat16)
        value_part = jnp.einsum(
            "hbk,bhe->khe", probs.astype(jnp.bfloat16), grad_part, preferred_element_type=jnp.float32
        )
        key_part = (
            jnp.einsum("hbk,bhe->khe", scores_grad, portion, preferred_element_type=jnp.float32)
            * score_scale
        )
        value_grad = value_grad.at[:key_end].add(value_part)
        key_grad = key_grad.at[:key_end].add(key_part)
        query_grads.append(
            jnp.einsum("hbk,khe->bhe", scores_grad, keys, preferred_element_type=jnp.float32)
            * score_scale
        )
    query_grad = jnp.concatenate(query_grads)
    return (query_grad.reshape(row_count, head_count, head_size), key_grad, value_grad)


def head_total(partial_value):
    return lax.psum(partial_value.astype(jnp.bfloat16), "tensor").astype(jnp.float32)


def relay_pieces(block, axis):
    count = lax.axis_size(axis)
    me = lax.axis_index(axis)
    pieces = [(block, me)]
    from_left, from_right = block, block
    for k in range(1, count):
        from_left = lax.ppermute(from_left, axis, [(i, i + 1) for i in range(k - 1, count - 1)])
        from_right = lax.ppermute(from_right, axis, [(i, i - 1) for i in range(1, count - k + 1)])
        pieces.append((from_left, me - k))
        pieces.append((from_right, me + k))
    return pieces


def relay_scatter(value, axis):
    count = lax.axis_size(axis)
    me = lax.axis_index(axis)
    shards = value.reshape((count, value.shape[0] // count) + value.shape[1:])

    def pick(index):
        return lax.dynamic_index_in_dim(shards, jnp.clip(index, 0, count - 1), 0, keepdims=False)

    to_right = to_left = None
    for k in range(1, count):
        send_right = pick(me + count - k).astype(jnp.float32)
        send_left = pick(me - (count - k)).astype(jnp.float32)
        if to_right is not None:
            send_right = send_right + to_right.astype(jnp.float32)
            send_left = send_left + to_left.astype(jnp.float32)
        to_right = lax.ppermute(
            send_right.astype(value.dtype), axis, [(i, i + 1) for i in range(min(k, count - 1))]
        )
        to_left = lax.ppermute(
            send_left.astype(value.dtype), axis, [(i, i - 1) for i in range(max(count - k, 1), count)]
        )
    total = pick(me).astype(jnp.float32)
    if to_right is not None:
        total = total + to_right.astype(jnp.float32) + to_left.astype(jnp.float32)
    return total.astype(value.dtype)


def _rotate(value, axis, count, step):
    return lax.ppermute(value, axis, [(i, (i + step) % count) for i in range(count)])


def direct_total(partial_value):
    count = lax.axis_size("tensor")
    me = lax.axis_index("tensor")
    low_value = partial_value.astype(jnp.bfloat16)
    shards = low_value.reshape((count, low_value.shape[0] // count) + low_value.shape[1:])
    reduced = lax.dynamic_index_in_dim(shards, me, 0, keepdims=False).astype(jnp.float32)
    for step in range(1, count):
        sent = lax.dynamic_index_in_dim(shards, (me + step) % count, 0, keepdims=False)
        reduced = reduced + _rotate(sent, "tensor", count, step).astype(jnp.float32)
    reduced = reduced.astype(jnp.bfloat16)
    pieces = [(reduced, me)] + [
        (_rotate(reduced, "tensor", count, step), (me - step) % count) for step in range(1, count)
    ]
    rows = []
    for owner in range(count):
        shard = jnp.zeros_like(reduced)
        for piece, source in pieces:
            shard = jnp.where(source == owner, piece, shard)
        rows.append(shard)
    return jnp.concatenate(rows).astype(jnp.float32)


def relay_total(partial_value):
    low_value = partial_value.astype(jnp.bfloat16)
    reduced = relay_scatter(low_value, "tensor")
    pieces = relay_pieces(reduced, "tensor")
    shards = []
    for owner in range(len(pieces) // 2 + 1):
        shard = jnp.zeros_like(reduced)
        for piece, source in pieces:
            shard = jnp.where(source == owner, piece, shard)
        shards.append(shard)
    return jnp.concatenate(shards).astype(jnp.float32)


def stacked_psum(matrix, rows, axis):
    pad = (-(matrix.shape[0] + len(rows))) % 16
    extra = jnp.stack(rows + [jnp.zeros_like(rows[0])] * pad)
    summed = lax.psum(jnp.concatenate([matrix, extra]).astype(jnp.bfloat16), axis)
    summed = summed.astype(jnp.float32)
    count = matrix.shape[0]
    return [summed[:count]] + [summed[count + i] for i in range(len(rows))]


def dp_sum(term):
    return lax.psum(term.astype(jnp.bfloat16), "dp").astype(jnp.float32)


def gathered_sum(block, weights, spec):
    count = weights.shape[0]
    total = None
    for piece, source in relay_pieces(block, "tensor"):
        weight = lax.dynamic_index_in_dim(weights, jnp.clip(source, 0, count - 1), 0, keepdims=False)
        partial_value = jnp.einsum(spec, piece, weight, preferred_element_type=jnp.float32)
        partial_value = partial_value.astype(jnp.bfloat16).astype(jnp.float32)
        total = partial_value if total is None else total + partial_value
        total = lax.optimization_barrier(total)
    return total


def local(
    frames,
    text_states,
    frame_len,
    text_token_length,
    self_gain,
    self_bias,
    cross_gain,
    cross_bias,
    feed_gain,
    feed_bias,
    self_qkv,
    self_out,
    cross_query,
    cross_keyval,
    cross_out,
    feed_up,
    feed_down,
    cotangent,
):
    clip_count, slot_len, model_width = frames.shape
    text_count = text_states.shape[1]
    local_width = self_out.shape[0]
    head_count = local_width // HEAD
    score_scale = HEAD ** (-0.5)
    row_total = clip_count * slot_len
    inputs = frames.reshape(row_total, model_width).astype(jnp.float32)
    out_grad = cotangent.reshape(row_total, model_width)
    normed_self = layer_norm(inputs, self_gain, self_bias).astype(jnp.bfloat16)
    projected = jnp.einsum(
        "sd,cde->cse", normed_self, self_qkv, preferred_element_type=jnp.float32
    ).astype(jnp.bfloat16)
    projected = projected.reshape(3, clip_count, slot_len, head_count, HEAD)

    def self_clip(entries):
        return attend(entries[0], entries[1], entries[2], entries[3], True, score_scale)

    self_heads, self_log = lax.map(self_clip, (projected[0], projected[1], projected[2], frame_len))
    self_flat = self_heads.reshape(row_total, local_width)
    self_out_all = lax.all_gather(self_out, "tensor")
    cross_out_all = lax.all_gather(cross_out, "tensor")
    cross_query_all = lax.all_gather(cross_query, "tensor")
    after_self = inputs + gathered_sum(self_flat, self_out_all, "sk,kd->sd")
    normed_cross = layer_norm(after_self, cross_gain, cross_bias).astype(jnp.bfloat16)
    cross_queries = jnp.dot(normed_cross, cross_query, preferred_element_type=jnp.float32).astype(
        jnp.bfloat16
    )
    cross_queries = cross_queries.reshape(clip_count, slot_len, head_count, HEAD)
    text_proj = jnp.einsum(
        "ctd,gde->gcte", text_states, cross_keyval, preferred_element_type=jnp.float32
    ).astype(jnp.bfloat16)
    text_proj = text_proj.reshape(2, clip_count, text_count, head_count, HEAD)

    def cross_clip(entries):
        return attend(entries[0], entries[1], entries[2], entries[3], False, score_scale)

    cross_heads, cross_log = lax.map(
        cross_clip, (cross_queries, text_proj[0], text_proj[1], text_token_length)
    )
    cross_flat = cross_heads.reshape(row_total, local_width)
    after_cross = after_self + gathered_sum(cross_flat, cross_out_all, "sk,kd->sd")
    normed_feed = layer_norm(after_cross, feed_gain, feed_bias).astype(jnp.bfloat16)
    upward = jnp.dot(normed_feed, feed_up, preferred_element_type=jnp.float32)
    active = gelu_exact(upward).astype(jnp.bfloat16)
    feed_part = jnp.dot(active, feed_down, preferred_element_type=jnp.float32)
    feed_low = feed_part.astype(jnp.bfloat16)
    active_grad = jnp.einsum("sd,kd->sk", out_grad, feed_down, preferred_element_type=jnp.float32)
    _, gelu_pull = jax.vjp(gelu_exact, upward)
    upward_grad = gelu_pull(active_grad)[0].astype(jnp.bfloat16)
    downward_gradient = jnp.einsum(
        "sk,sd->kd", active, out_grad, preferred_element_type=jnp.float32
    )
    up_grad = jnp.einsum("sd,sk->dk", normed_feed, upward_grad, preferred_element_type=jnp.float32)
    feed_input_part = jnp.einsum(
        "sk,dk->sd", upward_grad, feed_up, preferred_element_type=jnp.float32
    )
    feed_back = norm_back(after_cross, feed_gain, feed_bias, direct_total(feed_input_part))
    feed_sums = [dp_sum(up_grad), dp_sum(downward_gradient)]
    cross_grad_rows = out_grad.astype(jnp.float32) + feed_back[0]
    cross_grad_low = cross_grad_rows.astype(jnp.bfloat16)
    cout_grad = jnp.einsum(
        "sk,sd->kd", cross_flat, cross_grad_low, preferred_element_type=jnp.float32
    )
    cross_heads_grad = jnp.einsum(
        "sd,kd->sk", cross_grad_low, cross_out, preferred_element_type=jnp.float32
    ).astype(jnp.bfloat16)
    cross_heads_grad = cross_heads_grad.reshape(clip_count, slot_len, head_count, HEAD)

    def cross_clip_back(entries):
        return attend_back(
            entries[0],
            entries[1],
            entries[2],
            entries[3],
            entries[4],
            entries[5],
            False,
            score_scale,
        )

    cquery_heads, ckey_heads, cvalue_heads = lax.map(
        cross_clip_back,
        (cross_queries, text_proj[0], text_proj[1], cross_log, cross_heads_grad, text_token_length),
    )
    query_grad_low = cquery_heads.reshape(row_total, local_width).astype(jnp.bfloat16)
    keyval_grad_low = jnp.stack((ckey_heads, cvalue_heads)).astype(jnp.bfloat16)
    keyval_grad_low = keyval_grad_low.reshape(2, clip_count, text_count, local_width)
    cquery_grad = jnp.einsum(
        "sd,se->de", normed_cross, query_grad_low, preferred_element_type=jnp.float32
    )
    ckeyval_grad = jnp.einsum(
        "ctd,gcte->gde", text_states, keyval_grad_low, preferred_element_type=jnp.float32
    )
    text_part = jnp.einsum(
        "gcte,gde->ctd", keyval_grad_low, cross_keyval, preferred_element_type=jnp.float32
    )
    cross_sum = gathered_sum(query_grad_low, cross_query_all, "se,de->sd")
    feed_low, cross_sum = lax.optimization_barrier((feed_low, cross_sum))
    block_out = (after_cross + direct_total(feed_low)).astype(jnp.bfloat16)
    text_grad = lax.psum(text_part.astype(jnp.bfloat16), "tensor").astype(jnp.float32)
    cross_back = norm_back(after_self, cross_gain, cross_bias, cross_sum)
    self_grad_rows = cross_grad_rows + cross_back[0]
    feed_sums, self_grad_rows = lax.optimization_barrier((feed_sums, self_grad_rows))
    self_grad_low = self_grad_rows.astype(jnp.bfloat16)
    sout_grad = jnp.einsum(
        "sk,sd->kd", self_flat, self_grad_low, preferred_element_type=jnp.float32
    )
    self_heads_grad = jnp.einsum(
        "sd,kd->sk", self_grad_low, self_out, preferred_element_type=jnp.float32
    ).astype(jnp.bfloat16)
    self_heads_grad = self_heads_grad.reshape(clip_count, slot_len, head_count, HEAD)

    def self_clip_back(entries):
        return attend_back(
            entries[0],
            entries[1],
            entries[2],
            entries[3],
            entries[4],
            entries[5],
            True,
            score_scale,
        )

    self_query_heads, self_key_heads, self_value_heads = lax.map(
        self_clip_back,
        (projected[0], projected[1], projected[2], self_log, self_heads_grad, frame_len),
    )
    projection_gradient = jnp.stack((self_query_heads, self_key_heads, self_value_heads)).astype(
        jnp.bfloat16
    )
    projection_gradient = projection_gradient.reshape(3, row_total, local_width)
    qkv_grad = jnp.einsum(
        "sd,cse->cde", normed_self, projection_gradient, preferred_element_type=jnp.float32
    )
    self_input_part = jnp.einsum(
        "cse,cde->sd", projection_gradient, self_qkv, preferred_element_type=jnp.float32
    )
    self_back = norm_back(inputs, self_gain, self_bias, direct_total(self_input_part))
    self_norm_terms = (dp_sum(self_back[1]), dp_sum(self_back[2]))
    frames_grad = self_grad_rows + self_back[0]
    gain_terms = (
        self_back[1],
        self_back[2],
        cross_back[1],
        cross_back[2],
        feed_back[1],
        feed_back[2],
    )
    late_sums = [dp_sum(term) for term in (qkv_grad, sout_grad, cquery_grad, ckeyval_grad)]
    late_sums = late_sums + stacked_psum(
        cout_grad, [cross_back[1], cross_back[2], feed_back[1], feed_back[2]], "dp"
    )
    summed = (
        self_norm_terms[0],
        self_norm_terms[1],
        late_sums[5],
        late_sums[6],
        late_sums[7],
        late_sums[8],
        late_sums[0],
        late_sums[1],
        late_sums[2],
        late_sums[3],
        late_sums[4],
        feed_sums[0],
        feed_sums[1],
    )
    return (
        block_out.reshape(clip_count, slot_len, model_width),
        frames_grad.reshape(clip_count, slot_len, model_width),
        text_grad,
        summed[0],
        summed[1],
        summed[2],
        summed[3],
        summed[4],
        summed[5],
        summed[6],
        summed[7],
        summed[8],
        summed[9],
        summed[10],
        summed[11],
        summed[12],
    )


def solution(mesh):
    return jax.shard_map(
        local,
        mesh=mesh,
        in_specs=(
            P("dp", None, None),
            P("dp", None, None),
            P("dp"),
            P("dp"),
            P(),
            P(),
            P(),
            P(),
            P(),
            P(),
            P(None, None, "tensor"),
            P("tensor", None),
            P(None, "tensor"),
            P(None, None, "tensor"),
            P("tensor", None),
            P(None, "tensor"),
            P("tensor", None),
            P("dp", None, None),
        ),
        out_specs=(
            P("dp", None, None),
            P("dp", None, None),
            P("dp", None, None),
            P(),
            P(),
            P(),
            P(),
            P(),
            P(),
            P(None, None, "tensor"),
            P("tensor", None),
            P(None, "tensor"),
            P(None, None, "tensor"),
            P("tensor", None),
            P(None, "tensor"),
            P("tensor", None),
        ),
        check_vma=False,
    )
```

```python
import jax
import jax.numpy as jnp
from jax import lax
from jax.sharding import PartitionSpec as P

HEAD = 64


EPSILON = 1e-05
MASKED = -1e30


def layer_norm(inputs, norm_gain, norm_bias):
    row_mean = jnp.mean(inputs, axis=-1, keepdims=True)
    centred = inputs - row_mean
    spread = jnp.mean(centred * centred, axis=-1, keepdims=True)
    return centred * lax.rsqrt(spread + EPSILON) * norm_gain + norm_bias


def normalized(inputs):
    row_mean = jnp.mean(inputs, axis=-1, keepdims=True)
    centred = inputs - row_mean
    spread = jnp.mean(centred * centred, axis=-1, keepdims=True)
    return centred * lax.rsqrt(spread + EPSILON)


def norm_back(inputs, norm_gain, norm_bias, upstream):
    _, pullback = jax.vjp(layer_norm, inputs, norm_gain, norm_bias)
    return pullback(upstream)


def gelu_exact(inputs):
    return jax.nn.gelu(inputs, approximate=False)


def masked_scores(portion, offset, key_rows, key_limit, causal, score_scale):
    scores = (
        jnp.einsum("bhe,khe->hbk", portion, key_rows, preferred_element_type=jnp.float32)
        * score_scale
    )
    key_pos = jnp.arange(key_rows.shape[0])
    allowed = key_pos[None, :] < key_limit
    if causal:
        allowed = allowed & (key_pos[None, :] <= offset + jnp.arange(portion.shape[0])[:, None])
    return jnp.where(allowed[None], scores, MASKED)


def attend(queries, key_rows, values, key_limit, causal, score_scale):
    row_count, head_count, head_size = queries.shape
    block_len = min(512, row_count)
    portions = queries.reshape(row_count // block_len, block_len, head_count, head_size)
    offsets = jnp.arange(row_count // block_len) * block_len

    def one_block(entries):
        portion, offset = entries
        scores = masked_scores(portion, offset, key_rows, key_limit, causal, score_scale)
        row_max = jnp.max(scores, axis=-1, keepdims=True)
        unnormed = jnp.exp(scores - row_max)
        row_sum = jnp.sum(unnormed, axis=-1, keepdims=True)
        probs_low = (unnormed / row_sum).astype(jnp.bfloat16)
        result = jnp.einsum("hbk,khe->bhe", probs_low, values, preferred_element_type=jnp.float32)
        return (result.astype(jnp.bfloat16), row_max[..., 0] + jnp.log(row_sum[..., 0]))

    if not causal:
        result, log_total = lax.map(one_block, (portions, offsets))
        return (result.reshape(row_count, head_count, head_size), log_total)
    results, totals = [], []
    for index in range(row_count // block_len):
        key_end = (index + 1) * block_len
        scores = masked_scores(
            portions[index], index * block_len, key_rows[:key_end], key_limit, causal, score_scale
        )
        row_max = jnp.max(scores, axis=-1, keepdims=True)
        unnormed = jnp.exp(scores - row_max)
        row_sum = jnp.sum(unnormed, axis=-1, keepdims=True)
        probs_low = (unnormed / row_sum).astype(jnp.bfloat16)
        result = jnp.einsum(
            "hbk,khe->bhe", probs_low, values[:key_end], preferred_element_type=jnp.float32
        )
        results.append(result.astype(jnp.bfloat16))
        totals.append(row_max[..., 0] + jnp.log(row_sum[..., 0]))
    return (jnp.concatenate(results).reshape(row_count, head_count, head_size), jnp.stack(totals))


def attend_back(queries, key_rows, values, log_total, out_grad, key_limit, causal, score_scale):
    row_count, head_count, head_size = queries.shape
    block_len = min(512, row_count)
    portions = queries.reshape(row_count // block_len, block_len, head_count, head_size)
    grad_parts = out_grad.reshape(row_count // block_len, block_len, head_count, head_size)
    offsets = jnp.arange(row_count // block_len) * block_len

    def one_block(carry, entries):
        key_grad, value_grad = carry
        portion, grad_part, log_part, offset = entries
        scores = masked_scores(portion, offset, key_rows, key_limit, causal, score_scale)
        probs = jnp.exp(scores - log_part[..., None])
        probs_grad = jnp.einsum(
            "bhe,khe->hbk", grad_part, values, preferred_element_type=jnp.float32
        )
        row_dot = jnp.sum(probs * probs_grad, axis=-1, keepdims=True)
        scores_grad = (probs * (probs_grad - row_dot)).astype(jnp.bfloat16)
        value_grad = value_grad + jnp.einsum(
            "hbk,bhe->khe",
            probs.astype(jnp.bfloat16),
            grad_part,
            preferred_element_type=jnp.float32,
        )
        key_grad = (
            key_grad
            + jnp.einsum("hbk,bhe->khe", scores_grad, portion, preferred_element_type=jnp.float32)
            * score_scale
        )
        query_grad = (
            jnp.einsum("hbk,khe->bhe", scores_grad, key_rows, preferred_element_type=jnp.float32)
            * score_scale
        )
        return ((key_grad, value_grad), query_grad)

    empty = jnp.zeros(key_rows.shape, jnp.float32)
    if not causal:
        (key_grad, value_grad), query_grad = lax.scan(
            one_block, (empty, empty), (portions, grad_parts, log_total, offsets)
        )
        return (query_grad.reshape(row_count, head_count, head_size), key_grad, value_grad)
    key_grad, value_grad, query_grads = empty, empty, []
    for index in range(row_count // block_len):
        key_end = (index + 1) * block_len
        portion, grad_part = portions[index], grad_parts[index]
        keys, vals = key_rows[:key_end], values[:key_end]
        scores = masked_scores(portion, index * block_len, keys, key_limit, causal, score_scale)
        probs = jnp.exp(scores - log_total[index][..., None])
        probs_grad = jnp.einsum("bhe,khe->hbk", grad_part, vals, preferred_element_type=jnp.float32)
        row_dot = jnp.sum(probs * probs_grad, axis=-1, keepdims=True)
        scores_grad = (probs * (probs_grad - row_dot)).astype(jnp.bfloat16)
        value_part = jnp.einsum(
            "hbk,bhe->khe", probs.astype(jnp.bfloat16), grad_part, preferred_element_type=jnp.float32
        )
        key_part = (
            jnp.einsum("hbk,bhe->khe", scores_grad, portion, preferred_element_type=jnp.float32)
            * score_scale
        )
        value_grad = value_grad.at[:key_end].add(value_part)
        key_grad = key_grad.at[:key_end].add(key_part)
        query_grads.append(
            jnp.einsum("hbk,khe->bhe", scores_grad, keys, preferred_element_type=jnp.float32)
            * score_scale
        )
    query_grad = jnp.concatenate(query_grads)
    return (query_grad.reshape(row_count, head_count, head_size), key_grad, value_grad)


def head_total(partial_value):
    return lax.psum(partial_value.astype(jnp.bfloat16), "tensor").astype(jnp.float32)


def relay_pieces(block, axis):
    count = lax.axis_size(axis)
    me = lax.axis_index(axis)
    pieces = [(block, me)]
    from_left, from_right = block, block
    for k in range(1, count):
        from_left = lax.ppermute(from_left, axis, [(i, i + 1) for i in range(k - 1, count - 1)])
        from_right = lax.ppermute(from_right, axis, [(i, i - 1) for i in range(1, count - k + 1)])
        pieces.append((from_left, me - k))
        pieces.append((from_right, me + k))
    return pieces


def relay_scatter(value, axis):
    count = lax.axis_size(axis)
    me = lax.axis_index(axis)
    shards = value.reshape((count, value.shape[0] // count) + value.shape[1:])

    def pick(index):
        return lax.dynamic_index_in_dim(shards, jnp.clip(index, 0, count - 1), 0, keepdims=False)

    to_right = to_left = None
    for k in range(1, count):
        send_right = pick(me + count - k).astype(jnp.float32)
        send_left = pick(me - (count - k)).astype(jnp.float32)
        if to_right is not None:
            send_right = send_right + to_right.astype(jnp.float32)
            send_left = send_left + to_left.astype(jnp.float32)
        to_right = lax.ppermute(
            send_right.astype(value.dtype), axis, [(i, i + 1) for i in range(min(k, count - 1))]
        )
        to_left = lax.ppermute(
            send_left.astype(value.dtype), axis, [(i, i - 1) for i in range(max(count - k, 1), count)]
        )
    total = pick(me).astype(jnp.float32)
    if to_right is not None:
        total = total + to_right.astype(jnp.float32) + to_left.astype(jnp.float32)
    return total.astype(value.dtype)


def _rotate(value, axis, count, step):
    return lax.ppermute(value, axis, [(i, (i + step) % count) for i in range(count)])


def direct_total(partial_value):
    count = lax.axis_size("tensor")
    me = lax.axis_index("tensor")
    low_value = partial_value.astype(jnp.bfloat16)
    shards = low_value.reshape((count, low_value.shape[0] // count) + low_value.shape[1:])
    reduced = lax.dynamic_index_in_dim(shards, me, 0, keepdims=False).astype(jnp.float32)
    for step in range(1, count):
        sent = lax.dynamic_index_in_dim(shards, (me + step) % count, 0, keepdims=False)
        reduced = reduced + _rotate(sent, "tensor", count, step).astype(jnp.float32)
    reduced = reduced.astype(jnp.bfloat16)
    pieces = [(reduced, me)] + [
        (_rotate(reduced, "tensor", count, step), (me - step) % count) for step in range(1, count)
    ]
    rows = []
    for owner in range(count):
        shard = jnp.zeros_like(reduced)
        for piece, source in pieces:
            shard = jnp.where(source == owner, piece, shard)
        rows.append(shard)
    return jnp.concatenate(rows).astype(jnp.float32)


def relay_total(partial_value):
    low_value = partial_value.astype(jnp.bfloat16)
    reduced = relay_scatter(low_value, "tensor")
    pieces = relay_pieces(reduced, "tensor")
    shards = []
    for owner in range(len(pieces) // 2 + 1):
        shard = jnp.zeros_like(reduced)
        for piece, source in pieces:
            shard = jnp.where(source == owner, piece, shard)
        shards.append(shard)
    return jnp.concatenate(shards).astype(jnp.float32)


def stacked_psum(matrix, rows, axis):
    pad = (-(matrix.shape[0] + len(rows))) % 16
    extra = jnp.stack(rows + [jnp.zeros_like(rows[0])] * pad)
    summed = lax.psum(jnp.concatenate([matrix, extra]).astype(jnp.bfloat16), axis)
    summed = summed.astype(jnp.float32)
    count = matrix.shape[0]
    return [summed[:count]] + [summed[count + i] for i in range(len(rows))]


def dp_sum(term):
    return lax.psum(term.astype(jnp.bfloat16), "dp").astype(jnp.float32)


def direct_pieces(block, axis):
    count = lax.axis_size(axis)
    me = lax.axis_index(axis)
    return [(block, me)] + [
        (_rotate(block, axis, count, step), (me - step) % count) for step in range(1, count)
    ]


def gathered_sum(block, weights, spec, pieces_of=relay_pieces):
    count = weights.shape[0]
    total = None
    for piece, source in pieces_of(block, "tensor"):
        weight = lax.dynamic_index_in_dim(weights, jnp.clip(source, 0, count - 1), 0, keepdims=False)
        partial_value = jnp.einsum(spec, piece, weight, preferred_element_type=jnp.float32)
        partial_value = partial_value.astype(jnp.bfloat16).astype(jnp.float32)
        total = partial_value if total is None else total + partial_value
        total = lax.optimization_barrier(total)
    return total


def local(
    frames,
    text_states,
    frame_len,
    text_token_length,
    self_gain,
    self_bias,
    cross_gain,
    cross_bias,
    feed_gain,
    feed_bias,
    self_qkv,
    self_out,
    cross_query,
    cross_keyval,
    cross_out,
    feed_up,
    feed_down,
    cotangent,
):
    clip_count, slot_len, model_width = frames.shape
    text_count = text_states.shape[1]
    local_width = self_out.shape[0]
    head_count = local_width // HEAD
    score_scale = HEAD ** (-0.5)
    row_total = clip_count * slot_len
    inputs = frames.reshape(row_total, model_width).astype(jnp.float32)
    out_grad = cotangent.reshape(row_total, model_width)
    normed_self = layer_norm(inputs, self_gain, self_bias).astype(jnp.bfloat16)
    projected = jnp.einsum(
        "sd,cde->cse", normed_self, self_qkv, preferred_element_type=jnp.float32
    ).astype(jnp.bfloat16)
    projected = projected.reshape(3, clip_count, slot_len, head_count, HEAD)

    def self_clip(entries):
        return attend(entries[0], entries[1], entries[2], entries[3], True, score_scale)

    self_heads, self_log = lax.map(self_clip, (projected[0], projected[1], projected[2], frame_len))
    self_flat = self_heads.reshape(row_total, local_width)
    self_out_all = lax.all_gather(self_out, "tensor")
    cross_out_all = lax.all_gather(cross_out, "tensor")
    cross_query_all = lax.all_gather(cross_query, "tensor")
    after_self = inputs + gathered_sum(self_flat, self_out_all, "sk,kd->sd")
    normed_cross = layer_norm(after_self, cross_gain, cross_bias).astype(jnp.bfloat16)
    cross_queries = jnp.dot(normed_cross, cross_query, preferred_element_type=jnp.float32).astype(
        jnp.bfloat16
    )
    cross_queries = cross_queries.reshape(clip_count, slot_len, head_count, HEAD)
    text_proj = jnp.einsum(
        "ctd,gde->gcte", text_states, cross_keyval, preferred_element_type=jnp.float32
    ).astype(jnp.bfloat16)
    text_proj = text_proj.reshape(2, clip_count, text_count, head_count, HEAD)

    def cross_clip(entries):
        return attend(entries[0], entries[1], entries[2], entries[3], False, score_scale)

    cross_heads, cross_log = lax.map(
        cross_clip, (cross_queries, text_proj[0], text_proj[1], text_token_length)
    )
    cross_flat = cross_heads.reshape(row_total, local_width)
    after_cross = after_self + gathered_sum(cross_flat, cross_out_all, "sk,kd->sd")
    normed_feed = layer_norm(after_cross, feed_gain, feed_bias).astype(jnp.bfloat16)
    upward = jnp.dot(normed_feed, feed_up, preferred_element_type=jnp.float32)
    active = gelu_exact(upward).astype(jnp.bfloat16)
    feed_part = jnp.dot(active, feed_down, preferred_element_type=jnp.float32)
    feed_low = feed_part.astype(jnp.bfloat16)
    active_grad = jnp.einsum("sd,kd->sk", out_grad, feed_down, preferred_element_type=jnp.float32)
    _, gelu_pull = jax.vjp(gelu_exact, upward)
    upward_grad = gelu_pull(active_grad)[0].astype(jnp.bfloat16)
    downward_gradient = jnp.einsum(
        "sk,sd->kd", active, out_grad, preferred_element_type=jnp.float32
    )
    up_grad = jnp.einsum("sd,sk->dk", normed_feed, upward_grad, preferred_element_type=jnp.float32)
    feed_input_part = jnp.einsum(
        "sk,dk->sd", upward_grad, feed_up, preferred_element_type=jnp.float32
    )
    feed_back = norm_back(after_cross, feed_gain, feed_bias, direct_total(feed_input_part))
    feed_sums = [dp_sum(up_grad), dp_sum(downward_gradient)]
    cross_grad_rows = out_grad.astype(jnp.float32) + feed_back[0]
    cross_grad_low = cross_grad_rows.astype(jnp.bfloat16)
    cout_grad = jnp.einsum(
        "sk,sd->kd", cross_flat, cross_grad_low, preferred_element_type=jnp.float32
    )
    cross_heads_grad = jnp.einsum(
        "sd,kd->sk", cross_grad_low, cross_out, preferred_element_type=jnp.float32
    ).astype(jnp.bfloat16)
    cross_heads_grad = cross_heads_grad.reshape(clip_count, slot_len, head_count, HEAD)

    def cross_clip_back(entries):
        return attend_back(
            entries[0],
            entries[1],
            entries[2],
            entries[3],
            entries[4],
            entries[5],
            False,
            score_scale,
        )

    cquery_heads, ckey_heads, cvalue_heads = lax.map(
        cross_clip_back,
        (cross_queries, text_proj[0], text_proj[1], cross_log, cross_heads_grad, text_token_length),
    )
    query_grad_low = cquery_heads.reshape(row_total, local_width).astype(jnp.bfloat16)
    feed_low, query_grad_low = lax.optimization_barrier((feed_low, query_grad_low))
    block_out = (after_cross + lax.psum(feed_low, "tensor").astype(jnp.float32)).astype(
        jnp.bfloat16
    )
    keyval_grad_low = jnp.stack((ckey_heads, cvalue_heads)).astype(jnp.bfloat16)
    keyval_grad_low = keyval_grad_low.reshape(2, clip_count, text_count, local_width)
    cquery_grad = jnp.einsum(
        "sd,se->de", normed_cross, query_grad_low, preferred_element_type=jnp.float32
    )
    ckeyval_grad = jnp.einsum(
        "ctd,gcte->gde", text_states, keyval_grad_low, preferred_element_type=jnp.float32
    )
    text_part = jnp.einsum(
        "gcte,gde->ctd", keyval_grad_low, cross_keyval, preferred_element_type=jnp.float32
    )
    cross_sum = gathered_sum(query_grad_low, cross_query_all, "se,de->sd", direct_pieces)
    text_grad = lax.psum(text_part.astype(jnp.bfloat16), "tensor").astype(jnp.float32)
    cross_back = norm_back(after_self, cross_gain, cross_bias, cross_sum)
    self_grad_rows = cross_grad_rows + cross_back[0]
    feed_sums, self_grad_rows = lax.optimization_barrier((feed_sums, self_grad_rows))
    self_grad_low = self_grad_rows.astype(jnp.bfloat16)
    sout_grad = jnp.einsum(
        "sk,sd->kd", self_flat, self_grad_low, preferred_element_type=jnp.float32
    )
    self_heads_grad = jnp.einsum(
        "sd,kd->sk", self_grad_low, self_out, preferred_element_type=jnp.float32
    ).astype(jnp.bfloat16)
    self_heads_grad = self_heads_grad.reshape(clip_count, slot_len, head_count, HEAD)

    def self_clip_back(entries):
        return attend_back(
            entries[0],
            entries[1],
            entries[2],
            entries[3],
            entries[4],
            entries[5],
            True,
            score_scale,
        )

    self_query_heads, self_key_heads, self_value_heads = lax.map(
        self_clip_back,
        (projected[0], projected[1], projected[2], self_log, self_heads_grad, frame_len),
    )
    projection_gradient = jnp.stack((self_query_heads, self_key_heads, self_value_heads)).astype(
        jnp.bfloat16
    )
    projection_gradient = projection_gradient.reshape(3, row_total, local_width)
    qkv_grad = jnp.einsum(
        "sd,cse->cde", normed_self, projection_gradient, preferred_element_type=jnp.float32
    )
    self_input_part = jnp.einsum(
        "cse,cde->sd", projection_gradient, self_qkv, preferred_element_type=jnp.float32
    )
    self_back = norm_back(inputs, self_gain, self_bias, direct_total(self_input_part))
    self_norm_terms = (dp_sum(self_back[1]), dp_sum(self_back[2]))
    frames_grad = self_grad_rows + self_back[0]
    gain_terms = (
        self_back[1],
        self_back[2],
        cross_back[1],
        cross_back[2],
        feed_back[1],
        feed_back[2],
    )
    late_sums = [dp_sum(term) for term in (qkv_grad, sout_grad, cquery_grad, ckeyval_grad)]
    late_sums = late_sums + stacked_psum(
        cout_grad, [cross_back[1], cross_back[2], feed_back[1], feed_back[2]], "dp"
    )
    summed = (
        self_norm_terms[0],
        self_norm_terms[1],
        late_sums[5],
        late_sums[6],
        late_sums[7],
        late_sums[8],
        late_sums[0],
        late_sums[1],
        late_sums[2],
        late_sums[3],
        late_sums[4],
        feed_sums[0],
        feed_sums[1],
    )
    return (
        block_out.reshape(clip_count, slot_len, model_width),
        frames_grad.reshape(clip_count, slot_len, model_width),
        text_grad,
        summed[0],
        summed[1],
        summed[2],
        summed[3],
        summed[4],
        summed[5],
        summed[6],
        summed[7],
        summed[8],
        summed[9],
        summed[10],
        summed[11],
        summed[12],
    )


def solution(mesh):
    return jax.shard_map(
        local,
        mesh=mesh,
        in_specs=(
            P("dp", None, None),
            P("dp", None, None),
            P("dp"),
            P("dp"),
            P(),
            P(),
            P(),
            P(),
            P(),
            P(),
            P(None, None, "tensor"),
            P("tensor", None),
            P(None, "tensor"),
            P(None, None, "tensor"),
            P("tensor", None),
            P(None, "tensor"),
            P("tensor", None),
            P("dp", None, None),
        ),
        out_specs=(
            P("dp", None, None),
            P("dp", None, None),
            P("dp", None, None),
            P(),
            P(),
            P(),
            P(),
            P(),
            P(),
            P(None, None, "tensor"),
            P("tensor", None),
            P(None, "tensor"),
            P(None, None, "tensor"),
            P("tensor", None),
            P(None, "tensor"),
            P("tensor", None),
        ),
        check_vma=False,
    )
```

```python
import jax
import jax.numpy as jnp
from jax import lax
from jax.sharding import PartitionSpec as P

HEAD = 64


EPSILON = 1e-05
MASKED = -1e30


def layer_norm(inputs, norm_gain, norm_bias):
    row_mean = jnp.mean(inputs, axis=-1, keepdims=True)
    centred = inputs - row_mean
    spread = jnp.mean(centred * centred, axis=-1, keepdims=True)
    return centred * lax.rsqrt(spread + EPSILON) * norm_gain + norm_bias


def normalized(inputs):
    row_mean = jnp.mean(inputs, axis=-1, keepdims=True)
    centred = inputs - row_mean
    spread = jnp.mean(centred * centred, axis=-1, keepdims=True)
    return centred * lax.rsqrt(spread + EPSILON)


def norm_back(inputs, norm_gain, norm_bias, upstream):
    _, pullback = jax.vjp(layer_norm, inputs, norm_gain, norm_bias)
    return pullback(upstream)


def gelu_exact(inputs):
    return jax.nn.gelu(inputs, approximate=False)


def masked_scores(portion, offset, key_rows, key_limit, causal, score_scale):
    scores = (
        jnp.einsum("bhe,khe->hbk", portion, key_rows, preferred_element_type=jnp.float32)
        * score_scale
    )
    key_pos = jnp.arange(key_rows.shape[0])
    allowed = key_pos[None, :] < key_limit
    if causal:
        allowed = allowed & (key_pos[None, :] <= offset + jnp.arange(portion.shape[0])[:, None])
    return jnp.where(allowed[None], scores, MASKED)


def attend(queries, key_rows, values, key_limit, causal, score_scale):
    row_count, head_count, head_size = queries.shape
    block_len = min(512, row_count)
    portions = queries.reshape(row_count // block_len, block_len, head_count, head_size)
    offsets = jnp.arange(row_count // block_len) * block_len

    def one_block(entries):
        portion, offset = entries
        scores = masked_scores(portion, offset, key_rows, key_limit, causal, score_scale)
        row_max = jnp.max(scores, axis=-1, keepdims=True)
        unnormed = jnp.exp(scores - row_max)
        row_sum = jnp.sum(unnormed, axis=-1, keepdims=True)
        probs_low = (unnormed / row_sum).astype(jnp.bfloat16)
        result = jnp.einsum("hbk,khe->bhe", probs_low, values, preferred_element_type=jnp.float32)
        return (result.astype(jnp.bfloat16), row_max[..., 0] + jnp.log(row_sum[..., 0]))

    if not causal:
        result, log_total = lax.map(one_block, (portions, offsets))
        return (result.reshape(row_count, head_count, head_size), log_total)
    results, totals = [], []
    for index in range(row_count // block_len):
        key_end = (index + 1) * block_len
        scores = masked_scores(
            portions[index], index * block_len, key_rows[:key_end], key_limit, causal, score_scale
        )
        row_max = jnp.max(scores, axis=-1, keepdims=True)
        unnormed = jnp.exp(scores - row_max)
        row_sum = jnp.sum(unnormed, axis=-1, keepdims=True)
        probs_low = (unnormed / row_sum).astype(jnp.bfloat16)
        result = jnp.einsum(
            "hbk,khe->bhe", probs_low, values[:key_end], preferred_element_type=jnp.float32
        )
        results.append(result.astype(jnp.bfloat16))
        totals.append(row_max[..., 0] + jnp.log(row_sum[..., 0]))
    return (jnp.concatenate(results).reshape(row_count, head_count, head_size), jnp.stack(totals))


def attend_back(queries, key_rows, values, log_total, out_grad, key_limit, causal, score_scale):
    row_count, head_count, head_size = queries.shape
    block_len = min(512, row_count)
    portions = queries.reshape(row_count // block_len, block_len, head_count, head_size)
    grad_parts = out_grad.reshape(row_count // block_len, block_len, head_count, head_size)
    offsets = jnp.arange(row_count // block_len) * block_len

    def one_block(carry, entries):
        key_grad, value_grad = carry
        portion, grad_part, log_part, offset = entries
        scores = masked_scores(portion, offset, key_rows, key_limit, causal, score_scale)
        probs = jnp.exp(scores - log_part[..., None])
        probs_grad = jnp.einsum(
            "bhe,khe->hbk", grad_part, values, preferred_element_type=jnp.float32
        )
        row_dot = jnp.sum(probs * probs_grad, axis=-1, keepdims=True)
        scores_grad = (probs * (probs_grad - row_dot)).astype(jnp.bfloat16)
        value_grad = value_grad + jnp.einsum(
            "hbk,bhe->khe",
            probs.astype(jnp.bfloat16),
            grad_part,
            preferred_element_type=jnp.float32,
        )
        key_grad = (
            key_grad
            + jnp.einsum("hbk,bhe->khe", scores_grad, portion, preferred_element_type=jnp.float32)
            * score_scale
        )
        query_grad = (
            jnp.einsum("hbk,khe->bhe", scores_grad, key_rows, preferred_element_type=jnp.float32)
            * score_scale
        )
        return ((key_grad, value_grad), query_grad)

    empty = jnp.zeros(key_rows.shape, jnp.float32)
    if not causal:
        (key_grad, value_grad), query_grad = lax.scan(
            one_block, (empty, empty), (portions, grad_parts, log_total, offsets)
        )
        return (query_grad.reshape(row_count, head_count, head_size), key_grad, value_grad)
    key_grad, value_grad, query_grads = empty, empty, []
    for index in range(row_count // block_len):
        key_end = (index + 1) * block_len
        portion, grad_part = portions[index], grad_parts[index]
        keys, vals = key_rows[:key_end], values[:key_end]
        scores = masked_scores(portion, index * block_len, keys, key_limit, causal, score_scale)
        probs = jnp.exp(scores - log_total[index][..., None])
        probs_grad = jnp.einsum("bhe,khe->hbk", grad_part, vals, preferred_element_type=jnp.float32)
        row_dot = jnp.sum(probs * probs_grad, axis=-1, keepdims=True)
        scores_grad = (probs * (probs_grad - row_dot)).astype(jnp.bfloat16)
        value_part = jnp.einsum(
            "hbk,bhe->khe", probs.astype(jnp.bfloat16), grad_part, preferred_element_type=jnp.float32
        )
        key_part = (
            jnp.einsum("hbk,bhe->khe", scores_grad, portion, preferred_element_type=jnp.float32)
            * score_scale
        )
        value_grad = value_grad.at[:key_end].add(value_part)
        key_grad = key_grad.at[:key_end].add(key_part)
        query_grads.append(
            jnp.einsum("hbk,khe->bhe", scores_grad, keys, preferred_element_type=jnp.float32)
            * score_scale
        )
    query_grad = jnp.concatenate(query_grads)
    return (query_grad.reshape(row_count, head_count, head_size), key_grad, value_grad)


def head_total(partial_value):
    return lax.psum(partial_value.astype(jnp.bfloat16), "tensor").astype(jnp.float32)


def relay_pieces(block, axis):
    count = lax.axis_size(axis)
    me = lax.axis_index(axis)
    pieces = [(block, me)]
    from_left, from_right = block, block
    for k in range(1, count):
        from_left = lax.ppermute(from_left, axis, [(i, i + 1) for i in range(k - 1, count - 1)])
        from_right = lax.ppermute(from_right, axis, [(i, i - 1) for i in range(1, count - k + 1)])
        pieces.append((from_left, me - k))
        pieces.append((from_right, me + k))
    return pieces


def relay_scatter(value, axis):
    count = lax.axis_size(axis)
    me = lax.axis_index(axis)
    shards = value.reshape((count, value.shape[0] // count) + value.shape[1:])

    def pick(index):
        return lax.dynamic_index_in_dim(shards, jnp.clip(index, 0, count - 1), 0, keepdims=False)

    to_right = to_left = None
    for k in range(1, count):
        send_right = pick(me + count - k).astype(jnp.float32)
        send_left = pick(me - (count - k)).astype(jnp.float32)
        if to_right is not None:
            send_right = send_right + to_right.astype(jnp.float32)
            send_left = send_left + to_left.astype(jnp.float32)
        to_right = lax.ppermute(
            send_right.astype(value.dtype), axis, [(i, i + 1) for i in range(min(k, count - 1))]
        )
        to_left = lax.ppermute(
            send_left.astype(value.dtype), axis, [(i, i - 1) for i in range(max(count - k, 1), count)]
        )
    total = pick(me).astype(jnp.float32)
    if to_right is not None:
        total = total + to_right.astype(jnp.float32) + to_left.astype(jnp.float32)
    return total.astype(value.dtype)


def _rotate(value, axis, count, step):
    return lax.ppermute(value, axis, [(i, (i + step) % count) for i in range(count)])


def direct_total(partial_value):
    count = lax.axis_size("tensor")
    me = lax.axis_index("tensor")
    low_value = partial_value.astype(jnp.bfloat16)
    shards = low_value.reshape((count, low_value.shape[0] // count) + low_value.shape[1:])
    reduced = lax.dynamic_index_in_dim(shards, me, 0, keepdims=False).astype(jnp.float32)
    for step in range(1, count):
        sent = lax.dynamic_index_in_dim(shards, (me + step) % count, 0, keepdims=False)
        reduced = reduced + _rotate(sent, "tensor", count, step).astype(jnp.float32)
    reduced = reduced.astype(jnp.bfloat16)
    pieces = [(reduced, me)] + [
        (_rotate(reduced, "tensor", count, step), (me - step) % count) for step in range(1, count)
    ]
    rows = []
    for owner in range(count):
        shard = jnp.zeros_like(reduced)
        for piece, source in pieces:
            shard = jnp.where(source == owner, piece, shard)
        rows.append(shard)
    return jnp.concatenate(rows).astype(jnp.float32)


def relay_total(partial_value):
    low_value = partial_value.astype(jnp.bfloat16)
    reduced = relay_scatter(low_value, "tensor")
    pieces = relay_pieces(reduced, "tensor")
    shards = []
    for owner in range(len(pieces) // 2 + 1):
        shard = jnp.zeros_like(reduced)
        for piece, source in pieces:
            shard = jnp.where(source == owner, piece, shard)
        shards.append(shard)
    return jnp.concatenate(shards).astype(jnp.float32)


def stacked_psum(matrix, rows, axis):
    pad = (-(matrix.shape[0] + len(rows))) % 16
    extra = jnp.stack(rows + [jnp.zeros_like(rows[0])] * pad)
    summed = lax.psum(jnp.concatenate([matrix, extra]).astype(jnp.bfloat16), axis)
    summed = summed.astype(jnp.float32)
    count = matrix.shape[0]
    return [summed[:count]] + [summed[count + i] for i in range(len(rows))]


def dp_sum(term):
    return lax.psum(term.astype(jnp.bfloat16), "dp").astype(jnp.float32)


def gathered_sum(block, weights, spec):
    count = weights.shape[0]
    total = None
    for piece, source in relay_pieces(block, "tensor"):
        weight = lax.dynamic_index_in_dim(weights, jnp.clip(source, 0, count - 1), 0, keepdims=False)
        partial_value = jnp.einsum(spec, piece, weight, preferred_element_type=jnp.float32)
        partial_value = partial_value.astype(jnp.bfloat16).astype(jnp.float32)
        total = partial_value if total is None else total + partial_value
        total = lax.optimization_barrier(total)
    return total


def local(
    frames,
    text_states,
    frame_len,
    text_token_length,
    self_gain,
    self_bias,
    cross_gain,
    cross_bias,
    feed_gain,
    feed_bias,
    self_qkv,
    self_out,
    cross_query,
    cross_keyval,
    cross_out,
    feed_up,
    feed_down,
    cotangent,
):
    clip_count, slot_len, model_width = frames.shape
    text_count = text_states.shape[1]
    local_width = self_out.shape[0]
    head_count = local_width // HEAD
    score_scale = HEAD ** (-0.5)
    row_total = clip_count * slot_len
    inputs = frames.reshape(row_total, model_width).astype(jnp.float32)
    out_grad = cotangent.reshape(row_total, model_width)
    normed_self = layer_norm(inputs, self_gain, self_bias).astype(jnp.bfloat16)
    projected = jnp.einsum(
        "sd,cde->cse", normed_self, self_qkv, preferred_element_type=jnp.float32
    ).astype(jnp.bfloat16)
    projected = projected.reshape(3, clip_count, slot_len, head_count, HEAD)

    def self_clip(entries):
        return attend(entries[0], entries[1], entries[2], entries[3], True, score_scale)

    self_heads, self_log = lax.map(self_clip, (projected[0], projected[1], projected[2], frame_len))
    self_flat = self_heads.reshape(row_total, local_width)
    self_out_all = lax.all_gather(self_out, "tensor")
    cross_out_all = lax.all_gather(cross_out, "tensor")
    cross_query_all = lax.all_gather(cross_query, "tensor")
    after_self = inputs + gathered_sum(self_flat, self_out_all, "sk,kd->sd")
    normed_cross = layer_norm(after_self, cross_gain, cross_bias).astype(jnp.bfloat16)
    cross_queries = jnp.dot(normed_cross, cross_query, preferred_element_type=jnp.float32).astype(
        jnp.bfloat16
    )
    cross_queries = cross_queries.reshape(clip_count, slot_len, head_count, HEAD)
    text_proj = jnp.einsum(
        "ctd,gde->gcte", text_states, cross_keyval, preferred_element_type=jnp.float32
    ).astype(jnp.bfloat16)
    text_proj = text_proj.reshape(2, clip_count, text_count, head_count, HEAD)

    def cross_clip(entries):
        return attend(entries[0], entries[1], entries[2], entries[3], False, score_scale)

    cross_heads, cross_log = lax.map(
        cross_clip, (cross_queries, text_proj[0], text_proj[1], text_token_length)
    )
    cross_flat = cross_heads.reshape(row_total, local_width)
    after_cross = after_self + gathered_sum(cross_flat, cross_out_all, "sk,kd->sd")
    normed_feed = layer_norm(after_cross, feed_gain, feed_bias).astype(jnp.bfloat16)
    upward = jnp.dot(normed_feed, feed_up, preferred_element_type=jnp.float32)
    active = gelu_exact(upward).astype(jnp.bfloat16)
    feed_part = jnp.dot(active, feed_down, preferred_element_type=jnp.float32)
    feed_low = feed_part.astype(jnp.bfloat16)
    active_grad = jnp.einsum("sd,kd->sk", out_grad, feed_down, preferred_element_type=jnp.float32)
    _, gelu_pull = jax.vjp(gelu_exact, upward)
    upward_grad = gelu_pull(active_grad)[0].astype(jnp.bfloat16)
    downward_gradient = jnp.einsum(
        "sk,sd->kd", active, out_grad, preferred_element_type=jnp.float32
    )
    up_grad = jnp.einsum("sd,sk->dk", normed_feed, upward_grad, preferred_element_type=jnp.float32)
    feed_input_part = jnp.einsum(
        "sk,dk->sd", upward_grad, feed_up, preferred_element_type=jnp.float32
    )
    feed_back = norm_back(after_cross, feed_gain, feed_bias, relay_total(feed_input_part))
    feed_sums = [dp_sum(up_grad), dp_sum(downward_gradient)]
    cross_grad_rows = out_grad.astype(jnp.float32) + feed_back[0]
    cross_grad_low = cross_grad_rows.astype(jnp.bfloat16)
    cout_grad = jnp.einsum(
        "sk,sd->kd", cross_flat, cross_grad_low, preferred_element_type=jnp.float32
    )
    cross_heads_grad = jnp.einsum(
        "sd,kd->sk", cross_grad_low, cross_out, preferred_element_type=jnp.float32
    ).astype(jnp.bfloat16)
    cross_heads_grad = cross_heads_grad.reshape(clip_count, slot_len, head_count, HEAD)

    def cross_clip_back(entries):
        return attend_back(
            entries[0],
            entries[1],
            entries[2],
            entries[3],
            entries[4],
            entries[5],
            False,
            score_scale,
        )

    cquery_heads, ckey_heads, cvalue_heads = lax.map(
        cross_clip_back,
        (cross_queries, text_proj[0], text_proj[1], cross_log, cross_heads_grad, text_token_length),
    )
    query_grad_low = cquery_heads.reshape(row_total, local_width).astype(jnp.bfloat16)
    feed_low, query_grad_low = lax.optimization_barrier((feed_low, query_grad_low))
    block_out = (after_cross + lax.psum(feed_low, "tensor").astype(jnp.float32)).astype(
        jnp.bfloat16
    )
    keyval_grad_low = jnp.stack((ckey_heads, cvalue_heads)).astype(jnp.bfloat16)
    keyval_grad_low = keyval_grad_low.reshape(2, clip_count, text_count, local_width)
    cquery_grad = jnp.einsum(
        "sd,se->de", normed_cross, query_grad_low, preferred_element_type=jnp.float32
    )
    ckeyval_grad = jnp.einsum(
        "ctd,gcte->gde", text_states, keyval_grad_low, preferred_element_type=jnp.float32
    )
    text_part = jnp.einsum(
        "gcte,gde->ctd", keyval_grad_low, cross_keyval, preferred_element_type=jnp.float32
    )
    cross_sum = gathered_sum(query_grad_low, cross_query_all, "se,de->sd")
    text_grad = lax.psum(text_part.astype(jnp.bfloat16), "tensor").astype(jnp.float32)
    cross_back = norm_back(after_self, cross_gain, cross_bias, cross_sum)
    self_grad_rows = cross_grad_rows + cross_back[0]
    feed_sums, self_grad_rows = lax.optimization_barrier((feed_sums, self_grad_rows))
    self_grad_low = self_grad_rows.astype(jnp.bfloat16)
    sout_grad = jnp.einsum(
        "sk,sd->kd", self_flat, self_grad_low, preferred_element_type=jnp.float32
    )
    self_heads_grad = jnp.einsum(
        "sd,kd->sk", self_grad_low, self_out, preferred_element_type=jnp.float32
    ).astype(jnp.bfloat16)
    self_heads_grad = self_heads_grad.reshape(clip_count, slot_len, head_count, HEAD)

    def self_clip_back(entries):
        return attend_back(
            entries[0],
            entries[1],
            entries[2],
            entries[3],
            entries[4],
            entries[5],
            True,
            score_scale,
        )

    self_query_heads, self_key_heads, self_value_heads = lax.map(
        self_clip_back,
        (projected[0], projected[1], projected[2], self_log, self_heads_grad, frame_len),
    )
    projection_gradient = jnp.stack((self_query_heads, self_key_heads, self_value_heads)).astype(
        jnp.bfloat16
    )
    projection_gradient = projection_gradient.reshape(3, row_total, local_width)
    qkv_grad = jnp.einsum(
        "sd,cse->cde", normed_self, projection_gradient, preferred_element_type=jnp.float32
    )
    self_input_part = jnp.einsum(
        "cse,cde->sd", projection_gradient, self_qkv, preferred_element_type=jnp.float32
    )
    self_back = norm_back(inputs, self_gain, self_bias, direct_total(self_input_part))
    self_norm_terms = (dp_sum(self_back[1]), dp_sum(self_back[2]))
    frames_grad = self_grad_rows + self_back[0]
    gain_terms = (
        self_back[1],
        self_back[2],
        cross_back[1],
        cross_back[2],
        feed_back[1],
        feed_back[2],
    )
    late_sums = [dp_sum(term) for term in (qkv_grad, sout_grad, cquery_grad, ckeyval_grad)]
    late_sums = late_sums + stacked_psum(
        cout_grad, [cross_back[1], cross_back[2], feed_back[1], feed_back[2]], "dp"
    )
    summed = (
        self_norm_terms[0],
        self_norm_terms[1],
        late_sums[5],
        late_sums[6],
        late_sums[7],
        late_sums[8],
        late_sums[0],
        late_sums[1],
        late_sums[2],
        late_sums[3],
        late_sums[4],
        feed_sums[0],
        feed_sums[1],
    )
    return (
        block_out.reshape(clip_count, slot_len, model_width),
        frames_grad.reshape(clip_count, slot_len, model_width),
        text_grad,
        summed[0],
        summed[1],
        summed[2],
        summed[3],
        summed[4],
        summed[5],
        summed[6],
        summed[7],
        summed[8],
        summed[9],
        summed[10],
        summed[11],
        summed[12],
    )


def solution(mesh):
    return jax.shard_map(
        local,
        mesh=mesh,
        in_specs=(
            P("dp", None, None),
            P("dp", None, None),
            P("dp"),
            P("dp"),
            P(),
            P(),
            P(),
            P(),
            P(),
            P(),
            P(None, None, "tensor"),
            P("tensor", None),
            P(None, "tensor"),
            P(None, None, "tensor"),
            P("tensor", None),
            P(None, "tensor"),
            P("tensor", None),
            P("dp", None, None),
        ),
        out_specs=(
            P("dp", None, None),
            P("dp", None, None),
            P("dp", None, None),
            P(),
            P(),
            P(),
            P(),
            P(),
            P(),
            P(None, None, "tensor"),
            P("tensor", None),
            P(None, "tensor"),
            P(None, None, "tensor"),
            P("tensor", None),
            P(None, "tensor"),
            P("tensor", None),
        ),
        check_vma=False,
    )
```

```python
import jax
import jax.numpy as jnp
from jax import lax
from jax.sharding import PartitionSpec as P

HEAD = 64


EPSILON = 1e-05
MASKED = -1e30


def layer_norm(inputs, norm_gain, norm_bias):
    row_mean = jnp.mean(inputs, axis=-1, keepdims=True)
    centred = inputs - row_mean
    spread = jnp.mean(centred * centred, axis=-1, keepdims=True)
    return centred * lax.rsqrt(spread + EPSILON) * norm_gain + norm_bias


def normalized(inputs):
    row_mean = jnp.mean(inputs, axis=-1, keepdims=True)
    centred = inputs - row_mean
    spread = jnp.mean(centred * centred, axis=-1, keepdims=True)
    return centred * lax.rsqrt(spread + EPSILON)


def norm_back(inputs, norm_gain, norm_bias, upstream):
    _, pullback = jax.vjp(layer_norm, inputs, norm_gain, norm_bias)
    return pullback(upstream)


def gelu_exact(inputs):
    return jax.nn.gelu(inputs, approximate=False)


def masked_scores(portion, offset, key_rows, key_limit, causal, score_scale):
    scores = (
        jnp.einsum("bhe,khe->hbk", portion, key_rows, preferred_element_type=jnp.float32)
        * score_scale
    )
    key_pos = jnp.arange(key_rows.shape[0])
    allowed = key_pos[None, :] < key_limit
    if causal:
        allowed = allowed & (key_pos[None, :] <= offset + jnp.arange(portion.shape[0])[:, None])
    return jnp.where(allowed[None], scores, MASKED)


def attend(queries, key_rows, values, key_limit, causal, score_scale):
    row_count, head_count, head_size = queries.shape
    block_len = min(512, row_count)
    portions = queries.reshape(row_count // block_len, block_len, head_count, head_size)
    offsets = jnp.arange(row_count // block_len) * block_len

    def one_block(entries):
        portion, offset = entries
        scores = masked_scores(portion, offset, key_rows, key_limit, causal, score_scale)
        row_max = jnp.max(scores, axis=-1, keepdims=True)
        unnormed = jnp.exp(scores - row_max)
        row_sum = jnp.sum(unnormed, axis=-1, keepdims=True)
        probs_low = (unnormed / row_sum).astype(jnp.bfloat16)
        result = jnp.einsum("hbk,khe->bhe", probs_low, values, preferred_element_type=jnp.float32)
        return (result.astype(jnp.bfloat16), row_max[..., 0] + jnp.log(row_sum[..., 0]))

    if not causal:
        result, log_total = lax.map(one_block, (portions, offsets))
        return (result.reshape(row_count, head_count, head_size), log_total)
    results, totals = [], []
    for index in range(row_count // block_len):
        key_end = (index + 1) * block_len
        scores = masked_scores(
            portions[index], index * block_len, key_rows[:key_end], key_limit, causal, score_scale
        )
        row_max = jnp.max(scores, axis=-1, keepdims=True)
        unnormed = jnp.exp(scores - row_max)
        row_sum = jnp.sum(unnormed, axis=-1, keepdims=True)
        probs_low = (unnormed / row_sum).astype(jnp.bfloat16)
        result = jnp.einsum(
            "hbk,khe->bhe", probs_low, values[:key_end], preferred_element_type=jnp.float32
        )
        results.append(result.astype(jnp.bfloat16))
        totals.append(row_max[..., 0] + jnp.log(row_sum[..., 0]))
    return (jnp.concatenate(results).reshape(row_count, head_count, head_size), jnp.stack(totals))


def attend_back(queries, key_rows, values, log_total, out_grad, key_limit, causal, score_scale):
    row_count, head_count, head_size = queries.shape
    block_len = min(512, row_count)
    portions = queries.reshape(row_count // block_len, block_len, head_count, head_size)
    grad_parts = out_grad.reshape(row_count // block_len, block_len, head_count, head_size)
    offsets = jnp.arange(row_count // block_len) * block_len

    def one_block(carry, entries):
        key_grad, value_grad = carry
        portion, grad_part, log_part, offset = entries
        scores = masked_scores(portion, offset, key_rows, key_limit, causal, score_scale)
        probs = jnp.exp(scores - log_part[..., None])
        probs_grad = jnp.einsum(
            "bhe,khe->hbk", grad_part, values, preferred_element_type=jnp.float32
        )
        row_dot = jnp.sum(probs * probs_grad, axis=-1, keepdims=True)
        scores_grad = (probs * (probs_grad - row_dot)).astype(jnp.bfloat16)
        value_grad = value_grad + jnp.einsum(
            "hbk,bhe->khe",
            probs.astype(jnp.bfloat16),
            grad_part,
            preferred_element_type=jnp.float32,
        )
        key_grad = (
            key_grad
            + jnp.einsum("hbk,bhe->khe", scores_grad, portion, preferred_element_type=jnp.float32)
            * score_scale
        )
        query_grad = (
            jnp.einsum("hbk,khe->bhe", scores_grad, key_rows, preferred_element_type=jnp.float32)
            * score_scale
        )
        return ((key_grad, value_grad), query_grad)

    empty = jnp.zeros(key_rows.shape, jnp.float32)
    if not causal:
        (key_grad, value_grad), query_grad = lax.scan(
            one_block, (empty, empty), (portions, grad_parts, log_total, offsets)
        )
        return (query_grad.reshape(row_count, head_count, head_size), key_grad, value_grad)
    key_grad, value_grad, query_grads = empty, empty, []
    for index in range(row_count // block_len):
        key_end = (index + 1) * block_len
        portion, grad_part = portions[index], grad_parts[index]
        keys, vals = key_rows[:key_end], values[:key_end]
        scores = masked_scores(portion, index * block_len, keys, key_limit, causal, score_scale)
        probs = jnp.exp(scores - log_total[index][..., None])
        probs_grad = jnp.einsum("bhe,khe->hbk", grad_part, vals, preferred_element_type=jnp.float32)
        row_dot = jnp.sum(probs * probs_grad, axis=-1, keepdims=True)
        scores_grad = (probs * (probs_grad - row_dot)).astype(jnp.bfloat16)
        value_part = jnp.einsum(
            "hbk,bhe->khe", probs.astype(jnp.bfloat16), grad_part, preferred_element_type=jnp.float32
        )
        key_part = (
            jnp.einsum("hbk,bhe->khe", scores_grad, portion, preferred_element_type=jnp.float32)
            * score_scale
        )
        value_grad = value_grad.at[:key_end].add(value_part)
        key_grad = key_grad.at[:key_end].add(key_part)
        query_grads.append(
            jnp.einsum("hbk,khe->bhe", scores_grad, keys, preferred_element_type=jnp.float32)
            * score_scale
        )
    query_grad = jnp.concatenate(query_grads)
    return (query_grad.reshape(row_count, head_count, head_size), key_grad, value_grad)


def head_total(partial_value):
    return lax.psum(partial_value.astype(jnp.bfloat16), "tensor").astype(jnp.float32)


def relay_pieces(block, axis):
    count = lax.axis_size(axis)
    me = lax.axis_index(axis)
    pieces = [(block, me)]
    from_left, from_right = block, block
    for k in range(1, count):
        from_left = lax.ppermute(from_left, axis, [(i, i + 1) for i in range(k - 1, count - 1)])
        from_right = lax.ppermute(from_right, axis, [(i, i - 1) for i in range(1, count - k + 1)])
        pieces.append((from_left, me - k))
        pieces.append((from_right, me + k))
    return pieces


def relay_scatter(value, axis):
    count = lax.axis_size(axis)
    me = lax.axis_index(axis)
    shards = value.reshape((count, value.shape[0] // count) + value.shape[1:])

    def pick(index):
        return lax.dynamic_index_in_dim(shards, jnp.clip(index, 0, count - 1), 0, keepdims=False)

    to_right = to_left = None
    for k in range(1, count):
        send_right = pick(me + count - k).astype(jnp.float32)
        send_left = pick(me - (count - k)).astype(jnp.float32)
        if to_right is not None:
            send_right = send_right + to_right.astype(jnp.float32)
            send_left = send_left + to_left.astype(jnp.float32)
        to_right = lax.ppermute(
            send_right.astype(value.dtype), axis, [(i, i + 1) for i in range(min(k, count - 1))]
        )
        to_left = lax.ppermute(
            send_left.astype(value.dtype), axis, [(i, i - 1) for i in range(max(count - k, 1), count)]
        )
    total = pick(me).astype(jnp.float32)
    if to_right is not None:
        total = total + to_right.astype(jnp.float32) + to_left.astype(jnp.float32)
    return total.astype(value.dtype)


def _rotate(value, axis, count, step):
    return lax.ppermute(value, axis, [(i, (i + step) % count) for i in range(count)])


def direct_total(partial_value):
    count = lax.axis_size("tensor")
    me = lax.axis_index("tensor")
    low_value = partial_value.astype(jnp.bfloat16)
    shards = low_value.reshape((count, low_value.shape[0] // count) + low_value.shape[1:])
    reduced = lax.dynamic_index_in_dim(shards, me, 0, keepdims=False).astype(jnp.float32)
    for step in range(1, count):
        sent = lax.dynamic_index_in_dim(shards, (me + step) % count, 0, keepdims=False)
        reduced = reduced + _rotate(sent, "tensor", count, step).astype(jnp.float32)
    reduced = reduced.astype(jnp.bfloat16)
    pieces = [(reduced, me)] + [
        (_rotate(reduced, "tensor", count, step), (me - step) % count) for step in range(1, count)
    ]
    rows = []
    for owner in range(count):
        shard = jnp.zeros_like(reduced)
        for piece, source in pieces:
            shard = jnp.where(source == owner, piece, shard)
        rows.append(shard)
    return jnp.concatenate(rows).astype(jnp.float32)


def relay_total(partial_value):
    low_value = partial_value.astype(jnp.bfloat16)
    reduced = relay_scatter(low_value, "tensor")
    pieces = relay_pieces(reduced, "tensor")
    shards = []
    for owner in range(len(pieces) // 2 + 1):
        shard = jnp.zeros_like(reduced)
        for piece, source in pieces:
            shard = jnp.where(source == owner, piece, shard)
        shards.append(shard)
    return jnp.concatenate(shards).astype(jnp.float32)


def stacked_psum(matrix, rows, axis):
    pad = (-(matrix.shape[0] + len(rows))) % 16
    extra = jnp.stack(rows + [jnp.zeros_like(rows[0])] * pad)
    summed = lax.psum(jnp.concatenate([matrix, extra]).astype(jnp.bfloat16), axis)
    summed = summed.astype(jnp.float32)
    count = matrix.shape[0]
    return [summed[:count]] + [summed[count + i] for i in range(len(rows))]


def dp_sum(term):
    return lax.psum(term.astype(jnp.bfloat16), "dp").astype(jnp.float32)


def gathered_sum(block, weights, spec, pieces_of=relay_pieces):
    count = weights.shape[0]
    total = None
    for piece, source in pieces_of(block, "tensor"):
        weight = lax.dynamic_index_in_dim(weights, jnp.clip(source, 0, count - 1), 0, keepdims=False)
        partial_value = jnp.einsum(spec, piece, weight, preferred_element_type=jnp.float32)
        partial_value = partial_value.astype(jnp.bfloat16).astype(jnp.float32)
        total = partial_value if total is None else total + partial_value
        total = lax.optimization_barrier(total)
    return total


def local(
    frames,
    text_states,
    frame_len,
    text_token_length,
    self_gain,
    self_bias,
    cross_gain,
    cross_bias,
    feed_gain,
    feed_bias,
    self_qkv,
    self_out,
    cross_query,
    cross_keyval,
    cross_out,
    feed_up,
    feed_down,
    cotangent,
):
    clip_count, slot_len, model_width = frames.shape
    text_count = text_states.shape[1]
    local_width = self_out.shape[0]
    head_count = local_width // HEAD
    score_scale = HEAD ** (-0.5)
    row_total = clip_count * slot_len
    inputs = frames.reshape(row_total, model_width).astype(jnp.float32)
    out_grad = cotangent.reshape(row_total, model_width)
    normed_self = layer_norm(inputs, self_gain, self_bias).astype(jnp.bfloat16)
    projected = jnp.einsum(
        "sd,cde->cse", normed_self, self_qkv, preferred_element_type=jnp.float32
    ).astype(jnp.bfloat16)
    projected = projected.reshape(3, clip_count, slot_len, head_count, HEAD)

    def self_clip(entries):
        return attend(entries[0], entries[1], entries[2], entries[3], True, score_scale)

    self_heads, self_log = lax.map(self_clip, (projected[0], projected[1], projected[2], frame_len))
    self_flat = self_heads.reshape(row_total, local_width)
    self_out_all = lax.all_gather(self_out, "tensor")
    cross_out_all = lax.all_gather(cross_out, "tensor")
    cross_query_all = lax.all_gather(cross_query, "tensor")
    after_self = inputs + gathered_sum(self_flat, self_out_all, "sk,kd->sd")
    normed_cross = layer_norm(after_self, cross_gain, cross_bias).astype(jnp.bfloat16)
    cross_queries = jnp.dot(normed_cross, cross_query, preferred_element_type=jnp.float32).astype(
        jnp.bfloat16
    )
    cross_queries = cross_queries.reshape(clip_count, slot_len, head_count, HEAD)
    text_proj = jnp.einsum(
        "ctd,gde->gcte", text_states, cross_keyval, preferred_element_type=jnp.float32
    ).astype(jnp.bfloat16)
    text_proj = text_proj.reshape(2, clip_count, text_count, head_count, HEAD)

    def cross_clip(entries):
        return attend(entries[0], entries[1], entries[2], entries[3], False, score_scale)

    cross_heads, cross_log = lax.map(
        cross_clip, (cross_queries, text_proj[0], text_proj[1], text_token_length)
    )
    cross_flat = cross_heads.reshape(row_total, local_width)
    after_cross = after_self + gathered_sum(cross_flat, cross_out_all, "sk,kd->sd")
    normed_feed = layer_norm(after_cross, feed_gain, feed_bias).astype(jnp.bfloat16)
    upward = jnp.dot(normed_feed, feed_up, preferred_element_type=jnp.float32)
    active = gelu_exact(upward).astype(jnp.bfloat16)
    feed_part = jnp.dot(active, feed_down, preferred_element_type=jnp.float32)
    feed_low = feed_part.astype(jnp.bfloat16)
    active_grad = jnp.einsum("sd,kd->sk", out_grad, feed_down, preferred_element_type=jnp.float32)
    _, gelu_pull = jax.vjp(gelu_exact, upward)
    upward_grad = gelu_pull(active_grad)[0].astype(jnp.bfloat16)
    downward_gradient = jnp.einsum(
        "sk,sd->kd", active, out_grad, preferred_element_type=jnp.float32
    )
    up_grad = jnp.einsum("sd,sk->dk", normed_feed, upward_grad, preferred_element_type=jnp.float32)
    feed_input_part = jnp.einsum(
        "sk,dk->sd", upward_grad, feed_up, preferred_element_type=jnp.float32
    )
    feed_back = norm_back(after_cross, feed_gain, feed_bias, direct_total(feed_input_part))
    feed_sums = [dp_sum(up_grad), dp_sum(downward_gradient)]
    cross_grad_rows = out_grad.astype(jnp.float32) + feed_back[0]
    cross_grad_low = cross_grad_rows.astype(jnp.bfloat16)
    cout_grad = jnp.einsum(
        "sk,sd->kd", cross_flat, cross_grad_low, preferred_element_type=jnp.float32
    )
    cross_heads_grad = jnp.einsum(
        "sd,kd->sk", cross_grad_low, cross_out, preferred_element_type=jnp.float32
    ).astype(jnp.bfloat16)
    cross_heads_grad = cross_heads_grad.reshape(clip_count, slot_len, head_count, HEAD)

    def cross_clip_back(entries):
        return attend_back(
            entries[0],
            entries[1],
            entries[2],
            entries[3],
            entries[4],
            entries[5],
            False,
            score_scale,
        )

    cquery_heads, ckey_heads, cvalue_heads = lax.map(
        cross_clip_back,
        (cross_queries, text_proj[0], text_proj[1], cross_log, cross_heads_grad, text_token_length),
    )
    query_grad_low = cquery_heads.reshape(row_total, local_width).astype(jnp.bfloat16)
    keyval_grad_low = jnp.stack((ckey_heads, cvalue_heads)).astype(jnp.bfloat16)
    keyval_grad_low = keyval_grad_low.reshape(2, clip_count, text_count, local_width)
    cquery_grad = jnp.einsum(
        "sd,se->de", normed_cross, query_grad_low, preferred_element_type=jnp.float32
    )
    ckeyval_grad = jnp.einsum(
        "ctd,gcte->gde", text_states, keyval_grad_low, preferred_element_type=jnp.float32
    )
    text_part = jnp.einsum(
        "gcte,gde->ctd", keyval_grad_low, cross_keyval, preferred_element_type=jnp.float32
    )
    query_pieces = relay_pieces(query_grad_low, "tensor")
    feed_low, first_piece = lax.optimization_barrier((feed_low, query_pieces[1][0]))
    query_pieces[1] = (first_piece, query_pieces[1][1])
    block_out = (after_cross + lax.psum(feed_low, "tensor").astype(jnp.float32)).astype(
        jnp.bfloat16
    )
    cross_sum = gathered_sum(
        query_grad_low, cross_query_all, "se,de->sd", lambda block, axis: query_pieces
    )
    text_grad = lax.psum(text_part.astype(jnp.bfloat16), "tensor").astype(jnp.float32)
    cross_back = norm_back(after_self, cross_gain, cross_bias, cross_sum)
    self_grad_rows = cross_grad_rows + cross_back[0]
    feed_sums, self_grad_rows = lax.optimization_barrier((feed_sums, self_grad_rows))
    self_grad_low = self_grad_rows.astype(jnp.bfloat16)
    sout_grad = jnp.einsum(
        "sk,sd->kd", self_flat, self_grad_low, preferred_element_type=jnp.float32
    )
    self_heads_grad = jnp.einsum(
        "sd,kd->sk", self_grad_low, self_out, preferred_element_type=jnp.float32
    ).astype(jnp.bfloat16)
    self_heads_grad = self_heads_grad.reshape(clip_count, slot_len, head_count, HEAD)

    def self_clip_back(entries):
        return attend_back(
            entries[0],
            entries[1],
            entries[2],
            entries[3],
            entries[4],
            entries[5],
            True,
            score_scale,
        )

    self_query_heads, self_key_heads, self_value_heads = lax.map(
        self_clip_back,
        (projected[0], projected[1], projected[2], self_log, self_heads_grad, frame_len),
    )
    projection_gradient = jnp.stack((self_query_heads, self_key_heads, self_value_heads)).astype(
        jnp.bfloat16
    )
    projection_gradient = projection_gradient.reshape(3, row_total, local_width)
    qkv_grad = jnp.einsum(
        "sd,cse->cde", normed_self, projection_gradient, preferred_element_type=jnp.float32
    )
    self_input_part = jnp.einsum(
        "cse,cde->sd", projection_gradient, self_qkv, preferred_element_type=jnp.float32
    )
    self_back = norm_back(inputs, self_gain, self_bias, direct_total(self_input_part))
    self_norm_terms = (dp_sum(self_back[1]), dp_sum(self_back[2]))
    frames_grad = self_grad_rows + self_back[0]
    gain_terms = (
        self_back[1],
        self_back[2],
        cross_back[1],
        cross_back[2],
        feed_back[1],
        feed_back[2],
    )
    late_sums = [dp_sum(term) for term in (qkv_grad, sout_grad, cquery_grad, ckeyval_grad)]
    late_sums = late_sums + stacked_psum(
        cout_grad, [cross_back[1], cross_back[2], feed_back[1], feed_back[2]], "dp"
    )
    summed = (
        self_norm_terms[0],
        self_norm_terms[1],
        late_sums[5],
        late_sums[6],
        late_sums[7],
        late_sums[8],
        late_sums[0],
        late_sums[1],
        late_sums[2],
        late_sums[3],
        late_sums[4],
        feed_sums[0],
        feed_sums[1],
    )
    return (
        block_out.reshape(clip_count, slot_len, model_width),
        frames_grad.reshape(clip_count, slot_len, model_width),
        text_grad,
        summed[0],
        summed[1],
        summed[2],
        summed[3],
        summed[4],
        summed[5],
        summed[6],
        summed[7],
        summed[8],
        summed[9],
        summed[10],
        summed[11],
        summed[12],
    )


def solution(mesh):
    return jax.shard_map(
        local,
        mesh=mesh,
        in_specs=(
            P("dp", None, None),
            P("dp", None, None),
            P("dp"),
            P("dp"),
            P(),
            P(),
            P(),
            P(),
            P(),
            P(),
            P(None, None, "tensor"),
            P("tensor", None),
            P(None, "tensor"),
            P(None, None, "tensor"),
            P("tensor", None),
            P(None, "tensor"),
            P("tensor", None),
            P("dp", None, None),
        ),
        out_specs=(
            P("dp", None, None),
            P("dp", None, None),
            P("dp", None, None),
            P(),
            P(),
            P(),
            P(),
            P(),
            P(),
            P(None, None, "tensor"),
            P("tensor", None),
            P(None, "tensor"),
            P(None, None, "tensor"),
            P("tensor", None),
            P(None, "tensor"),
            P("tensor", None),
        ),
        check_vma=False,
    )
```

```python
import jax
import jax.numpy as jnp
from jax import lax
from jax.sharding import PartitionSpec as P

HEAD = 64


EPSILON = 1e-05
MASKED = -1e30


def layer_norm(inputs, norm_gain, norm_bias):
    row_mean = jnp.mean(inputs, axis=-1, keepdims=True)
    centred = inputs - row_mean
    spread = jnp.mean(centred * centred, axis=-1, keepdims=True)
    return centred * lax.rsqrt(spread + EPSILON) * norm_gain + norm_bias


def normalized(inputs):
    row_mean = jnp.mean(inputs, axis=-1, keepdims=True)
    centred = inputs - row_mean
    spread = jnp.mean(centred * centred, axis=-1, keepdims=True)
    return centred * lax.rsqrt(spread + EPSILON)


def norm_back(inputs, norm_gain, norm_bias, upstream):
    _, pullback = jax.vjp(layer_norm, inputs, norm_gain, norm_bias)
    return pullback(upstream)


def gelu_exact(inputs):
    return jax.nn.gelu(inputs, approximate=False)


def masked_scores(portion, offset, key_rows, key_limit, causal, score_scale):
    scores = (
        jnp.einsum("bhe,khe->hbk", portion, key_rows, preferred_element_type=jnp.float32)
        * score_scale
    )
    key_pos = jnp.arange(key_rows.shape[0])
    allowed = key_pos[None, :] < key_limit
    if causal:
        allowed = allowed & (key_pos[None, :] <= offset + jnp.arange(portion.shape[0])[:, None])
    return jnp.where(allowed[None], scores, MASKED)


def attend(queries, key_rows, values, key_limit, causal, score_scale):
    row_count, head_count, head_size = queries.shape
    block_len = min(512, row_count)
    portions = queries.reshape(row_count // block_len, block_len, head_count, head_size)
    offsets = jnp.arange(row_count // block_len) * block_len

    def one_block(entries):
        portion, offset = entries
        scores = masked_scores(portion, offset, key_rows, key_limit, causal, score_scale)
        row_max = jnp.max(scores, axis=-1, keepdims=True)
        unnormed = jnp.exp(scores - row_max)
        row_sum = jnp.sum(unnormed, axis=-1, keepdims=True)
        probs_low = (unnormed / row_sum).astype(jnp.bfloat16)
        result = jnp.einsum("hbk,khe->bhe", probs_low, values, preferred_element_type=jnp.float32)
        return (result.astype(jnp.bfloat16), row_max[..., 0] + jnp.log(row_sum[..., 0]))

    if not causal:
        result, log_total = lax.map(one_block, (portions, offsets))
        return (result.reshape(row_count, head_count, head_size), log_total)
    results, totals = [], []
    for index in range(row_count // block_len):
        key_end = (index + 1) * block_len
        scores = masked_scores(
            portions[index], index * block_len, key_rows[:key_end], key_limit, causal, score_scale
        )
        row_max = jnp.max(scores, axis=-1, keepdims=True)
        unnormed = jnp.exp(scores - row_max)
        row_sum = jnp.sum(unnormed, axis=-1, keepdims=True)
        probs_low = (unnormed / row_sum).astype(jnp.bfloat16)
        result = jnp.einsum(
            "hbk,khe->bhe", probs_low, values[:key_end], preferred_element_type=jnp.float32
        )
        results.append(result.astype(jnp.bfloat16))
        totals.append(row_max[..., 0] + jnp.log(row_sum[..., 0]))
    return (jnp.concatenate(results).reshape(row_count, head_count, head_size), jnp.stack(totals))


def attend_back(queries, key_rows, values, log_total, out_grad, key_limit, causal, score_scale):
    row_count, head_count, head_size = queries.shape
    block_len = min(512, row_count)
    portions = queries.reshape(row_count // block_len, block_len, head_count, head_size)
    grad_parts = out_grad.reshape(row_count // block_len, block_len, head_count, head_size)
    offsets = jnp.arange(row_count // block_len) * block_len

    def one_block(carry, entries):
        key_grad, value_grad = carry
        portion, grad_part, log_part, offset = entries
        scores = masked_scores(portion, offset, key_rows, key_limit, causal, score_scale)
        probs = jnp.exp(scores - log_part[..., None])
        probs_grad = jnp.einsum(
            "bhe,khe->hbk", grad_part, values, preferred_element_type=jnp.float32
        )
        row_dot = jnp.sum(probs * probs_grad, axis=-1, keepdims=True)
        scores_grad = (probs * (probs_grad - row_dot)).astype(jnp.bfloat16)
        value_grad = value_grad + jnp.einsum(
            "hbk,bhe->khe",
            probs.astype(jnp.bfloat16),
            grad_part,
            preferred_element_type=jnp.float32,
        )
        key_grad = (
            key_grad
            + jnp.einsum("hbk,bhe->khe", scores_grad, portion, preferred_element_type=jnp.float32)
            * score_scale
        )
        query_grad = (
            jnp.einsum("hbk,khe->bhe", scores_grad, key_rows, preferred_element_type=jnp.float32)
            * score_scale
        )
        return ((key_grad, value_grad), query_grad)

    empty = jnp.zeros(key_rows.shape, jnp.float32)
    if not causal:
        (key_grad, value_grad), query_grad = lax.scan(
            one_block, (empty, empty), (portions, grad_parts, log_total, offsets)
        )
        return (query_grad.reshape(row_count, head_count, head_size), key_grad, value_grad)
    key_grad, value_grad, query_grads = empty, empty, []
    for index in range(row_count // block_len):
        key_end = (index + 1) * block_len
        portion, grad_part = portions[index], grad_parts[index]
        keys, vals = key_rows[:key_end], values[:key_end]
        scores = masked_scores(portion, index * block_len, keys, key_limit, causal, score_scale)
        probs = jnp.exp(scores - log_total[index][..., None])
        probs_grad = jnp.einsum("bhe,khe->hbk", grad_part, vals, preferred_element_type=jnp.float32)
        row_dot = jnp.sum(probs * probs_grad, axis=-1, keepdims=True)
        scores_grad = (probs * (probs_grad - row_dot)).astype(jnp.bfloat16)
        value_part = jnp.einsum(
            "hbk,bhe->khe", probs.astype(jnp.bfloat16), grad_part, preferred_element_type=jnp.float32
        )
        key_part = (
            jnp.einsum("hbk,bhe->khe", scores_grad, portion, preferred_element_type=jnp.float32)
            * score_scale
        )
        value_grad = value_grad.at[:key_end].add(value_part)
        key_grad = key_grad.at[:key_end].add(key_part)
        query_grads.append(
            jnp.einsum("hbk,khe->bhe", scores_grad, keys, preferred_element_type=jnp.float32)
            * score_scale
        )
    query_grad = jnp.concatenate(query_grads)
    return (query_grad.reshape(row_count, head_count, head_size), key_grad, value_grad)


def head_total(partial_value):
    return lax.psum(partial_value.astype(jnp.bfloat16), "tensor").astype(jnp.float32)


def relay_pieces(block, axis):
    count = lax.axis_size(axis)
    me = lax.axis_index(axis)
    pieces = [(block, me)]
    from_left, from_right = block, block
    for k in range(1, count):
        from_left = lax.ppermute(from_left, axis, [(i, i + 1) for i in range(k - 1, count - 1)])
        from_right = lax.ppermute(from_right, axis, [(i, i - 1) for i in range(1, count - k + 1)])
        pieces.append((from_left, me - k))
        pieces.append((from_right, me + k))
    return pieces


def relay_scatter(value, axis):
    count = lax.axis_size(axis)
    me = lax.axis_index(axis)
    shards = value.reshape((count, value.shape[0] // count) + value.shape[1:])

    def pick(index):
        return lax.dynamic_index_in_dim(shards, jnp.clip(index, 0, count - 1), 0, keepdims=False)

    to_right = to_left = None
    for k in range(1, count):
        send_right = pick(me + count - k).astype(jnp.float32)
        send_left = pick(me - (count - k)).astype(jnp.float32)
        if to_right is not None:
            send_right = send_right + to_right.astype(jnp.float32)
            send_left = send_left + to_left.astype(jnp.float32)
        to_right = lax.ppermute(
            send_right.astype(value.dtype), axis, [(i, i + 1) for i in range(min(k, count - 1))]
        )
        to_left = lax.ppermute(
            send_left.astype(value.dtype), axis, [(i, i - 1) for i in range(max(count - k, 1), count)]
        )
    total = pick(me).astype(jnp.float32)
    if to_right is not None:
        total = total + to_right.astype(jnp.float32) + to_left.astype(jnp.float32)
    return total.astype(value.dtype)


def _rotate(value, axis, count, step):
    return lax.ppermute(value, axis, [(i, (i + step) % count) for i in range(count)])


def direct_total(partial_value):
    count = lax.axis_size("tensor")
    me = lax.axis_index("tensor")
    low_value = partial_value.astype(jnp.bfloat16)
    shards = low_value.reshape((count, low_value.shape[0] // count) + low_value.shape[1:])
    reduced = lax.dynamic_index_in_dim(shards, me, 0, keepdims=False).astype(jnp.float32)
    for step in range(1, count):
        sent = lax.dynamic_index_in_dim(shards, (me + step) % count, 0, keepdims=False)
        reduced = reduced + _rotate(sent, "tensor", count, step).astype(jnp.float32)
    reduced = reduced.astype(jnp.bfloat16)
    pieces = [(reduced, me)] + [
        (_rotate(reduced, "tensor", count, step), (me - step) % count) for step in range(1, count)
    ]
    rows = []
    for owner in range(count):
        shard = jnp.zeros_like(reduced)
        for piece, source in pieces:
            shard = jnp.where(source == owner, piece, shard)
        rows.append(shard)
    return jnp.concatenate(rows).astype(jnp.float32)


def relay_total(partial_value):
    low_value = partial_value.astype(jnp.bfloat16)
    reduced = relay_scatter(low_value, "tensor")
    pieces = relay_pieces(reduced, "tensor")
    shards = []
    for owner in range(len(pieces) // 2 + 1):
        shard = jnp.zeros_like(reduced)
        for piece, source in pieces:
            shard = jnp.where(source == owner, piece, shard)
        shards.append(shard)
    return jnp.concatenate(shards).astype(jnp.float32)


def stacked_psum(matrix, rows, axis):
    pad = (-(matrix.shape[0] + len(rows))) % 16
    extra = jnp.stack(rows + [jnp.zeros_like(rows[0])] * pad)
    summed = lax.psum(jnp.concatenate([matrix, extra]).astype(jnp.bfloat16), axis)
    summed = summed.astype(jnp.float32)
    count = matrix.shape[0]
    return [summed[:count]] + [summed[count + i] for i in range(len(rows))]


def dp_sum(term):
    return lax.psum(term.astype(jnp.bfloat16), "dp").astype(jnp.float32)


def gathered_sum(block, weights, spec, pieces_of=relay_pieces):
    count = weights.shape[0]
    total = None
    for piece, source in pieces_of(block, "tensor"):
        weight = lax.dynamic_index_in_dim(weights, jnp.clip(source, 0, count - 1), 0, keepdims=False)
        partial_value = jnp.einsum(spec, piece, weight, preferred_element_type=jnp.float32)
        partial_value = partial_value.astype(jnp.bfloat16).astype(jnp.float32)
        total = partial_value if total is None else total + partial_value
        total = lax.optimization_barrier(total)
    return total


def local(
    frames,
    text_states,
    frame_len,
    text_token_length,
    self_gain,
    self_bias,
    cross_gain,
    cross_bias,
    feed_gain,
    feed_bias,
    self_qkv,
    self_out,
    cross_query,
    cross_keyval,
    cross_out,
    feed_up,
    feed_down,
    cotangent,
):
    clip_count, slot_len, model_width = frames.shape
    text_count = text_states.shape[1]
    local_width = self_out.shape[0]
    head_count = local_width // HEAD
    score_scale = HEAD ** (-0.5)
    row_total = clip_count * slot_len
    inputs = frames.reshape(row_total, model_width).astype(jnp.float32)
    out_grad = cotangent.reshape(row_total, model_width)
    normed_self = layer_norm(inputs, self_gain, self_bias).astype(jnp.bfloat16)
    projected = jnp.einsum(
        "sd,cde->cse", normed_self, self_qkv, preferred_element_type=jnp.float32
    ).astype(jnp.bfloat16)
    projected = projected.reshape(3, clip_count, slot_len, head_count, HEAD)

    def self_clip(entries):
        return attend(entries[0], entries[1], entries[2], entries[3], True, score_scale)

    self_heads, self_log = lax.map(self_clip, (projected[0], projected[1], projected[2], frame_len))
    self_flat = self_heads.reshape(row_total, local_width)
    self_out_all = lax.all_gather(self_out, "tensor")
    cross_out_all = lax.all_gather(cross_out, "tensor")
    cross_query_all = lax.all_gather(cross_query, "tensor")
    after_self = inputs + gathered_sum(self_flat, self_out_all, "sk,kd->sd")
    normed_cross = layer_norm(after_self, cross_gain, cross_bias).astype(jnp.bfloat16)
    cross_queries = jnp.dot(normed_cross, cross_query, preferred_element_type=jnp.float32).astype(
        jnp.bfloat16
    )
    cross_queries = cross_queries.reshape(clip_count, slot_len, head_count, HEAD)
    text_proj = jnp.einsum(
        "ctd,gde->gcte", text_states, cross_keyval, preferred_element_type=jnp.float32
    ).astype(jnp.bfloat16)
    text_proj = text_proj.reshape(2, clip_count, text_count, head_count, HEAD)

    def cross_clip(entries):
        return attend(entries[0], entries[1], entries[2], entries[3], False, score_scale)

    cross_heads, cross_log = lax.map(
        cross_clip, (cross_queries, text_proj[0], text_proj[1], text_token_length)
    )
    cross_flat = cross_heads.reshape(row_total, local_width)
    after_cross = after_self + gathered_sum(cross_flat, cross_out_all, "sk,kd->sd")
    normed_feed = layer_norm(after_cross, feed_gain, feed_bias).astype(jnp.bfloat16)
    upward = jnp.dot(normed_feed, feed_up, preferred_element_type=jnp.float32)
    active = gelu_exact(upward).astype(jnp.bfloat16)
    feed_part = jnp.dot(active, feed_down, preferred_element_type=jnp.float32)
    feed_low = feed_part.astype(jnp.bfloat16)
    active_grad = jnp.einsum("sd,kd->sk", out_grad, feed_down, preferred_element_type=jnp.float32)
    _, gelu_pull = jax.vjp(gelu_exact, upward)
    upward_grad = gelu_pull(active_grad)[0].astype(jnp.bfloat16)
    downward_gradient = jnp.einsum(
        "sk,sd->kd", active, out_grad, preferred_element_type=jnp.float32
    )
    up_grad = jnp.einsum("sd,sk->dk", normed_feed, upward_grad, preferred_element_type=jnp.float32)
    feed_input_part = jnp.einsum(
        "sk,dk->sd", upward_grad, feed_up, preferred_element_type=jnp.float32
    )
    feed_back = norm_back(after_cross, feed_gain, feed_bias, direct_total(feed_input_part))
    feed_sums = [dp_sum(up_grad), dp_sum(downward_gradient)]
    cross_grad_rows = out_grad.astype(jnp.float32) + feed_back[0]
    cross_grad_low = cross_grad_rows.astype(jnp.bfloat16)
    cout_grad = jnp.einsum(
        "sk,sd->kd", cross_flat, cross_grad_low, preferred_element_type=jnp.float32
    )
    cross_heads_grad = jnp.einsum(
        "sd,kd->sk", cross_grad_low, cross_out, preferred_element_type=jnp.float32
    ).astype(jnp.bfloat16)
    cross_heads_grad = cross_heads_grad.reshape(clip_count, slot_len, head_count, HEAD)

    def cross_clip_back(entries):
        return attend_back(
            entries[0],
            entries[1],
            entries[2],
            entries[3],
            entries[4],
            entries[5],
            False,
            score_scale,
        )

    cquery_heads, ckey_heads, cvalue_heads = lax.map(
        cross_clip_back,
        (cross_queries, text_proj[0], text_proj[1], cross_log, cross_heads_grad, text_token_length),
    )
    query_grad_low = cquery_heads.reshape(row_total, local_width).astype(jnp.bfloat16)
    keyval_grad_low = jnp.stack((ckey_heads, cvalue_heads)).astype(jnp.bfloat16)
    keyval_grad_low = keyval_grad_low.reshape(2, clip_count, text_count, local_width)
    cquery_grad = jnp.einsum(
        "sd,se->de", normed_cross, query_grad_low, preferred_element_type=jnp.float32
    )
    ckeyval_grad = jnp.einsum(
        "ctd,gcte->gde", text_states, keyval_grad_low, preferred_element_type=jnp.float32
    )
    text_part = jnp.einsum(
        "gcte,gde->ctd", keyval_grad_low, cross_keyval, preferred_element_type=jnp.float32
    )
    query_pieces = relay_pieces(query_grad_low, "tensor")
    feed_low, held_piece = lax.optimization_barrier((feed_low, query_pieces[3][0]))
    query_pieces[3] = (held_piece, query_pieces[3][1])
    block_out = (after_cross + lax.psum(feed_low, "tensor").astype(jnp.float32)).astype(
        jnp.bfloat16
    )
    cross_sum = gathered_sum(
        query_grad_low, cross_query_all, "se,de->sd", lambda block, axis: query_pieces
    )
    text_grad = lax.psum(text_part.astype(jnp.bfloat16), "tensor").astype(jnp.float32)
    cross_back = norm_back(after_self, cross_gain, cross_bias, cross_sum)
    self_grad_rows = cross_grad_rows + cross_back[0]
    feed_sums, self_grad_rows = lax.optimization_barrier((feed_sums, self_grad_rows))
    self_grad_low = self_grad_rows.astype(jnp.bfloat16)
    sout_grad = jnp.einsum(
        "sk,sd->kd", self_flat, self_grad_low, preferred_element_type=jnp.float32
    )
    self_heads_grad = jnp.einsum(
        "sd,kd->sk", self_grad_low, self_out, preferred_element_type=jnp.float32
    ).astype(jnp.bfloat16)
    self_heads_grad = self_heads_grad.reshape(clip_count, slot_len, head_count, HEAD)

    def self_clip_back(entries):
        return attend_back(
            entries[0],
            entries[1],
            entries[2],
            entries[3],
            entries[4],
            entries[5],
            True,
            score_scale,
        )

    self_query_heads, self_key_heads, self_value_heads = lax.map(
        self_clip_back,
        (projected[0], projected[1], projected[2], self_log, self_heads_grad, frame_len),
    )
    projection_gradient = jnp.stack((self_query_heads, self_key_heads, self_value_heads)).astype(
        jnp.bfloat16
    )
    projection_gradient = projection_gradient.reshape(3, row_total, local_width)
    qkv_grad = jnp.einsum(
        "sd,cse->cde", normed_self, projection_gradient, preferred_element_type=jnp.float32
    )
    self_input_part = jnp.einsum(
        "cse,cde->sd", projection_gradient, self_qkv, preferred_element_type=jnp.float32
    )
    self_back = norm_back(inputs, self_gain, self_bias, direct_total(self_input_part))
    self_norm_terms = (dp_sum(self_back[1]), dp_sum(self_back[2]))
    frames_grad = self_grad_rows + self_back[0]
    gain_terms = (
        self_back[1],
        self_back[2],
        cross_back[1],
        cross_back[2],
        feed_back[1],
        feed_back[2],
    )
    late_sums = [dp_sum(term) for term in (qkv_grad, sout_grad, cquery_grad, ckeyval_grad)]
    late_sums = late_sums + stacked_psum(
        cout_grad, [cross_back[1], cross_back[2], feed_back[1], feed_back[2]], "dp"
    )
    summed = (
        self_norm_terms[0],
        self_norm_terms[1],
        late_sums[5],
        late_sums[6],
        late_sums[7],
        late_sums[8],
        late_sums[0],
        late_sums[1],
        late_sums[2],
        late_sums[3],
        late_sums[4],
        feed_sums[0],
        feed_sums[1],
    )
    return (
        block_out.reshape(clip_count, slot_len, model_width),
        frames_grad.reshape(clip_count, slot_len, model_width),
        text_grad,
        summed[0],
        summed[1],
        summed[2],
        summed[3],
        summed[4],
        summed[5],
        summed[6],
        summed[7],
        summed[8],
        summed[9],
        summed[10],
        summed[11],
        summed[12],
    )


def solution(mesh):
    return jax.shard_map(
        local,
        mesh=mesh,
        in_specs=(
            P("dp", None, None),
            P("dp", None, None),
            P("dp"),
            P("dp"),
            P(),
            P(),
            P(),
            P(),
            P(),
            P(),
            P(None, None, "tensor"),
            P("tensor", None),
            P(None, "tensor"),
            P(None, None, "tensor"),
            P("tensor", None),
            P(None, "tensor"),
            P("tensor", None),
            P("dp", None, None),
        ),
        out_specs=(
            P("dp", None, None),
            P("dp", None, None),
            P("dp", None, None),
            P(),
            P(),
            P(),
            P(),
            P(),
            P(),
            P(None, None, "tensor"),
            P("tensor", None),
            P(None, "tensor"),
            P(None, None, "tensor"),
            P("tensor", None),
            P(None, "tensor"),
            P("tensor", None),
        ),
        check_vma=False,
    )
```
